128 devices in a mesh: pos: 8 (over y, core), stream: 16 (over z, x).
Axes of the slice: x: 4, y: 4, z: 4, core: 2. Of those that a mesh axis runs over, the one named last changes fastest.
Arguments:
- tokens_in: bfloat16 [16, 4096, 8192], P('stream', 'pos'), may hold values from -6 to 6
- proj_in: bfloat16 [16, 4096, 256], P('stream', 'pos'), may hold values from -1.75 to 1.75
- step_raw: bfloat16 [16, 4096, 128], P('stream', 'pos')
- decay_log: float32 [128], replicated, may hold values from -0.7 to 0.7
- head_skip_weight: float32 [128], replicated, may hold values from 0.5 to 1.5
- row_counts: int32 [8, 16, 16], replicated, may hold values from 16 to 48, as said below
Outputs:
- layer_out: bfloat16 [16, 4096, 8192], P('stream', 'pos')
The draws below stay inside these ranges and needn't reach their ends.
Inputs may be any that keep to these rules, and one draw needn't show every extreme that they name: For each p, every row and every column of row_counts[p] sums to 512; all rows and columns of row_counts[p] hold the same list of values in some order, and the list splits into pairs whose sum is twice the list's mean; each row_counts[p] holds the value 48.
All inputs are finite; a program needn't handle non-finite values.
Results may differ from the reference program's by a relative error of at most 0.0037.
Values may be sent and summed in bfloat16 or wider, within the bound.
No kernel may reach another device: no remote copies, remote signals or barrier semaphores. Data moves between devices by JAX's collectives and lax.ppermute only.
A program may use at most 256 MiB of HBM per device.

```python
from functools import partial
import jax
import jax.numpy as jnp
from jax import lax

HEADS = 128
HDIM = 64
STATE = 128
TOK_DEV = 512
BLOCK = 512
INNER = 8192
SEQUENCE_SLOTS = 4096
N_POS = 8
N_STREAM = 16


def head_law(key):
    law_key = jax.random.fold_in(key, 7071)
    derived_prng_keys = jax.random.split(law_key, 3)
    fast_share = 0.5
    fast_heads = jax.random.uniform(derived_prng_keys[0], (HEADS,)) < fast_share
    absolute_amplitude = jnp.exp(jax.random.uniform(derived_prng_keys[1], (HEADS,), minval=-0.69, maxval=0.69))
    spread = jax.random.uniform(derived_prng_keys[2], (HEADS,))
    per_step = jnp.where(fast_heads, 1.0 / (10.0 + 30.0 * spread), (0.5 + spread) / SEQUENCE_SLOTS)
    return (absolute_amplitude, per_step)


def draw_decay_log(key, part):
    absolute_amplitude, per_step = head_law(key)
    return jnp.log(absolute_amplitude)


def draw_step_raw(key, part):
    absolute_amplitude, per_step = head_law(key)
    derived_prng_keys = jax.random.split(jax.random.fold_in(key, 313), 3)
    jitter = jnp.clip(0.3 * jax.random.normal(derived_prng_keys[0], (N_STREAM, SEQUENCE_SLOTS, HEADS)), -0.45, 0.45)
    discretization_deltas = (per_step / absolute_amplitude)[None, None, :] * jnp.exp(jitter)
    arrival_bundles = jax.random.uniform(derived_prng_keys[1], (N_STREAM, SEQUENCE_SLOTS, 1)) < 3.0 / SEQUENCE_SLOTS
    excitation_level = jax.random.uniform(derived_prng_keys[2], (N_STREAM, SEQUENCE_SLOTS, HEADS), minval=0.22, maxval=0.69)
    discretization_deltas = jnp.where(arrival_bundles, excitation_level / absolute_amplitude[None, None, :], discretization_deltas)
    return jnp.log(jnp.expm1(discretization_deltas)).astype(jnp.bfloat16)


def draw_row_counts(key, part):
    base_count = TOK_DEV // N_STREAM
    half_base = base_count // 2
    pair_count = N_STREAM // 2

    def one_place(place_key):
        derived_prng_keys = jax.random.split(place_key, 4)
        shift_size = jax.random.randint(derived_prng_keys[0], (pair_count,), 0, half_base + 1)
        shift_size = jnp.where(jnp.arange(pair_count) == 0, half_base, shift_size)
        values = jnp.concatenate([base_count + shift_size, base_count - shift_size])
        reorder = jax.random.permutation(derived_prng_keys[1], N_STREAM)
        values = jnp.take(values, reorder)
        row_perm = jax.random.permutation(derived_prng_keys[2], N_STREAM)
        col_perm = jax.random.permutation(derived_prng_keys[3], N_STREAM)
        offset = (col_perm[None, :] - row_perm[:, None]) % N_STREAM
        return jnp.take(values, offset).astype(jnp.int32)
    return jax.vmap(one_place)(jax.random.split(jax.random.fold_in(key, 977), N_POS))


def levels(stream_key, shape, shards, low, top_value):
    gain = 1.0
    for axis_at, blocks in shards:
        heights = jax.random.uniform(jax.random.fold_in(jax.random.fold_in(stream_key, 6), axis_at), (blocks,), jnp.float32, low / len(shards), top_value / len(shards))
        gain = gain * jnp.repeat(jnp.exp(heights), shape[axis_at] // blocks).reshape((-1,) + (1,) * (len(shape) - 1 - axis_at))
    return gain


def gaussian(key, extent, scale, most, shards=(), kind=jnp.bfloat16):
    array = scale * jax.random.normal(key, extent, jnp.float32)
    if shards:
        array = array * levels(key, extent, shards, -0.22, 0.18)
    return jnp.clip(array, -most, most).astype(kind)


def setup_inputs(seed: int = 0) -> dict:
    streams_of = jax.random.split(jax.random.key(seed), 7)
    tokens_in = gaussian(streams_of[0], (N_STREAM, SEQUENCE_SLOTS, INNER), 1.0, 6.0, ((0, 16), (1, 8)))
    proj_in = gaussian(streams_of[1], (N_STREAM, SEQUENCE_SLOTS, 2 * STATE), (STATE ** -0.25), 1.75, ((0, 16), (1, 8)))
    step_raw = draw_step_raw(jax.random.fold_in(streams_of[6], 71), 0)
    decay_log = draw_decay_log(jax.random.fold_in(streams_of[6], 71), 0)
    head_skip_weight = jnp.clip(jax.random.uniform(streams_of[4], (HEADS,), jnp.float32, 0.5, 1.5), 0.5, 1.5)
    row_counts = draw_row_counts(jax.random.fold_in(streams_of[6], 71), 0)
    return {"tokens_in": tokens_in, "proj_in": proj_in, "step_raw": step_raw, "decay_log": decay_log, "head_skip_weight": head_skip_weight, "row_counts": row_counts}


def stream_blocks(carry_state, block_data, decay_rates, head_skip_weight):
    tokens, input_projections, steps_raw = block_data
    length = tokens.shape[0]
    token_heads = tokens.reshape(length, HEADS, HDIM).astype(jnp.float32)
    inputs = input_projections[:, :STATE]
    readout = input_projections[:, STATE:]
    discretization_deltas = jax.nn.softplus(steps_raw.astype(jnp.float32))
    cumulated = jnp.cumsum(discretization_deltas * decay_rates[None, :], axis=0)
    scores = jnp.dot(readout, inputs.T, preferred_element_type=jnp.float32)
    causal = jnp.arange(length, dtype=jnp.int32)[:, None] >= jnp.arange(length, dtype=jnp.int32)[None, :]
    log_decay = jnp.where(causal[:, :, None], cumulated[:, None, :] - cumulated[None, :, :], -jnp.inf)
    weights = (scores[:, :, None] * jnp.exp(log_decay) * discretization_deltas[None, :, :]).astype(jnp.bfloat16)
    weights = lax.optimization_barrier(weights).astype(jnp.float32)
    local_part = jnp.einsum("tsh,shp->thp", weights, token_heads)
    readable = lax.optimization_barrier(carry_state.astype(jnp.bfloat16)).astype(jnp.float32)
    inherited = jnp.einsum("tn,hnp->thp", readout.astype(jnp.float32), readable)
    total = local_part + jnp.exp(cumulated)[:, :, None] * inherited + head_skip_weight[None, :, None] * token_heads
    ending = cumulated[-1]
    scaled = ((jnp.exp(ending[None, :] - cumulated) * discretization_deltas)[:, :, None] * token_heads).astype(jnp.bfloat16)
    scaled = lax.optimization_barrier(scaled).astype(jnp.float32)
    carried = jnp.einsum("sn,shp->hnp", inputs.astype(jnp.float32), scaled)
    new_state = jnp.exp(ending)[:, None, None] * carry_state + carried
    return new_state, total.astype(jnp.bfloat16).reshape(length, HEADS * HDIM)


def reference(tokens_in, proj_in, step_raw, decay_log, head_skip_weight, row_counts):
    decay_rates = -jnp.exp(decay_log)
    send_start = (jnp.cumsum(row_counts, axis=2) - row_counts).astype(jnp.int32)
    recv_end = jnp.cumsum(row_counts, axis=1).astype(jnp.int32)
    recv_start = (recv_end - row_counts).astype(jnp.int32)
    positions = jnp.arange(TOK_DEV, dtype=jnp.int32)
    source = jnp.sum((recv_end[:, :, :, None] <= positions[None, None, None, :]).astype(jnp.int32), axis=1).astype(jnp.int32)
    recv_from = jnp.take_along_axis(jnp.transpose(recv_start, (0, 2, 1)), source, axis=2)
    outgoing_offsets = jnp.take_along_axis(jnp.transpose(send_start, (0, 2, 1)), source, axis=2)
    place_base = jnp.arange(N_POS, dtype=jnp.int32)[:, None, None] * TOK_DEV
    flat_rows = (source * SEQUENCE_SLOTS + place_base + outgoing_offsets + positions[None, None, :] - recv_from).astype(jnp.int32)
    flat_rows = jnp.transpose(flat_rows, (1, 0, 2)).reshape(N_STREAM, SEQUENCE_SLOTS)
    token_flat = tokens_in.reshape(N_STREAM * SEQUENCE_SLOTS, HEADS * HDIM)
    proj_flat = proj_in.reshape(N_STREAM * SEQUENCE_SLOTS, 2 * STATE)
    step_flat = step_raw.reshape(N_STREAM * SEQUENCE_SLOTS, HEADS)
    block_count = SEQUENCE_SLOTS // BLOCK
    block_step = partial(stream_blocks, decay_rates=decay_rates, head_skip_weight=head_skip_weight)

    def one_stream(stream_rows):
        tokens = jnp.take(token_flat, stream_rows, axis=0).reshape(block_count, BLOCK, HEADS * HDIM)
        input_projections = jnp.take(proj_flat, stream_rows, axis=0).reshape(block_count, BLOCK, 2 * STATE)
        steps_raw = jnp.take(step_flat, stream_rows, axis=0).reshape(block_count, BLOCK, HEADS)
        start_state = jnp.zeros((HEADS, STATE, HDIM), jnp.float32)
        scanned = lax.scan(block_step, start_state, (tokens, input_projections, steps_raw))
        return scanned[1].reshape(SEQUENCE_SLOTS, HEADS * HDIM)

    return lax.map(one_stream, flat_rows)
```

```python
import functools

import jax
import jax.numpy as jnp
from jax import lax
from jax.experimental import pallas as pl
from jax.experimental.pallas import tpu as pltpu
from jax.sharding import PartitionSpec as P

GROUP = 8
TILE = 128


def output_kernel(
    scores_ref, cumg_ref, cumt_ref, stept_ref, tok_ref, skip_ref, c_ref, rd_ref, out_ref
):
    length = scores_ref.shape[0]
    heads = cumt_ref.shape[0]
    lane_low = lax.broadcasted_iota(jnp.int32, (1, 128), 1) < 64
    for q in range(heads // 2):
        x = tok_ref[:, 128 * q : 128 * (q + 1)]
        readable = rd_ref[q]
        skip = skip_ref[:, 128 * q : 128 * (q + 1)]
        for i in range(length // TILE):
            r0 = i * TILE
            width = (i + 1) * TILE
            rows = lax.broadcasted_iota(jnp.int32, (TILE, width), 0) + r0
            cols = lax.broadcasted_iota(jnp.int32, (TILE, width), 1)
            causal = rows >= cols
            sc = scores_ref[r0 : r0 + TILE, 0:width]
            parts = []
            decays = []
            for j in range(2):
                h = 2 * q + j
                ct = cumg_ref[0, r0 : r0 + TILE, h : h + 1]
                cs = cumt_ref[h : h + 1, 0:width]
                st = stept_ref[h : h + 1, 0:width]
                w = jnp.where(causal, jnp.exp(ct - cs), 0.0)
                wb = ((sc * w) * st).astype(jnp.bfloat16)
                parts.append(jnp.dot(wb, x[0:width], preferred_element_type=jnp.float32))
                decays.append(jnp.exp(ct))
            local = jnp.where(lane_low, parts[0], parts[1])
            inherited = jnp.dot(
                c_ref[r0 : r0 + TILE, :], readable, preferred_element_type=jnp.float32
            )
            decay = jnp.where(lane_low, decays[0], decays[1])
            xt = x[r0 : r0 + TILE].astype(jnp.float32)
            total = local + decay * inherited + skip * xt
            out_ref[r0 : r0 + TILE, 128 * q : 128 * (q + 1)] = total.astype(out_ref.dtype)


def block_output(scores, cum, steps, tokens, skip_lanes, readout, readable):
    length, heads = cum.shape
    groups = heads // GROUP
    width = GROUP * (tokens.shape[1] // heads)
    cum_grouped = cum.reshape(length, groups, GROUP).transpose(1, 0, 2)
    return pl.pallas_call(
        output_kernel,
        grid=(groups,),
        in_specs=[
            pl.BlockSpec((length, length), lambda g: (0, 0)),
            pl.BlockSpec((1, length, GROUP), lambda g: (g, 0, 0)),
            pl.BlockSpec((GROUP, length), lambda g: (g, 0)),
            pl.BlockSpec((GROUP, length), lambda g: (g, 0)),
            pl.BlockSpec((length, width), lambda g: (0, g)),
            pl.BlockSpec((1, width), lambda g: (0, g)),
            pl.BlockSpec((length, readout.shape[1]), lambda g: (0, 0)),
            pl.BlockSpec((GROUP // 2, readable.shape[1], 128), lambda g: (g, 0, 0)),
        ],
        out_specs=pl.BlockSpec((length, width), lambda g: (0, g)),
        out_shape=jax.ShapeDtypeStruct(tokens.shape, jnp.bfloat16),
        compiler_params=pltpu.CompilerParams(dimension_semantics=("arbitrary",)),
    )(scores, cum_grouped, cum.T, steps.T, tokens, skip_lanes, readout, readable)


def deliver(rows, pick_rows, flat_rows, stream_count, capacity):
    width = rows.shape[1]
    send = jnp.take(rows, pick_rows, axis=0).reshape(stream_count, capacity, width)
    arrived = lax.all_to_all(send, "stream", split_axis=0, concat_axis=0, tiled=True)
    return jnp.take(arrived.reshape(stream_count * capacity, width), flat_rows, axis=0)


def on_device(tokens_in, proj_in, step_raw, decay_log, head_skip_weight, row_counts):
    stream_count = lax.axis_size("stream")
    stream_index = lax.axis_index("stream")
    place_count = lax.axis_size("pos")
    place_index = lax.axis_index("pos")
    tokens = tokens_in[0]
    local_rows = tokens.shape[0]
    head_count = step_raw.shape[2]
    head_size = tokens.shape[1] // head_count
    state_size = proj_in.shape[2] // 2
    capacity = 3 * local_rows // (2 * stream_count)

    place_counts = lax.dynamic_index_in_dim(row_counts, place_index, 0, keepdims=False)
    send_counts = lax.dynamic_index_in_dim(place_counts, stream_index, 0, keepdims=False)
    recv_counts = lax.dynamic_index_in_dim(place_counts, stream_index, 1, keepdims=False)
    send_start = jnp.cumsum(send_counts) - send_counts
    slot_range = jnp.arange(capacity, dtype=jnp.int32)
    pick_rows = jnp.clip(send_start[:, None] + slot_range[None, :], 0, local_rows - 1).reshape(-1)
    recv_end = jnp.cumsum(recv_counts)
    recv_start = recv_end - recv_counts
    positions = jnp.arange(local_rows, dtype=jnp.int32)
    source = jnp.sum((recv_end[:, None] <= positions[None, :]).astype(jnp.int32), axis=0)
    source_start = jnp.take(recv_start, jnp.clip(source, 0, stream_count - 1))
    flat_rows = source * capacity + positions - source_start

    ordered_tokens = deliver(tokens, pick_rows, flat_rows, stream_count, capacity)
    ordered_proj = deliver(proj_in[0], pick_rows, flat_rows, stream_count, capacity)
    ordered_steps = deliver(step_raw[0], pick_rows, flat_rows, stream_count, capacity)

    inputs = ordered_proj[:, :state_size]
    readout = ordered_proj[:, state_size:]
    decay_rates = -jnp.exp(decay_log)
    steps = jax.nn.softplus(ordered_steps.astype(jnp.float32))
    cum = jnp.cumsum(steps * decay_rates[None, :], axis=0)
    ending = cum[-1]
    scale = jnp.exp(ending[None, :] - cum) * steps
    pairs = head_count // 2
    scaled = (scale[:, :, None] * ordered_tokens.reshape(local_rows, head_count, head_size)).astype(
        jnp.bfloat16
    )
    scaled = scaled.reshape(local_rows, pairs, 2 * head_size)
    carried = jnp.einsum("sn,sqc->qnc", inputs, scaled, preferred_element_type=jnp.float32)

    block_decay = jnp.exp(ending)
    all_decay = lax.all_gather(block_decay, "pos")
    all_carried = lax.all_gather(carried, "pos")
    earlier = jnp.arange(place_count, dtype=jnp.int32)
    between = (earlier[None, :] > earlier[:, None]) & (earlier[None, :] < place_index)
    weight = jnp.prod(jnp.where(between[:, :, None], all_decay[None, :, :], 1.0), axis=1)
    weight = jnp.where((earlier < place_index)[:, None], weight, 0.0)
    lane_weight = jnp.repeat(weight, head_size, axis=1).reshape(place_count, pairs, 1, 2 * head_size)
    state = jnp.sum(lane_weight * all_carried, axis=0)
    readable = state.astype(jnp.bfloat16)

    scores = jnp.dot(readout, inputs.T, preferred_element_type=jnp.float32)
    skip_lanes = jnp.repeat(head_skip_weight, head_size).reshape(1, -1)
    result = block_output(scores, cum, steps, ordered_tokens, skip_lanes, readout, readable)
    return result[None]


def solution(mesh):
    in_specs = (
        P("stream", "pos", None),
        P("stream", "pos", None),
        P("stream", "pos", None),
        P(),
        P(),
        P(),
    )
    out_specs = P("stream", "pos", None)
    return jax.shard_map(
        on_device, mesh=mesh, in_specs=in_specs, out_specs=out_specs, check_vma=False
    )
```

```python
import jax
import jax.numpy as jnp
from jax import lax
from jax.experimental import pallas as pl
from jax.experimental.pallas import tpu as pltpu
from jax.sharding import PartitionSpec as P

GROUP = 8
TILE = 128
CHUNKS = 4
EXTRA = 8


def lane_pick(low, high):
    lane_low = lax.broadcasted_iota(jnp.int32, (1, 128), 1) < 64
    return jnp.where(lane_low, low, high)


def carried_kernel(bt_ref, facg_ref, decay_ref, tok_ref, out_ref):
    pairs = out_ref.shape[0]
    state_size = bt_ref.shape[0]
    for q in range(pairs):
        x = tok_ref[:, 128 * q : 128 * (q + 1)].astype(jnp.float32)
        factor = lane_pick(facg_ref[0, :, 2 * q : 2 * q + 1], facg_ref[0, :, 2 * q + 1 : 2 * q + 2])
        scaled = (factor * x).astype(jnp.bfloat16)
        out_ref[q, 0:state_size, :] = jnp.dot(
            bt_ref[...], scaled, preferred_element_type=jnp.float32
        )
        rows = lax.broadcasted_iota(jnp.int32, (EXTRA, 128), 0)
        decay = decay_ref[:, 128 * q : 128 * (q + 1)]
        out_ref[q, state_size : state_size + EXTRA, :] = jnp.where(rows == 0, decay, 0.0)


def local_kernel(scores_ref, cumg_ref, cumt_ref, stept_ref, tok_ref, skip_ref, out_ref):
    length = scores_ref.shape[0]
    heads = cumt_ref.shape[0]
    for q in range(heads // 2):
        x = tok_ref[:, 128 * q : 128 * (q + 1)]
        skip = skip_ref[:, 128 * q : 128 * (q + 1)]
        for i in range(length // TILE):
            r0 = i * TILE
            width = (i + 1) * TILE
            rows = lax.broadcasted_iota(jnp.int32, (TILE, width), 0) + r0
            cols = lax.broadcasted_iota(jnp.int32, (TILE, width), 1)
            causal = rows >= cols
            sc = scores_ref[r0 : r0 + TILE, 0:width]
            parts = []
            for j in range(2):
                h = 2 * q + j
                ct = cumg_ref[0, r0 : r0 + TILE, h : h + 1]
                cs = cumt_ref[h : h + 1, 0:width]
                st = stept_ref[h : h + 1, 0:width]
                w = jnp.where(causal, jnp.exp(ct - cs), 0.0)
                wb = ((sc * w) * st).astype(jnp.bfloat16)
                parts.append(jnp.dot(wb, x[0:width], preferred_element_type=jnp.float32))
            xt = x[r0 : r0 + TILE].astype(jnp.float32)
            total = lane_pick(parts[0], parts[1]) + skip * xt
            out_ref[r0 : r0 + TILE, 128 * q : 128 * (q + 1)] = total


def combine_kernel(place_ref, *refs):
    if len(refs) == 6:
        refs = refs[1:]
    part_ref, gath_ref, cumg_ref, c_ref, out_ref = refs
    here = place_ref[0]
    peers = gath_ref.shape[0]
    pairs = gath_ref.shape[1]
    state_size = c_ref.shape[1]
    for q in range(pairs):
        run = jnp.ones((1, 128), jnp.float32)
        state = jnp.zeros((state_size, 128), jnp.float32)
        for k in range(peers - 1, -1, -1):
            if k + 1 < peers:
                later = gath_ref[k + 1, q, state_size : state_size + 1, :]
                run = jnp.where(k + 1 < here, run * later, 1.0)
            weight = jnp.where(k < here, run, 0.0)
            state = state + weight * gath_ref[k, q, 0:state_size, :]
        readable = state.astype(jnp.bfloat16)
        inherited = jnp.dot(c_ref[...], readable, preferred_element_type=jnp.float32)
        decay = lane_pick(
            jnp.exp(cumg_ref[0, :, 2 * q : 2 * q + 1]), jnp.exp(cumg_ref[0, :, 2 * q + 1 : 2 * q + 2])
        )
        total = part_ref[:, 128 * q : 128 * (q + 1)] + decay * inherited
        out_ref[:, 128 * q : 128 * (q + 1)] = total.astype(out_ref.dtype)


def arbitrary():
    return pltpu.CompilerParams(dimension_semantics=("arbitrary",))


def carried_call(bt, fac_grouped, decay_lanes, tokens, first):
    length, width = tokens.shape
    groups = width // (GROUP * 64)
    state_size = bt.shape[0]
    return pl.pallas_call(
        carried_kernel,
        grid=(groups,),
        in_specs=[
            pl.BlockSpec(bt.shape, lambda g: (0, 0)),
            pl.BlockSpec((1, length, GROUP), lambda g: (g + first, 0, 0)),
            pl.BlockSpec((1, GROUP * 64), lambda g: (0, g + first)),
            pl.BlockSpec((length, GROUP * 64), lambda g: (0, g)),
        ],
        out_specs=pl.BlockSpec((GROUP // 2, state_size + EXTRA, 128), lambda g: (g, 0, 0)),
        out_shape=jax.ShapeDtypeStruct((width // 128, state_size + EXTRA, 128), jnp.float32),
        compiler_params=arbitrary(),
    )(bt, fac_grouped, decay_lanes, tokens)


def local_call(scores, cum_grouped, cum_t, step_t, tokens, skip_lanes, first):
    length, width = tokens.shape
    groups = width // (GROUP * 64)
    return pl.pallas_call(
        local_kernel,
        grid=(groups,),
        in_specs=[
            pl.BlockSpec((length, length), lambda g: (0, 0)),
            pl.BlockSpec((1, length, GROUP), lambda g: (g + first, 0, 0)),
            pl.BlockSpec((GROUP, length), lambda g: (g + first, 0)),
            pl.BlockSpec((GROUP, length), lambda g: (g + first, 0)),
            pl.BlockSpec((length, GROUP * 64), lambda g: (0, g)),
            pl.BlockSpec((1, GROUP * 64), lambda g: (0, g + first)),
        ],
        out_specs=pl.BlockSpec((length, GROUP * 64), lambda g: (0, g)),
        out_shape=jax.ShapeDtypeStruct((length, width), jnp.float32),
        compiler_params=arbitrary(),
    )(scores, cum_grouped, cum_t, step_t, tokens, skip_lanes)


def combine_call(buffer, place, partial, gathered, cum_grouped, readout, first, total_width):
    length, width = partial.shape
    groups = width // (GROUP * 64)
    state_rows = gathered.shape[2]
    in_specs = [
        pl.BlockSpec((length, GROUP * 64), lambda g: (0, g)),
        pl.BlockSpec((gathered.shape[0], GROUP // 2, state_rows, 128), lambda g: (0, g, 0, 0)),
        pl.BlockSpec((1, length, GROUP), lambda g: (g + first, 0, 0)),
        pl.BlockSpec(readout.shape, lambda g: (0, 0)),
    ]
    operands = [partial, gathered, cum_grouped, readout]
    aliases = {}
    if buffer is not None:
        in_specs = [pl.BlockSpec(memory_space=pl.ANY)] + in_specs
        operands = [buffer] + operands
        aliases = {1: 0}
    return pl.pallas_call(
        combine_kernel,
        grid=(groups,),
        in_specs=[pl.BlockSpec(memory_space=pltpu.SMEM)] + in_specs,
        out_specs=pl.BlockSpec((length, GROUP * 64), lambda g: (0, g + first)),
        out_shape=jax.ShapeDtypeStruct((length, total_width), jnp.bfloat16),
        input_output_aliases=aliases,
        compiler_params=arbitrary(),
    )(place, *operands)


def deliver(rows, pick_rows, flat_rows, stream_count, capacity):
    width = rows.shape[1]
    send = jnp.take(rows, pick_rows, axis=0, mode="clip").reshape(stream_count, capacity, width)
    arrived = lax.all_to_all(send, "stream", split_axis=0, concat_axis=0, tiled=True)
    return jnp.take(
        arrived.reshape(stream_count * capacity, width), flat_rows, axis=0, mode="clip"
    )


def on_device(tokens_in, proj_in, step_raw, decay_log, head_skip_weight, row_counts):
    stream_count = lax.axis_size("stream")
    stream_index = lax.axis_index("stream")
    place_index = lax.axis_index("pos")
    tokens = tokens_in[0]
    local_rows, inner = tokens.shape
    head_count = step_raw.shape[2]
    head_size = inner // head_count
    state_size = proj_in.shape[2] // 2
    capacity = 3 * local_rows // (2 * stream_count)

    place_counts = lax.dynamic_index_in_dim(row_counts, place_index, 0, keepdims=False)
    send_counts = lax.dynamic_index_in_dim(place_counts, stream_index, 0, keepdims=False)
    recv_counts = lax.dynamic_index_in_dim(place_counts, stream_index, 1, keepdims=False)
    send_start = jnp.cumsum(send_counts) - send_counts
    slot_range = jnp.arange(capacity, dtype=jnp.int32)
    pick_rows = jnp.clip(send_start[:, None] + slot_range[None, :], 0, local_rows - 1).reshape(-1)
    recv_end = jnp.cumsum(recv_counts)
    recv_start = recv_end - recv_counts
    positions = jnp.arange(local_rows, dtype=jnp.int32)
    source = jnp.sum((recv_end[:, None] <= positions[None, :]).astype(jnp.int32), axis=0)
    source = jnp.clip(source, 0, stream_count - 1)
    source_start = jnp.take(recv_start, source)
    flat_rows = source * capacity + positions - source_start

    ordered_proj = deliver(proj_in[0], pick_rows, flat_rows, stream_count, capacity)
    ordered_steps = deliver(step_raw[0], pick_rows, flat_rows, stream_count, capacity)

    inputs = ordered_proj[:, :state_size]
    readout = ordered_proj[:, state_size:]
    decay_rates = -jnp.exp(decay_log)
    steps = jax.nn.softplus(ordered_steps.astype(jnp.float32))
    cum = jnp.cumsum(steps * decay_rates[None, :], axis=0)
    ending = cum[-1]
    factor = jnp.exp(ending[None, :] - cum) * steps
    groups = head_count // GROUP

    def grouped(a):
        return a.reshape(local_rows, groups, GROUP).transpose(1, 0, 2)

    cum_grouped = grouped(cum)
    fac_grouped = grouped(factor)
    cum_t = cum.T
    step_t = steps.T
    decay_lanes = jnp.repeat(jnp.exp(ending), head_size).reshape(1, -1)
    skip_lanes = jnp.repeat(head_skip_weight, head_size).reshape(1, -1)
    scores = jnp.dot(readout, inputs.T, preferred_element_type=jnp.float32)
    bt = inputs.T
    place = place_index.astype(jnp.int32).reshape(1)

    width = inner // CHUNKS
    groups_per_chunk = groups // CHUNKS
    pieces = []
    for c in range(CHUNKS):
        chunk_tokens = deliver(
            tokens[:, c * width : (c + 1) * width], pick_rows, flat_rows, stream_count, capacity
        )
        first = c * groups_per_chunk
        carried = carried_call(bt, fac_grouped, decay_lanes, chunk_tokens, first)
        gathered = lax.all_gather(carried, "pos")
        partial = local_call(scores, cum_grouped, cum_t, step_t, chunk_tokens, skip_lanes, first)
        pieces.append((partial, gathered, first))
    result = None
    for partial, gathered, first in pieces:
        result = combine_call(
            result, place, partial, gathered, cum_grouped, readout, first, inner
        )
    return result[None]


def solution(mesh):
    in_specs = (
        P("stream", "pos", None),
        P("stream", "pos", None),
        P("stream", "pos", None),
        P(),
        P(),
        P(),
    )
    out_specs = P("stream", "pos", None)
    return jax.shard_map(
        on_device, mesh=mesh, in_specs=in_specs, out_specs=out_specs, check_vma=False
    )
```

```python
import jax
import jax.numpy as jnp
from jax import lax
from jax.experimental import pallas as pl
from jax.experimental.pallas import tpu as pltpu
from jax.sharding import PartitionSpec as P

GROUP = 8
TILE = 128
CHUNKS = 4
EXTRA = 8


def lane_pick(low, high):
    lane_low = lax.broadcasted_iota(jnp.int32, (1, 128), 1) < 64
    return jnp.where(lane_low, low, high)


def carried_kernel(bt_ref, facg_ref, decay_ref, tok_ref, out_ref):
    pairs = out_ref.shape[0]
    state_size = bt_ref.shape[0]
    for q in range(pairs):
        x = tok_ref[:, 128 * q : 128 * (q + 1)].astype(jnp.float32)
        factor = lane_pick(facg_ref[0, :, 2 * q : 2 * q + 1], facg_ref[0, :, 2 * q + 1 : 2 * q + 2])
        scaled = (factor * x).astype(jnp.bfloat16)
        out_ref[q, 0:state_size, :] = jnp.dot(
            bt_ref[...], scaled, preferred_element_type=jnp.float32
        )
        rows = lax.broadcasted_iota(jnp.int32, (EXTRA, 128), 0)
        decay = decay_ref[:, 128 * q : 128 * (q + 1)]
        out_ref[q, state_size : state_size + EXTRA, :] = jnp.where(rows == 0, decay, 0.0)


def local_kernel(scores_ref, cumg_ref, cumt_ref, stept_ref, tok_ref, skip_ref, out_ref):
    length = scores_ref.shape[0]
    heads = cumt_ref.shape[0]
    for q in range(heads // 2):
        x = tok_ref[:, 128 * q : 128 * (q + 1)]
        skip = skip_ref[:, 128 * q : 128 * (q + 1)]
        for i in range(length // TILE):
            r0 = i * TILE
            width = (i + 1) * TILE
            rows = lax.broadcasted_iota(jnp.int32, (TILE, width), 0) + r0
            cols = lax.broadcasted_iota(jnp.int32, (TILE, width), 1)
            causal = rows >= cols
            sc = scores_ref[r0 : r0 + TILE, 0:width]
            parts = []
            for j in range(2):
                h = 2 * q + j
                ct = cumg_ref[0, r0 : r0 + TILE, h : h + 1]
                cs = cumt_ref[h : h + 1, 0:width]
                st = stept_ref[h : h + 1, 0:width]
                w = jnp.where(causal, jnp.exp(ct - cs), 0.0)
                wb = ((sc * w) * st).astype(jnp.bfloat16)
                parts.append(jnp.dot(wb, x[0:width], preferred_element_type=jnp.float32))
            xt = x[r0 : r0 + TILE].astype(jnp.float32)
            total = lane_pick(parts[0], parts[1]) + skip * xt
            out_ref[r0 : r0 + TILE, 128 * q : 128 * (q + 1)] = total


def combine_kernel(place_ref, *refs):
    if len(refs) == 6:
        refs = refs[1:]
    part_ref, gath_ref, cumg_ref, c_ref, out_ref = refs
    here = place_ref[0]
    peers = gath_ref.shape[0]
    pairs = gath_ref.shape[1]
    state_size = c_ref.shape[1]
    for q in range(pairs):
        run = jnp.ones((1, 128), jnp.float32)
        state = jnp.zeros((state_size, 128), jnp.float32)
        for k in range(peers - 1, -1, -1):
            if k + 1 < peers:
                later = gath_ref[k + 1, q, state_size : state_size + 1, :]
                run = jnp.where(k + 1 < here, run * later, 1.0)
            weight = jnp.where(k < here, run, 0.0)
            state = state + weight * gath_ref[k, q, 0:state_size, :]
        readable = state.astype(jnp.bfloat16)
        inherited = jnp.dot(c_ref[...], readable, preferred_element_type=jnp.float32)
        decay = lane_pick(
            jnp.exp(cumg_ref[0, :, 2 * q : 2 * q + 1]), jnp.exp(cumg_ref[0, :, 2 * q + 1 : 2 * q + 2])
        )
        total = part_ref[:, 128 * q : 128 * (q + 1)] + decay * inherited
        out_ref[:, 128 * q : 128 * (q + 1)] = total.astype(out_ref.dtype)


def arbitrary():
    return pltpu.CompilerParams(dimension_semantics=("arbitrary",))


def carried_call(bt, fac_grouped, decay_lanes, tokens, first):
    length, width = tokens.shape
    groups = width // (GROUP * 64)
    state_size = bt.shape[0]
    return pl.pallas_call(
        carried_kernel,
        grid=(groups,),
        in_specs=[
            pl.BlockSpec(bt.shape, lambda g: (0, 0)),
            pl.BlockSpec((1, length, GROUP), lambda g: (g + first, 0, 0)),
            pl.BlockSpec((1, GROUP * 64), lambda g: (0, g + first)),
            pl.BlockSpec((length, GROUP * 64), lambda g: (0, g)),
        ],
        out_specs=pl.BlockSpec((GROUP // 2, state_size + EXTRA, 128), lambda g: (g, 0, 0)),
        out_shape=jax.ShapeDtypeStruct((width // 128, state_size + EXTRA, 128), jnp.float32),
        compiler_params=arbitrary(),
    )(bt, fac_grouped, decay_lanes, tokens)


def local_call(scores, cum_grouped, cum_t, step_t, tokens, skip_lanes, first):
    length, width = tokens.shape
    groups = width // (GROUP * 64)
    return pl.pallas_call(
        local_kernel,
        grid=(groups,),
        in_specs=[
            pl.BlockSpec((length, length), lambda g: (0, 0)),
            pl.BlockSpec((1, length, GROUP), lambda g: (g + first, 0, 0)),
            pl.BlockSpec((GROUP, length), lambda g: (g + first, 0)),
            pl.BlockSpec((GROUP, length), lambda g: (g + first, 0)),
            pl.BlockSpec((length, GROUP * 64), lambda g: (0, g)),
            pl.BlockSpec((1, GROUP * 64), lambda g: (0, g + first)),
        ],
        out_specs=pl.BlockSpec((length, GROUP * 64), lambda g: (0, g)),
        out_shape=jax.ShapeDtypeStruct((length, width), jnp.float32),
        compiler_params=arbitrary(),
    )(scores, cum_grouped, cum_t, step_t, tokens, skip_lanes)


def combine_call(buffer, place, partial, gathered, cum_grouped, readout, first, total_width):
    length, width = partial.shape
    groups = width // (GROUP * 64)
    state_rows = gathered.shape[2]
    in_specs = [
        pl.BlockSpec((length, GROUP * 64), lambda g: (0, g)),
        pl.BlockSpec((gathered.shape[0], GROUP // 2, state_rows, 128), lambda g: (0, g, 0, 0)),
        pl.BlockSpec((1, length, GROUP), lambda g: (g + first, 0, 0)),
        pl.BlockSpec(readout.shape, lambda g: (0, 0)),
    ]
    operands = [partial, gathered, cum_grouped, readout]
    aliases = {}
    if buffer is not None:
        in_specs = [pl.BlockSpec(memory_space=pl.ANY)] + in_specs
        operands = [buffer] + operands
        aliases = {1: 0}
    return pl.pallas_call(
        combine_kernel,
        grid=(groups,),
        in_specs=[pl.BlockSpec(memory_space=pltpu.SMEM)] + in_specs,
        out_specs=pl.BlockSpec((length, GROUP * 64), lambda g: (0, g + first)),
        out_shape=jax.ShapeDtypeStruct((length, total_width), jnp.bfloat16),
        input_output_aliases=aliases,
        compiler_params=arbitrary(),
    )(place, *operands)


def deliver(rows, pick_rows, flat_rows, stream_count, capacity, previous=None):
    width = rows.shape[1]
    send = jnp.take(rows, pick_rows, axis=0, mode="clip").reshape(stream_count, capacity, width)
    arrived = lax.all_to_all(send, "stream", split_axis=0, concat_axis=0, tiled=True)
    if previous is not None:
        arrived, _ = lax.optimization_barrier((arrived, previous))
    return jnp.take(
        arrived.reshape(stream_count * capacity, width), flat_rows, axis=0, mode="clip"
    )


def on_device(tokens_in, proj_in, step_raw, decay_log, head_skip_weight, row_counts):
    stream_count = lax.axis_size("stream")
    stream_index = lax.axis_index("stream")
    place_index = lax.axis_index("pos")
    tokens = tokens_in[0]
    local_rows, inner = tokens.shape
    head_count = step_raw.shape[2]
    head_size = inner // head_count
    state_size = proj_in.shape[2] // 2
    capacity = 3 * local_rows // (2 * stream_count)

    place_counts = lax.dynamic_index_in_dim(row_counts, place_index, 0, keepdims=False)
    send_counts = lax.dynamic_index_in_dim(place_counts, stream_index, 0, keepdims=False)
    recv_counts = lax.dynamic_index_in_dim(place_counts, stream_index, 1, keepdims=False)
    send_start = jnp.cumsum(send_counts) - send_counts
    slot_range = jnp.arange(capacity, dtype=jnp.int32)
    pick_rows = jnp.clip(send_start[:, None] + slot_range[None, :], 0, local_rows - 1).reshape(-1)
    recv_end = jnp.cumsum(recv_counts)
    recv_start = recv_end - recv_counts
    positions = jnp.arange(local_rows, dtype=jnp.int32)
    source = jnp.sum((recv_end[:, None] <= positions[None, :]).astype(jnp.int32), axis=0)
    source = jnp.clip(source, 0, stream_count - 1)
    source_start = jnp.take(recv_start, source)
    flat_rows = source * capacity + positions - source_start

    small = jnp.concatenate([proj_in[0], step_raw[0]], axis=1)
    ordered_small = deliver(small, pick_rows, flat_rows, stream_count, capacity)
    ordered_proj = ordered_small[:, : 2 * state_size]
    ordered_steps = ordered_small[:, 2 * state_size :]

    inputs = ordered_proj[:, :state_size]
    readout = ordered_proj[:, state_size:]
    decay_rates = -jnp.exp(decay_log)
    steps = jax.nn.softplus(ordered_steps.astype(jnp.float32))
    cum = jnp.cumsum(steps * decay_rates[None, :], axis=0)
    ending = cum[-1]
    factor = jnp.exp(ending[None, :] - cum) * steps
    groups = head_count // GROUP

    def grouped(a):
        return a.reshape(local_rows, groups, GROUP).transpose(1, 0, 2)

    cum_grouped = grouped(cum)
    fac_grouped = grouped(factor)
    cum_t = cum.T
    step_t = steps.T
    decay_lanes = jnp.repeat(jnp.exp(ending), head_size).reshape(1, -1)
    skip_lanes = jnp.repeat(head_skip_weight, head_size).reshape(1, -1)
    scores = jnp.dot(readout, inputs.T, preferred_element_type=jnp.float32)
    bt = inputs.T
    place = place_index.astype(jnp.int32).reshape(1)

    width = inner // CHUNKS
    groups_per_chunk = groups // CHUNKS
    pieces = []
    previous = None
    for c in range(CHUNKS):
        chunk_tokens = deliver(
            tokens[:, c * width : (c + 1) * width], pick_rows, flat_rows, stream_count, capacity,
            previous,
        )
        first = c * groups_per_chunk
        carried = carried_call(bt, fac_grouped, decay_lanes, chunk_tokens, first)
        gathered = lax.all_gather(carried, "pos")
        partial = local_call(scores, cum_grouped, cum_t, step_t, chunk_tokens, skip_lanes, first)
        pieces.append((partial, gathered, first))
        previous = partial
    result = None
    for partial, gathered, first in pieces:
        result = combine_call(
            result, place, partial, gathered, cum_grouped, readout, first, inner
        )
    return result[None]


def solution(mesh):
    in_specs = (
        P("stream", "pos", None),
        P("stream", "pos", None),
        P("stream", "pos", None),
        P(),
        P(),
        P(),
    )
    out_specs = P("stream", "pos", None)
    return jax.shard_map(
        on_device, mesh=mesh, in_specs=in_specs, out_specs=out_specs, check_vma=False
    )
```

```python
import jax
import jax.numpy as jnp
from jax import lax
from jax.experimental import pallas as pl
from jax.experimental.pallas import tpu as pltpu
from jax.sharding import PartitionSpec as P

GROUP = 8
TILE = 128
CHUNK_GROUPS = (2, 4, 4, 4, 2)
EXTRA = 8


def lane_pick(low, high):
    lane_low = lax.broadcasted_iota(jnp.int32, (1, 128), 1) < 64
    return jnp.where(lane_low, low, high)


def carried_kernel(bt_ref, facg_ref, decay_ref, tok_ref, out_ref):
    pairs = out_ref.shape[0]
    state_size = bt_ref.shape[0]
    for q in range(pairs):
        x = tok_ref[:, 128 * q : 128 * (q + 1)].astype(jnp.float32)
        factor = lane_pick(facg_ref[0, :, 2 * q : 2 * q + 1], facg_ref[0, :, 2 * q + 1 : 2 * q + 2])
        scaled = (factor * x).astype(jnp.bfloat16)
        out_ref[q, 0:state_size, :] = jnp.dot(
            bt_ref[...], scaled, preferred_element_type=jnp.float32
        )
        rows = lax.broadcasted_iota(jnp.int32, (EXTRA, 128), 0)
        decay = decay_ref[:, 128 * q : 128 * (q + 1)]
        out_ref[q, state_size : state_size + EXTRA, :] = jnp.where(rows == 0, decay, 0.0)


def local_kernel(scores_ref, cumg_ref, cumt_ref, stept_ref, tok_ref, skip_ref, out_ref):
    length = scores_ref.shape[0]
    heads = cumt_ref.shape[0]
    for q in range(heads // 2):
        x = tok_ref[:, 128 * q : 128 * (q + 1)]
        skip = skip_ref[:, 128 * q : 128 * (q + 1)]
        for i in range(length // TILE):
            r0 = i * TILE
            width = (i + 1) * TILE
            rows = lax.broadcasted_iota(jnp.int32, (TILE, width), 0) + r0
            cols = lax.broadcasted_iota(jnp.int32, (TILE, width), 1)
            causal = rows >= cols
            sc = scores_ref[r0 : r0 + TILE, 0:width]
            parts = []
            for j in range(2):
                h = 2 * q + j
                ct = cumg_ref[0, r0 : r0 + TILE, h : h + 1]
                cs = cumt_ref[h : h + 1, 0:width]
                st = stept_ref[h : h + 1, 0:width]
                w = jnp.where(causal, jnp.exp(ct - cs), 0.0)
                wb = ((sc * w) * st).astype(jnp.bfloat16)
                parts.append(jnp.dot(wb, x[0:width], preferred_element_type=jnp.float32))
            xt = x[r0 : r0 + TILE].astype(jnp.float32)
            total = lane_pick(parts[0], parts[1]) + skip * xt
            out_ref[r0 : r0 + TILE, 128 * q : 128 * (q + 1)] = total


def combine_kernel(place_ref, *refs):
    if len(refs) == 6:
        refs = refs[1:]
    part_ref, gath_ref, cumg_ref, c_ref, out_ref = refs
    here = place_ref[0]
    peers = gath_ref.shape[0]
    pairs = gath_ref.shape[1]
    state_size = c_ref.shape[1]
    for q in range(pairs):
        run = jnp.ones((1, 128), jnp.float32)
        state = jnp.zeros((state_size, 128), jnp.float32)
        for k in range(peers - 1, -1, -1):
            if k + 1 < peers:
                later = gath_ref[k + 1, q, state_size : state_size + 1, :]
                run = jnp.where(k + 1 < here, run * later, 1.0)
            weight = jnp.where(k < here, run, 0.0)
            state = state + weight * gath_ref[k, q, 0:state_size, :]
        readable = state.astype(jnp.bfloat16)
        inherited = jnp.dot(c_ref[...], readable, preferred_element_type=jnp.float32)
        decay = lane_pick(
            jnp.exp(cumg_ref[0, :, 2 * q : 2 * q + 1]), jnp.exp(cumg_ref[0, :, 2 * q + 1 : 2 * q + 2])
        )
        total = part_ref[:, 128 * q : 128 * (q + 1)] + decay * inherited
        out_ref[:, 128 * q : 128 * (q + 1)] = total.astype(out_ref.dtype)


def arbitrary():
    return pltpu.CompilerParams(dimension_semantics=("arbitrary",))


def carried_call(bt, fac_grouped, decay_lanes, tokens, first):
    length, width = tokens.shape
    groups = width // (GROUP * 64)
    state_size = bt.shape[0]
    return pl.pallas_call(
        carried_kernel,
        grid=(groups,),
        in_specs=[
            pl.BlockSpec(bt.shape, lambda g: (0, 0)),
            pl.BlockSpec((1, length, GROUP), lambda g: (g + first, 0, 0)),
            pl.BlockSpec((1, GROUP * 64), lambda g: (0, g + first)),
            pl.BlockSpec((length, GROUP * 64), lambda g: (0, g)),
        ],
        out_specs=pl.BlockSpec((GROUP // 2, state_size + EXTRA, 128), lambda g: (g, 0, 0)),
        out_shape=jax.ShapeDtypeStruct((width // 128, state_size + EXTRA, 128), jnp.float32),
        compiler_params=arbitrary(),
    )(bt, fac_grouped, decay_lanes, tokens)


def local_call(scores, cum_grouped, cum_t, step_t, tokens, skip_lanes, first):
    length, width = tokens.shape
    groups = width // (GROUP * 64)
    return pl.pallas_call(
        local_kernel,
        grid=(groups,),
        in_specs=[
            pl.BlockSpec((length, length), lambda g: (0, 0)),
            pl.BlockSpec((1, length, GROUP), lambda g: (g + first, 0, 0)),
            pl.BlockSpec((GROUP, length), lambda g: (g + first, 0)),
            pl.BlockSpec((GROUP, length), lambda g: (g + first, 0)),
            pl.BlockSpec((length, GROUP * 64), lambda g: (0, g)),
            pl.BlockSpec((1, GROUP * 64), lambda g: (0, g + first)),
        ],
        out_specs=pl.BlockSpec((length, GROUP * 64), lambda g: (0, g)),
        out_shape=jax.ShapeDtypeStruct((length, width), jnp.float32),
        compiler_params=arbitrary(),
    )(scores, cum_grouped, cum_t, step_t, tokens, skip_lanes)


def combine_call(buffer, place, partial, gathered, cum_grouped, readout, first, total_width):
    length, width = partial.shape
    groups = width // (GROUP * 64)
    state_rows = gathered.shape[2]
    in_specs = [
        pl.BlockSpec((length, GROUP * 64), lambda g: (0, g)),
        pl.BlockSpec((gathered.shape[0], GROUP // 2, state_rows, 128), lambda g: (0, g, 0, 0)),
        pl.BlockSpec((1, length, GROUP), lambda g: (g + first, 0, 0)),
        pl.BlockSpec(readout.shape, lambda g: (0, 0)),
    ]
    operands = [partial, gathered, cum_grouped, readout]
    aliases = {}
    if buffer is not None:
        in_specs = [pl.BlockSpec(memory_space=pl.ANY)] + in_specs
        operands = [buffer] + operands
        aliases = {1: 0}
    return pl.pallas_call(
        combine_kernel,
        grid=(groups,),
        in_specs=[pl.BlockSpec(memory_space=pltpu.SMEM)] + in_specs,
        out_specs=pl.BlockSpec((length, GROUP * 64), lambda g: (0, g + first)),
        out_shape=jax.ShapeDtypeStruct((length, total_width), jnp.bfloat16),
        input_output_aliases=aliases,
        compiler_params=arbitrary(),
    )(place, *operands)


def send_rows(rows, pick_rows, stream_count, capacity):
    width = rows.shape[1]
    return jnp.take(rows, pick_rows, axis=0, mode="clip").reshape(stream_count, capacity, width)


def receive_rows(arrived, flat_rows):
    width = arrived.shape[2]
    return jnp.take(arrived.reshape(-1, width), flat_rows, axis=0, mode="clip")


def deliver(rows, pick_rows, flat_rows, stream_count, capacity):
    send = send_rows(rows, pick_rows, stream_count, capacity)
    arrived = lax.all_to_all(send, "stream", split_axis=0, concat_axis=0, tiled=True)
    return receive_rows(arrived, flat_rows)


def on_device(tokens_in, proj_in, step_raw, decay_log, head_skip_weight, row_counts):
    stream_count = lax.axis_size("stream")
    stream_index = lax.axis_index("stream")
    place_index = lax.axis_index("pos")
    tokens = tokens_in[0]
    local_rows, inner = tokens.shape
    head_count = step_raw.shape[2]
    head_size = inner // head_count
    state_size = proj_in.shape[2] // 2
    capacity = 3 * local_rows // (2 * stream_count)

    place_counts = lax.dynamic_index_in_dim(row_counts, place_index, 0, keepdims=False)
    send_counts = lax.dynamic_index_in_dim(place_counts, stream_index, 0, keepdims=False)
    recv_counts = lax.dynamic_index_in_dim(place_counts, stream_index, 1, keepdims=False)
    send_start = jnp.cumsum(send_counts) - send_counts
    slot_range = jnp.arange(capacity, dtype=jnp.int32)
    pick_rows = jnp.clip(send_start[:, None] + slot_range[None, :], 0, local_rows - 1).reshape(-1)
    recv_end = jnp.cumsum(recv_counts)
    recv_start = recv_end - recv_counts
    positions = jnp.arange(local_rows, dtype=jnp.int32)
    source = jnp.sum((recv_end[:, None] <= positions[None, :]).astype(jnp.int32), axis=0)
    source = jnp.clip(source, 0, stream_count - 1)
    source_start = jnp.take(recv_start, source)
    flat_rows = source * capacity + positions - source_start

    small = jnp.concatenate([proj_in[0], step_raw[0]], axis=1)
    ordered_small = deliver(small, pick_rows, flat_rows, stream_count, capacity)
    ordered_proj = ordered_small[:, : 2 * state_size]
    ordered_steps = ordered_small[:, 2 * state_size :]

    inputs = ordered_proj[:, :state_size]
    readout = ordered_proj[:, state_size:]
    decay_rates = -jnp.exp(decay_log)
    steps = jax.nn.softplus(ordered_steps.astype(jnp.float32))
    cum = jnp.cumsum(steps * decay_rates[None, :], axis=0)
    ending = cum[-1]
    factor = jnp.exp(ending[None, :] - cum) * steps
    groups = head_count // GROUP

    def grouped(a):
        return a.reshape(local_rows, groups, GROUP).transpose(1, 0, 2)

    cum_grouped = grouped(cum)
    fac_grouped = grouped(factor)
    cum_t = cum.T
    step_t = steps.T
    decay_lanes = jnp.repeat(jnp.exp(ending), head_size).reshape(1, -1)
    skip_lanes = jnp.repeat(head_skip_weight, head_size).reshape(1, -1)
    scores = jnp.dot(readout, inputs.T, preferred_element_type=jnp.float32)
    bt = inputs.T
    place = place_index.astype(jnp.int32).reshape(1)

    sizes = CHUNK_GROUPS
    firsts = [sum(sizes[:c]) for c in range(len(sizes))]
    group_width = GROUP * head_size
    sends = [
        send_rows(tokens[:, f * group_width : (f + n) * group_width], pick_rows, stream_count, capacity)
        for f, n in zip(firsts, sizes)
    ]
    partials = []
    gathers = []
    result = None
    done = 0
    for c in range(len(sizes)):
        arrived = lax.all_to_all(sends[c], "stream", split_axis=0, concat_axis=0, tiled=True)
        tied = {"arrived": arrived}
        if c + 1 < len(sizes):
            tied["send"] = sends[c + 1]
        if c >= 1:
            tied["partial"] = partials[c - 1]
        if c >= 2:
            result = combine_call(
                result, place, partials[done], gathers[done], cum_grouped, readout,
                firsts[done], inner,
            )
            done += 1
            tied["result"] = result
        tied = lax.optimization_barrier(tied)
        arrived = tied["arrived"]
        if c + 1 < len(sizes):
            sends[c + 1] = tied["send"]
        if c >= 2:
            result = tied["result"]
        chunk_tokens = receive_rows(arrived, flat_rows)
        carried = carried_call(bt, fac_grouped, decay_lanes, chunk_tokens, firsts[c])
        gathers.append(lax.all_gather(carried, "pos"))
        partials.append(
            local_call(scores, cum_grouped, cum_t, step_t, chunk_tokens, skip_lanes, firsts[c])
        )
    while done < len(sizes):
        result = combine_call(
            result, place, partials[done], gathers[done], cum_grouped, readout, firsts[done], inner
        )
        done += 1
    return result[None]


def solution(mesh):
    in_specs = (
        P("stream", "pos", None),
        P("stream", "pos", None),
        P("stream", "pos", None),
        P(),
        P(),
        P(),
    )
    out_specs = P("stream", "pos", None)
    return jax.shard_map(
        on_device, mesh=mesh, in_specs=in_specs, out_specs=out_specs, check_vma=False
    )
```

```python
import jax
import jax.numpy as jnp
from jax import lax
from jax.experimental import pallas as pl
from jax.experimental.pallas import tpu as pltpu
from jax.sharding import PartitionSpec as P

GROUP = 8
TILE = 128
CHUNK_GROUPS = (4, 4, 4, 4)
EXTRA = 16


def lane_pick(low, high):
    lane_low = lax.broadcasted_iota(jnp.int32, (1, 128), 1) < 64
    return jnp.where(lane_low, low, high)


def carried_kernel(bt_ref, facg_ref, decay_ref, tok_ref, out_ref):
    pairs = out_ref.shape[0]
    state_size = bt_ref.shape[0]
    for q in range(pairs):
        x = tok_ref[:, 128 * q : 128 * (q + 1)].astype(jnp.float32)
        factor = lane_pick(facg_ref[0, :, 2 * q : 2 * q + 1], facg_ref[0, :, 2 * q + 1 : 2 * q + 2])
        scaled = (factor * x).astype(jnp.bfloat16)
        out_ref[q, 0:state_size, :] = jnp.dot(
            bt_ref[...], scaled, preferred_element_type=jnp.float32
        ).astype(out_ref.dtype)
        rows = lax.broadcasted_iota(jnp.int32, (EXTRA, 128), 0)
        decay = decay_ref[:, 128 * q : 128 * (q + 1)]
        high = decay.astype(out_ref.dtype)
        low = (decay - high.astype(jnp.float32)).astype(out_ref.dtype)
        extra = jnp.where(rows == 0, high, jnp.where(rows == 1, low, jnp.zeros_like(high)))
        out_ref[q, state_size : state_size + EXTRA, :] = extra


def local_kernel(scores_ref, cumg_ref, cumt_ref, stept_ref, tok_ref, skip_ref, out_ref):
    length = scores_ref.shape[0]
    heads = cumt_ref.shape[0]
    for q in range(heads // 2):
        x = tok_ref[:, 128 * q : 128 * (q + 1)]
        skip = skip_ref[:, 128 * q : 128 * (q + 1)]
        for i in range(length // TILE):
            r0 = i * TILE
            width = (i + 1) * TILE
            rows = lax.broadcasted_iota(jnp.int32, (TILE, width), 0) + r0
            cols = lax.broadcasted_iota(jnp.int32, (TILE, width), 1)
            causal = rows >= cols
            sc = scores_ref[r0 : r0 + TILE, 0:width]
            parts = []
            for j in range(2):
                h = 2 * q + j
                ct = cumg_ref[0, r0 : r0 + TILE, h : h + 1]
                cs = cumt_ref[h : h + 1, 0:width]
                st = stept_ref[h : h + 1, 0:width]
                w = jnp.where(causal, jnp.exp(ct - cs), 0.0)
                wb = ((sc * w) * st).astype(jnp.bfloat16)
                parts.append(jnp.dot(wb, x[0:width], preferred_element_type=jnp.float32))
            xt = x[r0 : r0 + TILE].astype(jnp.float32)
            total = lane_pick(parts[0], parts[1]) + skip * xt
            out_ref[r0 : r0 + TILE, 128 * q : 128 * (q + 1)] = total


def combine_kernel(place_ref, *refs):
    if len(refs) == 6:
        refs = refs[1:]
    part_ref, gath_ref, cumg_ref, c_ref, out_ref = refs
    here = place_ref[0]
    peers = gath_ref.shape[0]
    pairs = gath_ref.shape[1]
    state_size = c_ref.shape[1]
    for q in range(pairs):
        run = jnp.ones((1, 128), jnp.float32)
        state = jnp.zeros((state_size, 128), jnp.float32)
        for k in range(peers - 1, -1, -1):
            if k + 1 < peers:
                pair = gath_ref[k + 1, q, state_size : state_size + 2, :].astype(jnp.float32)
                later = pair[0:1] + pair[1:2]
                run = jnp.where(k + 1 < here, run * later, 1.0)
            weight = jnp.where(k < here, run, 0.0)
            state = state + weight * gath_ref[k, q, 0:state_size, :].astype(jnp.float32)
        readable = state.astype(jnp.bfloat16)
        inherited = jnp.dot(c_ref[...], readable, preferred_element_type=jnp.float32)
        decay = lane_pick(
            jnp.exp(cumg_ref[0, :, 2 * q : 2 * q + 1]), jnp.exp(cumg_ref[0, :, 2 * q + 1 : 2 * q + 2])
        )
        total = part_ref[:, 128 * q : 128 * (q + 1)] + decay * inherited
        out_ref[:, 128 * q : 128 * (q + 1)] = total.astype(out_ref.dtype)


def arbitrary():
    return pltpu.CompilerParams(dimension_semantics=("arbitrary",))


def carried_call(bt, fac_grouped, decay_lanes, tokens, first):
    length, width = tokens.shape
    groups = width // (GROUP * 64)
    state_size = bt.shape[0]
    return pl.pallas_call(
        carried_kernel,
        grid=(groups,),
        in_specs=[
            pl.BlockSpec(bt.shape, lambda g: (0, 0)),
            pl.BlockSpec((1, length, GROUP), lambda g: (g + first, 0, 0)),
            pl.BlockSpec((1, GROUP * 64), lambda g: (0, g + first)),
            pl.BlockSpec((length, GROUP * 64), lambda g: (0, g)),
        ],
        out_specs=pl.BlockSpec((GROUP // 2, state_size + EXTRA, 128), lambda g: (g, 0, 0)),
        out_shape=jax.ShapeDtypeStruct((width // 128, state_size + EXTRA, 128), jnp.bfloat16),
        compiler_params=arbitrary(),
    )(bt, fac_grouped, decay_lanes, tokens)


def local_call(scores, cum_grouped, cum_t, step_t, tokens, skip_lanes, first):
    length, width = tokens.shape
    groups = width // (GROUP * 64)
    return pl.pallas_call(
        local_kernel,
        grid=(groups,),
        in_specs=[
            pl.BlockSpec((length, length), lambda g: (0, 0)),
            pl.BlockSpec((1, length, GROUP), lambda g: (g + first, 0, 0)),
            pl.BlockSpec((GROUP, length), lambda g: (g + first, 0)),
            pl.BlockSpec((GROUP, length), lambda g: (g + first, 0)),
            pl.BlockSpec((length, GROUP * 64), lambda g: (0, g)),
            pl.BlockSpec((1, GROUP * 64), lambda g: (0, g + first)),
        ],
        out_specs=pl.BlockSpec((length, GROUP * 64), lambda g: (0, g)),
        out_shape=jax.ShapeDtypeStruct((length, width), jnp.float32),
        compiler_params=arbitrary(),
    )(scores, cum_grouped, cum_t, step_t, tokens, skip_lanes)


def combine_call(buffer, place, partial, gathered, cum_grouped, readout, first, total_width):
    length, width = partial.shape
    groups = width // (GROUP * 64)
    state_rows = gathered.shape[2]
    in_specs = [
        pl.BlockSpec((length, GROUP * 64), lambda g: (0, g)),
        pl.BlockSpec((gathered.shape[0], GROUP // 2, state_rows, 128), lambda g: (0, g, 0, 0)),
        pl.BlockSpec((1, length, GROUP), lambda g: (g + first, 0, 0)),
        pl.BlockSpec(readout.shape, lambda g: (0, 0)),
    ]
    operands = [partial, gathered, cum_grouped, readout]
    aliases = {}
    if buffer is not None:
        in_specs = [pl.BlockSpec(memory_space=pl.ANY)] + in_specs
        operands = [buffer] + operands
        aliases = {1: 0}
    return pl.pallas_call(
        combine_kernel,
        grid=(groups,),
        in_specs=[pl.BlockSpec(memory_space=pltpu.SMEM)] + in_specs,
        out_specs=pl.BlockSpec((length, GROUP * 64), lambda g: (0, g + first)),
        out_shape=jax.ShapeDtypeStruct((length, total_width), jnp.bfloat16),
        input_output_aliases=aliases,
        compiler_params=arbitrary(),
    )(place, *operands)


def send_rows(rows, pick_rows, stream_count, capacity):
    width = rows.shape[1]
    return jnp.take(rows, pick_rows, axis=0, mode="clip").reshape(stream_count, capacity, width)


def receive_rows(arrived, flat_rows):
    width = arrived.shape[2]
    return jnp.take(arrived.reshape(-1, width), flat_rows, axis=0, mode="clip")


def deliver(rows, pick_rows, flat_rows, stream_count, capacity):
    send = send_rows(rows, pick_rows, stream_count, capacity)
    arrived = lax.all_to_all(send, "stream", split_axis=0, concat_axis=0, tiled=True)
    return receive_rows(arrived, flat_rows)


def on_device(tokens_in, proj_in, step_raw, decay_log, head_skip_weight, row_counts):
    stream_count = lax.axis_size("stream")
    stream_index = lax.axis_index("stream")
    place_index = lax.axis_index("pos")
    tokens = tokens_in[0]
    local_rows, inner = tokens.shape
    head_count = step_raw.shape[2]
    head_size = inner // head_count
    state_size = proj_in.shape[2] // 2
    capacity = 3 * local_rows // (2 * stream_count)

    place_counts = lax.dynamic_index_in_dim(row_counts, place_index, 0, keepdims=False)
    send_counts = lax.dynamic_index_in_dim(place_counts, stream_index, 0, keepdims=False)
    recv_counts = lax.dynamic_index_in_dim(place_counts, stream_index, 1, keepdims=False)
    send_start = jnp.cumsum(send_counts) - send_counts
    slot_range = jnp.arange(capacity, dtype=jnp.int32)
    pick_rows = jnp.clip(send_start[:, None] + slot_range[None, :], 0, local_rows - 1).reshape(-1)
    recv_end = jnp.cumsum(recv_counts)
    recv_start = recv_end - recv_counts
    positions = jnp.arange(local_rows, dtype=jnp.int32)
    source = jnp.sum((recv_end[:, None] <= positions[None, :]).astype(jnp.int32), axis=0)
    source = jnp.clip(source, 0, stream_count - 1)
    source_start = jnp.take(recv_start, source)
    flat_rows = source * capacity + positions - source_start

    small = jnp.concatenate([proj_in[0], step_raw[0]], axis=1)
    ordered_small = deliver(small, pick_rows, flat_rows, stream_count, capacity)
    ordered_proj = ordered_small[:, : 2 * state_size]
    ordered_steps = ordered_small[:, 2 * state_size :]

    inputs = ordered_proj[:, :state_size]
    readout = ordered_proj[:, state_size:]
    decay_rates = -jnp.exp(decay_log)
    steps = jax.nn.softplus(ordered_steps.astype(jnp.float32))
    cum = jnp.cumsum(steps * decay_rates[None, :], axis=0)
    ending = cum[-1]
    factor = jnp.exp(ending[None, :] - cum) * steps
    groups = head_count // GROUP

    def grouped(a):
        return a.reshape(local_rows, groups, GROUP).transpose(1, 0, 2)

    cum_grouped = grouped(cum)
    fac_grouped = grouped(factor)
    cum_t = cum.T
    step_t = steps.T
    decay_lanes = jnp.repeat(jnp.exp(ending), head_size).reshape(1, -1)
    skip_lanes = jnp.repeat(head_skip_weight, head_size).reshape(1, -1)
    scores = jnp.dot(readout, inputs.T, preferred_element_type=jnp.float32)
    bt = inputs.T
    place = place_index.astype(jnp.int32).reshape(1)

    sizes = CHUNK_GROUPS
    firsts = [sum(sizes[:c]) for c in range(len(sizes))]
    group_width = GROUP * head_size
    sends = [
        send_rows(tokens[:, f * group_width : (f + n) * group_width], pick_rows, stream_count, capacity)
        for f, n in zip(firsts, sizes)
    ]
    partials = []
    gathers = []
    result = None
    done = 0
    for c in range(len(sizes)):
        arrived = lax.all_to_all(sends[c], "stream", split_axis=0, concat_axis=0, tiled=True)
        tied = {"arrived": arrived}
        if c + 1 < len(sizes):
            tied["send"] = sends[c + 1]
        if c >= 1:
            tied["partial"] = partials[c - 1]
        if c >= 2:
            result = combine_call(
                result, place, partials[done], gathers[done], cum_grouped, readout,
                firsts[done], inner,
            )
            done += 1
            tied["result"] = result
        tied = lax.optimization_barrier(tied)
        arrived = tied["arrived"]
        if c + 1 < len(sizes):
            sends[c + 1] = tied["send"]
        if c >= 2:
            result = tied["result"]
        chunk_tokens = receive_rows(arrived, flat_rows)
        carried = carried_call(bt, fac_grouped, decay_lanes, chunk_tokens, firsts[c])
        gathers.append(lax.all_gather(carried, "pos"))
        partials.append(
            local_call(scores, cum_grouped, cum_t, step_t, chunk_tokens, skip_lanes, firsts[c])
        )
    while done < len(sizes):
        result = combine_call(
            result, place, partials[done], gathers[done], cum_grouped, readout, firsts[done], inner
        )
        done += 1
    return result[None]


def solution(mesh):
    in_specs = (
        P("stream", "pos", None),
        P("stream", "pos", None),
        P("stream", "pos", None),
        P(),
        P(),
        P(),
    )
    out_specs = P("stream", "pos", None)
    return jax.shard_map(
        on_device, mesh=mesh, in_specs=in_specs, out_specs=out_specs, check_vma=False
    )
```

```python
import jax
import jax.numpy as jnp
from jax import lax
from jax.experimental import pallas as pl
from jax.experimental.pallas import tpu as pltpu
from jax.sharding import PartitionSpec as P

GROUP = 8
TILE = 128
CHUNK_GROUPS = (4, 4, 4, 4)
EXTRA = 16


def lane_pick(low, high):
    lane_low = lax.broadcasted_iota(jnp.int32, (1, 128), 1) < 64
    return jnp.where(lane_low, low, high)


def carried_kernel(bt_ref, decay_ref, scaled_ref, out_ref):
    pairs = out_ref.shape[0]
    state_size = bt_ref.shape[0]
    for q in range(pairs):
        scaled = scaled_ref[:, 128 * q : 128 * (q + 1)]
        out_ref[q, 0:state_size, :] = jnp.dot(
            bt_ref[...], scaled, preferred_element_type=jnp.float32
        ).astype(out_ref.dtype)
        rows = lax.broadcasted_iota(jnp.int32, (EXTRA, 128), 0)
        decay = decay_ref[:, 128 * q : 128 * (q + 1)]
        high = decay.astype(out_ref.dtype)
        low = (decay - high.astype(jnp.float32)).astype(out_ref.dtype)
        extra = jnp.where(rows == 0, high, jnp.where(rows == 1, low, jnp.zeros_like(high)))
        out_ref[q, state_size : state_size + EXTRA, :] = extra


def local_kernel(scores_ref, cumg_ref, cumt_ref, stept_ref, tok_ref, skip_ref, out_ref):
    length = scores_ref.shape[0]
    heads = cumt_ref.shape[0]
    for q in range(heads // 2):
        x = tok_ref[:, 128 * q : 128 * (q + 1)]
        skip = skip_ref[:, 128 * q : 128 * (q + 1)]
        for i in range(length // TILE):
            r0 = i * TILE
            width = (i + 1) * TILE
            rows = lax.broadcasted_iota(jnp.int32, (TILE, width), 0) + r0
            cols = lax.broadcasted_iota(jnp.int32, (TILE, width), 1)
            causal = rows >= cols
            sc = scores_ref[r0 : r0 + TILE, 0:width]
            parts = []
            for j in range(2):
                h = 2 * q + j
                ct = cumg_ref[0, r0 : r0 + TILE, h : h + 1]
                cs = cumt_ref[h : h + 1, 0:width]
                st = stept_ref[h : h + 1, 0:width]
                w = jnp.where(causal, jnp.exp(ct - cs), 0.0)
                wb = ((sc * w) * st).astype(jnp.bfloat16)
                parts.append(jnp.dot(wb, x[0:width], preferred_element_type=jnp.float32))
            xt = x[r0 : r0 + TILE].astype(jnp.float32)
            total = lane_pick(parts[0], parts[1]) + skip * xt
            out_ref[r0 : r0 + TILE, 128 * q : 128 * (q + 1)] = total


def combine_kernel(place_ref, *refs):
    if len(refs) == 6:
        refs = refs[1:]
    part_ref, gath_ref, cumg_ref, c_ref, out_ref = refs
    here = place_ref[0]
    peers = gath_ref.shape[0]
    pairs = gath_ref.shape[1]
    state_size = c_ref.shape[1]
    for q in range(pairs):
        run = jnp.ones((1, 128), jnp.float32)
        state = jnp.zeros((state_size, 128), jnp.float32)
        for k in range(peers - 1, -1, -1):
            if k + 1 < peers:
                pair = gath_ref[k + 1, q, state_size : state_size + 2, :].astype(jnp.float32)
                later = pair[0:1] + pair[1:2]
                run = jnp.where(k + 1 < here, run * later, 1.0)
            weight = jnp.where(k < here, run, 0.0)
            state = state + weight * gath_ref[k, q, 0:state_size, :].astype(jnp.float32)
        readable = state.astype(jnp.bfloat16)
        inherited = jnp.dot(c_ref[...], readable, preferred_element_type=jnp.float32)
        decay = lane_pick(
            jnp.exp(cumg_ref[0, :, 2 * q : 2 * q + 1]), jnp.exp(cumg_ref[0, :, 2 * q + 1 : 2 * q + 2])
        )
        total = part_ref[:, 128 * q : 128 * (q + 1)] + decay * inherited
        out_ref[:, 128 * q : 128 * (q + 1)] = total.astype(out_ref.dtype)


def arbitrary():
    return pltpu.CompilerParams(dimension_semantics=("arbitrary",))


def carried_call(bt, decay_lanes, scaled, first):
    length, width = scaled.shape
    groups = width // (GROUP * 64)
    state_size = bt.shape[0]
    return pl.pallas_call(
        carried_kernel,
        grid=(groups,),
        in_specs=[
            pl.BlockSpec(bt.shape, lambda g: (0, 0)),
            pl.BlockSpec((1, GROUP * 64), lambda g: (0, g + first)),
            pl.BlockSpec((length, GROUP * 64), lambda g: (0, g)),
        ],
        out_specs=pl.BlockSpec((GROUP // 2, state_size + EXTRA, 128), lambda g: (g, 0, 0)),
        out_shape=jax.ShapeDtypeStruct((width // 128, state_size + EXTRA, 128), jnp.bfloat16),
        compiler_params=arbitrary(),
    )(bt, decay_lanes, scaled)


def local_call(scores, cum_grouped, cum_t, step_t, tokens, skip_lanes, first):
    length, width = tokens.shape
    groups = width // (GROUP * 64)
    return pl.pallas_call(
        local_kernel,
        grid=(groups,),
        in_specs=[
            pl.BlockSpec((length, length), lambda g: (0, 0)),
            pl.BlockSpec((1, length, GROUP), lambda g: (g + first, 0, 0)),
            pl.BlockSpec((GROUP, length), lambda g: (g + first, 0)),
            pl.BlockSpec((GROUP, length), lambda g: (g + first, 0)),
            pl.BlockSpec((length, GROUP * 64), lambda g: (0, g)),
            pl.BlockSpec((1, GROUP * 64), lambda g: (0, g + first)),
        ],
        out_specs=pl.BlockSpec((length, GROUP * 64), lambda g: (0, g)),
        out_shape=jax.ShapeDtypeStruct((length, width), jnp.float32),
        compiler_params=arbitrary(),
    )(scores, cum_grouped, cum_t, step_t, tokens, skip_lanes)


def combine_call(buffer, place, partial, gathered, cum_grouped, readout, first, total_width):
    length, width = partial.shape
    groups = width // (GROUP * 64)
    state_rows = gathered.shape[2]
    in_specs = [
        pl.BlockSpec((length, GROUP * 64), lambda g: (0, g)),
        pl.BlockSpec((gathered.shape[0], GROUP // 2, state_rows, 128), lambda g: (0, g, 0, 0)),
        pl.BlockSpec((1, length, GROUP), lambda g: (g + first, 0, 0)),
        pl.BlockSpec(readout.shape, lambda g: (0, 0)),
    ]
    operands = [partial, gathered, cum_grouped, readout]
    aliases = {}
    if buffer is not None:
        in_specs = [pl.BlockSpec(memory_space=pl.ANY)] + in_specs
        operands = [buffer] + operands
        aliases = {1: 0}
    return pl.pallas_call(
        combine_kernel,
        grid=(groups,),
        in_specs=[pl.BlockSpec(memory_space=pltpu.SMEM)] + in_specs,
        out_specs=pl.BlockSpec((length, GROUP * 64), lambda g: (0, g + first)),
        out_shape=jax.ShapeDtypeStruct((length, total_width), jnp.bfloat16),
        input_output_aliases=aliases,
        compiler_params=arbitrary(),
    )(place, *operands)


def send_rows(rows, pick_rows, stream_count, capacity):
    width = rows.shape[1]
    picked = jnp.take(rows, pick_rows, axis=0, mode="clip", indices_are_sorted=True)
    return picked.reshape(stream_count, capacity, width)


def receive_rows(arrived, flat_rows):
    width = arrived.shape[2]
    return jnp.take(
        arrived.reshape(-1, width), flat_rows, axis=0, mode="clip",
        unique_indices=True, indices_are_sorted=True,
    )


def deliver(rows, pick_rows, flat_rows, stream_count, capacity):
    send = send_rows(rows, pick_rows, stream_count, capacity)
    arrived = lax.all_to_all(send, "stream", split_axis=0, concat_axis=0, tiled=True)
    return receive_rows(arrived, flat_rows)


def on_device(tokens_in, proj_in, step_raw, decay_log, head_skip_weight, row_counts):
    stream_count = lax.axis_size("stream")
    stream_index = lax.axis_index("stream")
    place_index = lax.axis_index("pos")
    tokens = tokens_in[0]
    local_rows, inner = tokens.shape
    head_count = step_raw.shape[2]
    head_size = inner // head_count
    state_size = proj_in.shape[2] // 2
    capacity = 3 * local_rows // (2 * stream_count)

    place_counts = lax.dynamic_index_in_dim(row_counts, place_index, 0, keepdims=False)
    send_counts = lax.dynamic_index_in_dim(place_counts, stream_index, 0, keepdims=False)
    recv_counts = lax.dynamic_index_in_dim(place_counts, stream_index, 1, keepdims=False)
    send_start = jnp.cumsum(send_counts) - send_counts
    slot_range = jnp.arange(capacity, dtype=jnp.int32)
    pick_rows = jnp.clip(send_start[:, None] + slot_range[None, :], 0, local_rows - 1).reshape(-1)
    recv_end = jnp.cumsum(recv_counts)
    recv_start = recv_end - recv_counts
    positions = jnp.arange(local_rows, dtype=jnp.int32)
    source = jnp.sum((recv_end[:, None] <= positions[None, :]).astype(jnp.int32), axis=0)
    source = jnp.clip(source, 0, stream_count - 1)
    source_start = jnp.take(recv_start, source)
    flat_rows = source * capacity + positions - source_start

    small = jnp.concatenate([proj_in[0], step_raw[0]], axis=1)
    ordered_small = deliver(small, pick_rows, flat_rows, stream_count, capacity)
    ordered_proj = ordered_small[:, : 2 * state_size]
    ordered_steps = ordered_small[:, 2 * state_size :]

    inputs = ordered_proj[:, :state_size]
    readout = ordered_proj[:, state_size:]
    decay_rates = -jnp.exp(decay_log)
    steps = jax.nn.softplus(ordered_steps.astype(jnp.float32))
    cum = jnp.cumsum(steps * decay_rates[None, :], axis=0)
    ending = cum[-1]
    factor = jnp.exp(ending[None, :] - cum) * steps
    groups = head_count // GROUP

    def grouped(a):
        return a.reshape(local_rows, groups, GROUP).transpose(1, 0, 2)

    cum_grouped = grouped(cum)
    cum_t = cum.T
    step_t = steps.T
    decay_lanes = jnp.repeat(jnp.exp(ending), head_size).reshape(1, -1)
    skip_lanes = jnp.repeat(head_skip_weight, head_size).reshape(1, -1)
    scores = jnp.dot(readout, inputs.T, preferred_element_type=jnp.float32)
    bt = inputs.T
    place = place_index.astype(jnp.int32).reshape(1)

    sizes = CHUNK_GROUPS
    firsts = [sum(sizes[:c]) for c in range(len(sizes))]
    group_width = GROUP * head_size
    sends = [
        send_rows(tokens[:, f * group_width : (f + n) * group_width], pick_rows, stream_count, capacity)
        for f, n in zip(firsts, sizes)
    ]
    partials = []
    gathers = []
    result = None
    done = 0
    for c in range(len(sizes)):
        arrived = lax.all_to_all(sends[c], "stream", split_axis=0, concat_axis=0, tiled=True)
        tied = {"arrived": arrived}
        if c + 1 < len(sizes):
            tied["send"] = sends[c + 1]
        if c >= 1:
            tied["partial"] = partials[c - 1]
        if c >= 2:
            result = combine_call(
                result, place, partials[done], gathers[done], cum_grouped, readout,
                firsts[done], inner,
            )
            done += 1
            tied["result"] = result
        tied = lax.optimization_barrier(tied)
        arrived = tied["arrived"]
        if c + 1 < len(sizes):
            sends[c + 1] = tied["send"]
        if c >= 2:
            result = tied["result"]
        chunk_tokens = receive_rows(arrived, flat_rows)
        heads_here = sizes[c] * GROUP
        chunk_factor = factor[:, firsts[c] * GROUP : firsts[c] * GROUP + heads_here]
        scaled = (
            chunk_factor[:, :, None] * chunk_tokens.reshape(local_rows, heads_here, head_size)
        ).astype(jnp.bfloat16)
        scaled = scaled.reshape(local_rows, heads_here * head_size)
        carried = carried_call(bt, decay_lanes, scaled, firsts[c])
        gathers.append(lax.all_gather(carried, "pos"))
        partials.append(
            local_call(scores, cum_grouped, cum_t, step_t, chunk_tokens, skip_lanes, firsts[c])
        )
    while done < len(sizes):
        result = combine_call(
            result, place, partials[done], gathers[done], cum_grouped, readout, firsts[done], inner
        )
        done += 1
    return result[None]


def solution(mesh):
    in_specs = (
        P("stream", "pos", None),
        P("stream", "pos", None),
        P("stream", "pos", None),
        P(),
        P(),
        P(),
    )
    out_specs = P("stream", "pos", None)
    return jax.shard_map(
        on_device, mesh=mesh, in_specs=in_specs, out_specs=out_specs, check_vma=False
    )
```

```python
import jax
import jax.numpy as jnp
from jax import lax
from jax.experimental import pallas as pl
from jax.experimental.pallas import tpu as pltpu
from jax.sharding import PartitionSpec as P

GROUP = 8
TILE = 128
CHUNK_GROUPS = (4, 4, 4, 4)
EXTRA = 16


def lane_pick(low, high):
    lane_low = lax.broadcasted_iota(jnp.int32, (1, 128), 1) < 64
    return jnp.where(lane_low, low, high)


def carried_kernel(bt_ref, facg_ref, decay_ref, tok_ref, out_ref):
    pairs = out_ref.shape[0]
    state_size = bt_ref.shape[0]
    for q in range(pairs):
        x = tok_ref[:, 128 * q : 128 * (q + 1)].astype(jnp.float32)
        factor = lane_pick(facg_ref[0, :, 2 * q : 2 * q + 1], facg_ref[0, :, 2 * q + 1 : 2 * q + 2])
        scaled = (factor * x).astype(jnp.bfloat16)
        out_ref[q, 0:state_size, :] = jnp.dot(
            bt_ref[...], scaled, preferred_element_type=jnp.float32
        ).astype(out_ref.dtype)
        rows = lax.broadcasted_iota(jnp.int32, (EXTRA, 128), 0)
        decay = decay_ref[:, 128 * q : 128 * (q + 1)]
        high = decay.astype(out_ref.dtype)
        low = (decay - high.astype(jnp.float32)).astype(out_ref.dtype)
        extra = jnp.where(rows == 0, high, jnp.where(rows == 1, low, jnp.zeros_like(high)))
        out_ref[q, state_size : state_size + EXTRA, :] = extra


def local_kernel(scores_ref, cumg_ref, cumt_ref, stept_ref, tok_ref, skip_ref, out_ref):
    length = scores_ref.shape[0]
    heads = cumt_ref.shape[0]
    for q in range(heads // 2):
        x = tok_ref[:, 128 * q : 128 * (q + 1)]
        skip = skip_ref[:, 128 * q : 128 * (q + 1)]
        for i in range(length // TILE):
            r0 = i * TILE
            width = (i + 1) * TILE
            rows = lax.broadcasted_iota(jnp.int32, (TILE, width), 0) + r0
            cols = lax.broadcasted_iota(jnp.int32, (TILE, width), 1)
            causal = rows >= cols
            sc = scores_ref[r0 : r0 + TILE, 0:width]
            parts = []
            for j in range(2):
                h = 2 * q + j
                ct = cumg_ref[0, r0 : r0 + TILE, h : h + 1]
                cs = cumt_ref[h : h + 1, 0:width]
                st = stept_ref[h : h + 1, 0:width]
                w = jnp.where(causal, jnp.exp(ct - cs), 0.0)
                wb = ((sc * w) * st).astype(jnp.bfloat16)
                parts.append(jnp.dot(wb, x[0:width], preferred_element_type=jnp.float32))
            xt = x[r0 : r0 + TILE].astype(jnp.float32)
            total = lane_pick(parts[0], parts[1]) + skip * xt
            out_ref[r0 : r0 + TILE, 128 * q : 128 * (q + 1)] = total


def combine_kernel(place_ref, *refs):
    if len(refs) == 6:
        refs = refs[1:]
    part_ref, gath_ref, cumg_ref, c_ref, out_ref = refs
    here = place_ref[0]
    peers = gath_ref.shape[0]
    pairs = gath_ref.shape[1]
    state_size = c_ref.shape[1]
    for q in range(pairs):
        run = jnp.ones((1, 128), jnp.float32)
        state = jnp.zeros((state_size, 128), jnp.float32)
        for k in range(peers - 1, -1, -1):
            if k + 1 < peers:
                pair = gath_ref[k + 1, q, state_size : state_size + 2, :].astype(jnp.float32)
                later = pair[0:1] + pair[1:2]
                run = jnp.where(k + 1 < here, run * later, 1.0)
            weight = jnp.where(k < here, run, 0.0)
            state = state + weight * gath_ref[k, q, 0:state_size, :].astype(jnp.float32)
        readable = state.astype(jnp.bfloat16)
        inherited = jnp.dot(c_ref[...], readable, preferred_element_type=jnp.float32)
        decay = lane_pick(
            jnp.exp(cumg_ref[0, :, 2 * q : 2 * q + 1]), jnp.exp(cumg_ref[0, :, 2 * q + 1 : 2 * q + 2])
        )
        total = part_ref[:, 128 * q : 128 * (q + 1)] + decay * inherited
        out_ref[:, 128 * q : 128 * (q + 1)] = total.astype(out_ref.dtype)


def arbitrary():
    return pltpu.CompilerParams(dimension_semantics=("arbitrary",))


def carried_call(bt, fac_grouped, decay_lanes, tokens, first):
    length, width = tokens.shape
    groups = width // (GROUP * 64)
    state_size = bt.shape[0]
    return pl.pallas_call(
        carried_kernel,
        grid=(groups,),
        in_specs=[
            pl.BlockSpec(bt.shape, lambda g: (0, 0)),
            pl.BlockSpec((1, length, GROUP), lambda g: (g + first, 0, 0)),
            pl.BlockSpec((1, GROUP * 64), lambda g: (0, g + first)),
            pl.BlockSpec((length, GROUP * 64), lambda g: (0, g)),
        ],
        out_specs=pl.BlockSpec((GROUP // 2, state_size + EXTRA, 128), lambda g: (g, 0, 0)),
        out_shape=jax.ShapeDtypeStruct((width // 128, state_size + EXTRA, 128), jnp.bfloat16),
        compiler_params=arbitrary(),
    )(bt, fac_grouped, decay_lanes, tokens)


def local_call(scores, cum_grouped, cum_t, step_t, tokens, skip_lanes, first):
    length, width = tokens.shape
    groups = width // (GROUP * 64)
    return pl.pallas_call(
        local_kernel,
        grid=(groups,),
        in_specs=[
            pl.BlockSpec((length, length), lambda g: (0, 0)),
            pl.BlockSpec((1, length, GROUP), lambda g: (g + first, 0, 0)),
            pl.BlockSpec((GROUP, length), lambda g: (g + first, 0)),
            pl.BlockSpec((GROUP, length), lambda g: (g + first, 0)),
            pl.BlockSpec((length, GROUP * 64), lambda g: (0, g)),
            pl.BlockSpec((1, GROUP * 64), lambda g: (0, g + first)),
        ],
        out_specs=pl.BlockSpec((length, GROUP * 64), lambda g: (0, g)),
        out_shape=jax.ShapeDtypeStruct((length, width), jnp.float32),
        compiler_params=arbitrary(),
    )(scores, cum_grouped, cum_t, step_t, tokens, skip_lanes)


def combine_call(buffer, place, partial, gathered, cum_grouped, readout, first, total_width):
    length, width = partial.shape
    groups = width // (GROUP * 64)
    state_rows = gathered.shape[2]
    in_specs = [
        pl.BlockSpec((length, GROUP * 64), lambda g: (0, g)),
        pl.BlockSpec((gathered.shape[0], GROUP // 2, state_rows, 128), lambda g: (0, g, 0, 0)),
        pl.BlockSpec((1, length, GROUP), lambda g: (g + first, 0, 0)),
        pl.BlockSpec(readout.shape, lambda g: (0, 0)),
    ]
    operands = [partial, gathered, cum_grouped, readout]
    aliases = {}
    if buffer is not None:
        in_specs = [pl.BlockSpec(memory_space=pl.ANY)] + in_specs
        operands = [buffer] + operands
        aliases = {1: 0}
    return pl.pallas_call(
        combine_kernel,
        grid=(groups,),
        in_specs=[pl.BlockSpec(memory_space=pltpu.SMEM)] + in_specs,
        out_specs=pl.BlockSpec((length, GROUP * 64), lambda g: (0, g + first)),
        out_shape=jax.ShapeDtypeStruct((length, total_width), jnp.bfloat16),
        input_output_aliases=aliases,
        compiler_params=arbitrary(),
    )(place, *operands)


def send_rows(rows, windows, stream_count, capacity):
    return jnp.stack(
        [lax.dynamic_slice_in_dim(rows, windows[d], capacity, 0) for d in range(stream_count)]
    )


def receive_rows(arrived, flat_rows):
    width = arrived.shape[2]
    return jnp.take(arrived.reshape(-1, width), flat_rows, axis=0, mode="clip")


def deliver(rows, windows, flat_rows, stream_count, capacity):
    send = send_rows(rows, windows, stream_count, capacity)
    arrived = lax.all_to_all(send, "stream", split_axis=0, concat_axis=0, tiled=True)
    return receive_rows(arrived, flat_rows)


def on_device(tokens_in, proj_in, step_raw, decay_log, head_skip_weight, row_counts):
    stream_count = lax.axis_size("stream")
    stream_index = lax.axis_index("stream")
    place_index = lax.axis_index("pos")
    tokens = tokens_in[0]
    local_rows, inner = tokens.shape
    head_count = step_raw.shape[2]
    head_size = inner // head_count
    state_size = proj_in.shape[2] // 2
    capacity = 3 * local_rows // (2 * stream_count)

    place_counts = lax.dynamic_index_in_dim(row_counts, place_index, 0, keepdims=False)
    send_counts = lax.dynamic_index_in_dim(place_counts, stream_index, 0, keepdims=False)
    recv_counts = lax.dynamic_index_in_dim(place_counts, stream_index, 1, keepdims=False)
    send_start = jnp.cumsum(send_counts) - send_counts
    windows = jnp.minimum(send_start, local_rows - capacity)
    recv_end = jnp.cumsum(recv_counts)
    recv_start = recv_end - recv_counts
    earlier_streams = jnp.arange(stream_count, dtype=jnp.int32) < stream_index
    their_start = jnp.sum(jnp.where(earlier_streams[None, :], place_counts, 0), axis=1)
    their_offset = their_start - jnp.minimum(their_start, local_rows - capacity)
    positions = jnp.arange(local_rows, dtype=jnp.int32)
    source = jnp.sum((recv_end[:, None] <= positions[None, :]).astype(jnp.int32), axis=0)
    source = jnp.clip(source, 0, stream_count - 1)
    source_start = jnp.take(recv_start - their_offset, source)
    flat_rows = source * capacity + positions - source_start

    small = jnp.concatenate([proj_in[0], step_raw[0]], axis=1)
    ordered_small = deliver(small, windows, flat_rows, stream_count, capacity)
    ordered_proj = ordered_small[:, : 2 * state_size]
    ordered_steps = ordered_small[:, 2 * state_size :]

    inputs = ordered_proj[:, :state_size]
    readout = ordered_proj[:, state_size:]
    decay_rates = -jnp.exp(decay_log)
    steps = jax.nn.softplus(ordered_steps.astype(jnp.float32))
    cum = jnp.cumsum(steps * decay_rates[None, :], axis=0)
    ending = cum[-1]
    factor = jnp.exp(ending[None, :] - cum) * steps
    groups = head_count // GROUP

    def grouped(a):
        return a.reshape(local_rows, groups, GROUP).transpose(1, 0, 2)

    cum_grouped = grouped(cum)
    fac_grouped = grouped(factor)
    cum_t = cum.T
    step_t = steps.T
    decay_lanes = jnp.repeat(jnp.exp(ending), head_size).reshape(1, -1)
    skip_lanes = jnp.repeat(head_skip_weight, head_size).reshape(1, -1)
    scores = jnp.dot(readout, inputs.T, preferred_element_type=jnp.float32)
    bt = inputs.T
    place = place_index.astype(jnp.int32).reshape(1)

    sizes = CHUNK_GROUPS
    firsts = [sum(sizes[:c]) for c in range(len(sizes))]
    group_width = GROUP * head_size
    sends = [
        send_rows(tokens[:, f * group_width : (f + n) * group_width], windows, stream_count, capacity)
        for f, n in zip(firsts, sizes)
    ]
    partials = []
    gathers = []
    result = None
    done = 0
    for c in range(len(sizes)):
        arrived = lax.all_to_all(sends[c], "stream", split_axis=0, concat_axis=0, tiled=True)
        tied = {"arrived": arrived}
        if c + 1 < len(sizes):
            tied["send"] = sends[c + 1]
        if c >= 1:
            tied["partial"] = partials[c - 1]
        if c >= 2:
            result = combine_call(
                result, place, partials[done], gathers[done], cum_grouped, readout,
                firsts[done], inner,
            )
            done += 1
            tied["result"] = result
        tied = lax.optimization_barrier(tied)
        arrived = tied["arrived"]
        if c + 1 < len(sizes):
            sends[c + 1] = tied["send"]
        if c >= 2:
            result = tied["result"]
        chunk_tokens = receive_rows(arrived, flat_rows)
        carried = carried_call(bt, fac_grouped, decay_lanes, chunk_tokens, firsts[c])
        gathers.append(lax.all_gather(carried, "pos"))
        partials.append(
            local_call(scores, cum_grouped, cum_t, step_t, chunk_tokens, skip_lanes, firsts[c])
        )
    while done < len(sizes):
        result = combine_call(
            result, place, partials[done], gathers[done], cum_grouped, readout, firsts[done], inner
        )
        done += 1
    return result[None]


def solution(mesh):
    in_specs = (
        P("stream", "pos", None),
        P("stream", "pos", None),
        P("stream", "pos", None),
        P(),
        P(),
        P(),
    )
    out_specs = P("stream", "pos", None)
    return jax.shard_map(
        on_device, mesh=mesh, in_specs=in_specs, out_specs=out_specs, check_vma=False
    )
```

```python
import jax
import jax.numpy as jnp
from jax import lax
from jax.experimental import pallas as pl
from jax.experimental.pallas import tpu as pltpu
from jax.sharding import PartitionSpec as P

GROUP = 8
TILE = 128
CHUNK_GROUPS = (4, 4, 4, 3, 1)
EXTRA = 16


def lane_pick(low, high):
    lane_low = lax.broadcasted_iota(jnp.int32, (1, 128), 1) < 64
    return jnp.where(lane_low, low, high)


def carried_kernel(bt_ref, facg_ref, decay_ref, tok_ref, out_ref):
    pairs = out_ref.shape[0]
    state_size = bt_ref.shape[0]
    for q in range(pairs):
        x = tok_ref[:, 128 * q : 128 * (q + 1)].astype(jnp.float32)
        factor = lane_pick(facg_ref[0, :, 2 * q : 2 * q + 1], facg_ref[0, :, 2 * q + 1 : 2 * q + 2])
        scaled = (factor * x).astype(jnp.bfloat16)
        out_ref[q, 0:state_size, :] = jnp.dot(
            bt_ref[...], scaled, preferred_element_type=jnp.float32
        ).astype(out_ref.dtype)
        rows = lax.broadcasted_iota(jnp.int32, (EXTRA, 128), 0)
        decay = decay_ref[:, 128 * q : 128 * (q + 1)]
        high = decay.astype(out_ref.dtype)
        low = (decay - high.astype(jnp.float32)).astype(out_ref.dtype)
        extra = jnp.where(rows == 0, high, jnp.where(rows == 1, low, jnp.zeros_like(high)))
        out_ref[q, state_size : state_size + EXTRA, :] = extra


def local_kernel(scores_ref, cumg_ref, cumt_ref, stept_ref, tok_ref, skip_ref, out_ref):
    length = scores_ref.shape[0]
    heads = cumt_ref.shape[0]
    for q in range(heads // 2):
        x = tok_ref[:, 128 * q : 128 * (q + 1)]
        skip = skip_ref[:, 128 * q : 128 * (q + 1)]
        for i in range(length // TILE):
            r0 = i * TILE
            width = (i + 1) * TILE
            rows = lax.broadcasted_iota(jnp.int32, (TILE, width), 0) + r0
            cols = lax.broadcasted_iota(jnp.int32, (TILE, width), 1)
            causal = rows >= cols
            sc = scores_ref[r0 : r0 + TILE, 0:width]
            parts = []
            for j in range(2):
                h = 2 * q + j
                ct = cumg_ref[0, r0 : r0 + TILE, h : h + 1]
                cs = cumt_ref[h : h + 1, 0:width]
                st = stept_ref[h : h + 1, 0:width]
                w = jnp.where(causal, jnp.exp(ct - cs), 0.0)
                wb = ((sc * w) * st).astype(jnp.bfloat16)
                parts.append(jnp.dot(wb, x[0:width], preferred_element_type=jnp.float32))
            xt = x[r0 : r0 + TILE].astype(jnp.float32)
            total = lane_pick(parts[0], parts[1]) + skip * xt
            out_ref[r0 : r0 + TILE, 128 * q : 128 * (q + 1)] = total


def combine_kernel(place_ref, *refs):
    if len(refs) == 6:
        refs = refs[1:]
    part_ref, gath_ref, cumg_ref, c_ref, out_ref = refs
    here = place_ref[0]
    peers = gath_ref.shape[0]
    pairs = gath_ref.shape[1]
    state_size = c_ref.shape[1]
    for q in range(pairs):
        run = jnp.ones((1, 128), jnp.float32)
        state = jnp.zeros((state_size, 128), jnp.float32)
        for k in range(peers - 1, -1, -1):
            if k + 1 < peers:
                pair = gath_ref[k + 1, q, state_size : state_size + 2, :].astype(jnp.float32)
                later = pair[0:1] + pair[1:2]
                run = jnp.where(k + 1 < here, run * later, 1.0)
            weight = jnp.where(k < here, run, 0.0)
            state = state + weight * gath_ref[k, q, 0:state_size, :].astype(jnp.float32)
        readable = state.astype(jnp.bfloat16)
        inherited = jnp.dot(c_ref[...], readable, preferred_element_type=jnp.float32)
        decay = lane_pick(
            jnp.exp(cumg_ref[0, :, 2 * q : 2 * q + 1]), jnp.exp(cumg_ref[0, :, 2 * q + 1 : 2 * q + 2])
        )
        total = part_ref[:, 128 * q : 128 * (q + 1)] + decay * inherited
        out_ref[:, 128 * q : 128 * (q + 1)] = total.astype(out_ref.dtype)


def arbitrary():
    return pltpu.CompilerParams(dimension_semantics=("arbitrary",))


def carried_call(bt, fac_grouped, decay_lanes, tokens, first):
    length, width = tokens.shape
    groups = width // (GROUP * 64)
    state_size = bt.shape[0]
    return pl.pallas_call(
        carried_kernel,
        grid=(groups,),
        in_specs=[
            pl.BlockSpec(bt.shape, lambda g: (0, 0)),
            pl.BlockSpec((1, length, GROUP), lambda g: (g + first, 0, 0)),
            pl.BlockSpec((1, GROUP * 64), lambda g: (0, g + first)),
            pl.BlockSpec((length, GROUP * 64), lambda g: (0, g)),
        ],
        out_specs=pl.BlockSpec((GROUP // 2, state_size + EXTRA, 128), lambda g: (g, 0, 0)),
        out_shape=jax.ShapeDtypeStruct((width // 128, state_size + EXTRA, 128), jnp.bfloat16),
        compiler_params=arbitrary(),
    )(bt, fac_grouped, decay_lanes, tokens)


def local_call(scores, cum_grouped, cum_t, step_t, tokens, skip_lanes, first):
    length, width = tokens.shape
    groups = width // (GROUP * 64)
    return pl.pallas_call(
        local_kernel,
        grid=(groups,),
        in_specs=[
            pl.BlockSpec((length, length), lambda g: (0, 0)),
            pl.BlockSpec((1, length, GROUP), lambda g: (g + first, 0, 0)),
            pl.BlockSpec((GROUP, length), lambda g: (g + first, 0)),
            pl.BlockSpec((GROUP, length), lambda g: (g + first, 0)),
            pl.BlockSpec((length, GROUP * 64), lambda g: (0, g)),
            pl.BlockSpec((1, GROUP * 64), lambda g: (0, g + first)),
        ],
        out_specs=pl.BlockSpec((length, GROUP * 64), lambda g: (0, g)),
        out_shape=jax.ShapeDtypeStruct((length, width), jnp.float32),
        compiler_params=arbitrary(),
    )(scores, cum_grouped, cum_t, step_t, tokens, skip_lanes)


def combine_call(buffer, place, partial, gathered, cum_grouped, readout, first, total_width):
    length, width = partial.shape
    groups = width // (GROUP * 64)
    state_rows = gathered.shape[2]
    in_specs = [
        pl.BlockSpec((length, GROUP * 64), lambda g: (0, g)),
        pl.BlockSpec((gathered.shape[0], GROUP // 2, state_rows, 128), lambda g: (0, g, 0, 0)),
        pl.BlockSpec((1, length, GROUP), lambda g: (g + first, 0, 0)),
        pl.BlockSpec(readout.shape, lambda g: (0, 0)),
    ]
    operands = [partial, gathered, cum_grouped, readout]
    aliases = {}
    if buffer is not None:
        in_specs = [pl.BlockSpec(memory_space=pl.ANY)] + in_specs
        operands = [buffer] + operands
        aliases = {1: 0}
    return pl.pallas_call(
        combine_kernel,
        grid=(groups,),
        in_specs=[pl.BlockSpec(memory_space=pltpu.SMEM)] + in_specs,
        out_specs=pl.BlockSpec((length, GROUP * 64), lambda g: (0, g + first)),
        out_shape=jax.ShapeDtypeStruct((length, total_width), jnp.bfloat16),
        input_output_aliases=aliases,
        compiler_params=arbitrary(),
    )(place, *operands)


def send_rows(rows, pick_rows, stream_count, capacity):
    width = rows.shape[1]
    return jnp.take(rows, pick_rows, axis=0, mode="clip").reshape(stream_count, capacity, width)


def receive_rows(arrived, flat_rows):
    width = arrived.shape[2]
    return jnp.take(arrived.reshape(-1, width), flat_rows, axis=0, mode="clip")


def deliver(rows, pick_rows, flat_rows, stream_count, capacity):
    send = send_rows(rows, pick_rows, stream_count, capacity)
    arrived = lax.all_to_all(send, "stream", split_axis=0, concat_axis=0, tiled=True)
    return receive_rows(arrived, flat_rows)


def on_device(tokens_in, proj_in, step_raw, decay_log, head_skip_weight, row_counts):
    stream_count = lax.axis_size("stream")
    stream_index = lax.axis_index("stream")
    place_index = lax.axis_index("pos")
    tokens = tokens_in[0]
    local_rows, inner = tokens.shape
    head_count = step_raw.shape[2]
    head_size = inner // head_count
    state_size = proj_in.shape[2] // 2
    capacity = 3 * local_rows // (2 * stream_count)

    place_counts = lax.dynamic_index_in_dim(row_counts, place_index, 0, keepdims=False)
    send_counts = lax.dynamic_index_in_dim(place_counts, stream_index, 0, keepdims=False)
    recv_counts = lax.dynamic_index_in_dim(place_counts, stream_index, 1, keepdims=False)
    send_start = jnp.cumsum(send_counts) - send_counts
    slot_range = jnp.arange(capacity, dtype=jnp.int32)
    pick_rows = jnp.clip(send_start[:, None] + slot_range[None, :], 0, local_rows - 1).reshape(-1)
    recv_end = jnp.cumsum(recv_counts)
    recv_start = recv_end - recv_counts
    positions = jnp.arange(local_rows, dtype=jnp.int32)
    source = jnp.sum((recv_end[:, None] <= positions[None, :]).astype(jnp.int32), axis=0)
    source = jnp.clip(source, 0, stream_count - 1)
    source_start = jnp.take(recv_start, source)
    flat_rows = source * capacity + positions - source_start

    small = jnp.concatenate([proj_in[0], step_raw[0]], axis=1)
    ordered_small = deliver(small, pick_rows, flat_rows, stream_count, capacity)
    ordered_proj = ordered_small[:, : 2 * state_size]
    ordered_steps = ordered_small[:, 2 * state_size :]

    inputs = ordered_proj[:, :state_size]
    readout = ordered_proj[:, state_size:]
    decay_rates = -jnp.exp(decay_log)
    steps = jax.nn.softplus(ordered_steps.astype(jnp.float32))
    cum = jnp.cumsum(steps * decay_rates[None, :], axis=0)
    ending = cum[-1]
    factor = jnp.exp(ending[None, :] - cum) * steps
    groups = head_count // GROUP

    def grouped(a):
        return a.reshape(local_rows, groups, GROUP).transpose(1, 0, 2)

    cum_grouped = grouped(cum)
    fac_grouped = grouped(factor)
    cum_t = cum.T
    step_t = steps.T
    decay_lanes = jnp.repeat(jnp.exp(ending), head_size).reshape(1, -1)
    skip_lanes = jnp.repeat(head_skip_weight, head_size).reshape(1, -1)
    scores = jnp.dot(readout, inputs.T, preferred_element_type=jnp.float32)
    bt = inputs.T
    place = place_index.astype(jnp.int32).reshape(1)

    sizes = CHUNK_GROUPS
    firsts = [sum(sizes[:c]) for c in range(len(sizes))]
    group_width = GROUP * head_size
    sends = [
        send_rows(tokens[:, f * group_width : (f + n) * group_width], pick_rows, stream_count, capacity)
        for f, n in zip(firsts, sizes)
    ]
    partials = []
    gathers = []
    result = None
    done = 0
    for c in range(len(sizes)):
        arrived = lax.all_to_all(sends[c], "stream", split_axis=0, concat_axis=0, tiled=True)
        tied = {"arrived": arrived}
        if c + 1 < len(sizes):
            tied["send"] = sends[c + 1]
        if c >= 1:
            tied["partial"] = partials[c - 1]
        if c >= 2:
            result = combine_call(
                result, place, partials[done], gathers[done], cum_grouped, readout,
                firsts[done], inner,
            )
            done += 1
            tied["result"] = result
        tied = lax.optimization_barrier(tied)
        arrived = tied["arrived"]
        if c + 1 < len(sizes):
            sends[c + 1] = tied["send"]
        if c >= 2:
            result = tied["result"]
        chunk_tokens = receive_rows(arrived, flat_rows)
        carried = carried_call(bt, fac_grouped, decay_lanes, chunk_tokens, firsts[c])
        gathers.append(lax.all_gather(carried, "pos"))
        partials.append(
            local_call(scores, cum_grouped, cum_t, step_t, chunk_tokens, skip_lanes, firsts[c])
        )
    while done < len(sizes):
        result = combine_call(
            result, place, partials[done], gathers[done], cum_grouped, readout, firsts[done], inner
        )
        done += 1
    return result[None]


def solution(mesh):
    in_specs = (
        P("stream", "pos", None),
        P("stream", "pos", None),
        P("stream", "pos", None),
        P(),
        P(),
        P(),
    )
    out_specs = P("stream", "pos", None)
    return jax.shard_map(
        on_device, mesh=mesh, in_specs=in_specs, out_specs=out_specs, check_vma=False
    )
```

```python
import jax
import jax.numpy as jnp
from jax import lax
from jax.experimental import pallas as pl
from jax.experimental.pallas import tpu as pltpu
from jax.sharding import PartitionSpec as P

GROUP = 8
TILE = 128
CHUNK_GROUPS = (4, 4, 4, 3, 1)
EXTRA = 16


def lane_pick(low, high):
    lane_low = lax.broadcasted_iota(jnp.int32, (1, 128), 1) < 64
    return jnp.where(lane_low, low, high)


def carried_kernel(bt_ref, facg_ref, decay_ref, tok_ref, out_ref):
    pairs = out_ref.shape[0]
    state_size = bt_ref.shape[0]
    for q in range(pairs):
        x = tok_ref[:, 128 * q : 128 * (q + 1)].astype(jnp.float32)
        factor = lane_pick(facg_ref[0, :, 2 * q : 2 * q + 1], facg_ref[0, :, 2 * q + 1 : 2 * q + 2])
        scaled = (factor * x).astype(jnp.bfloat16)
        out_ref[q, 0:state_size, :] = jnp.dot(
            bt_ref[...], scaled, preferred_element_type=jnp.float32
        ).astype(out_ref.dtype)
        rows = lax.broadcasted_iota(jnp.int32, (EXTRA, 128), 0)
        decay = decay_ref[:, 128 * q : 128 * (q + 1)]
        high = decay.astype(out_ref.dtype)
        low = (decay - high.astype(jnp.float32)).astype(out_ref.dtype)
        extra = jnp.where(rows == 0, high, jnp.where(rows == 1, low, jnp.zeros_like(high)))
        out_ref[q, state_size : state_size + EXTRA, :] = extra


def local_kernel(scores_ref, cumg_ref, cumt_ref, stept_ref, tok_ref, skip_ref, out_ref):
    length = scores_ref.shape[0]
    heads = cumt_ref.shape[0]
    for q in range(heads // 2):
        x = tok_ref[:, 128 * q : 128 * (q + 1)]
        skip = skip_ref[:, 128 * q : 128 * (q + 1)]
        for i in range(length // TILE):
            r0 = i * TILE
            width = (i + 1) * TILE
            rows = lax.broadcasted_iota(jnp.int32, (TILE, width), 0) + r0
            cols = lax.broadcasted_iota(jnp.int32, (TILE, width), 1)
            causal = rows >= cols
            sc = scores_ref[r0 : r0 + TILE, 0:width]
            parts = []
            for j in range(2):
                h = 2 * q + j
                ct = cumg_ref[0, r0 : r0 + TILE, h : h + 1]
                cs = cumt_ref[h : h + 1, 0:width]
                st = stept_ref[h : h + 1, 0:width]
                w = jnp.where(causal, jnp.exp(ct - cs), 0.0)
                wb = ((sc * w) * st).astype(jnp.bfloat16)
                parts.append(jnp.dot(wb, x[0:width], preferred_element_type=jnp.float32))
            xt = x[r0 : r0 + TILE].astype(jnp.float32)
            total = lane_pick(parts[0], parts[1]) + skip * xt
            out_ref[r0 : r0 + TILE, 128 * q : 128 * (q + 1)] = total


def combine_kernel(place_ref, *refs):
    if len(refs) == 6:
        refs = refs[1:]
    part_ref, gath_ref, cumg_ref, c_ref, out_ref = refs
    here = place_ref[0]
    peers = gath_ref.shape[0]
    pairs = gath_ref.shape[1]
    state_size = c_ref.shape[1]
    relative = peers < lax.axis_size("pos")
    for q in range(pairs):
        run = jnp.ones((1, 128), jnp.float32)
        state = jnp.zeros((state_size, 128), jnp.float32)
        if relative:
            for j in range(peers):
                if j > 0:
                    pair = gath_ref[j - 1, q, state_size : state_size + 2, :].astype(jnp.float32)
                    run = run * (pair[0:1] + pair[1:2])
                state = state + run * gath_ref[j, q, 0:state_size, :].astype(jnp.float32)
        for k in range(peers - 1, -1, -1) if not relative else ():
            if k + 1 < peers:
                pair = gath_ref[k + 1, q, state_size : state_size + 2, :].astype(jnp.float32)
                later = pair[0:1] + pair[1:2]
                run = jnp.where(k + 1 < here, run * later, 1.0)
            weight = jnp.where(k < here, run, 0.0)
            state = state + weight * gath_ref[k, q, 0:state_size, :].astype(jnp.float32)
        readable = state.astype(jnp.bfloat16)
        inherited = jnp.dot(c_ref[...], readable, preferred_element_type=jnp.float32)
        decay = lane_pick(
            jnp.exp(cumg_ref[0, :, 2 * q : 2 * q + 1]), jnp.exp(cumg_ref[0, :, 2 * q + 1 : 2 * q + 2])
        )
        total = part_ref[:, 128 * q : 128 * (q + 1)] + decay * inherited
        out_ref[:, 128 * q : 128 * (q + 1)] = total.astype(out_ref.dtype)


def arbitrary():
    return pltpu.CompilerParams(dimension_semantics=("arbitrary",))


def carried_call(bt, fac_grouped, decay_lanes, tokens, first):
    length, width = tokens.shape
    groups = width // (GROUP * 64)
    state_size = bt.shape[0]
    return pl.pallas_call(
        carried_kernel,
        grid=(groups,),
        in_specs=[
            pl.BlockSpec(bt.shape, lambda g: (0, 0)),
            pl.BlockSpec((1, length, GROUP), lambda g: (g + first, 0, 0)),
            pl.BlockSpec((1, GROUP * 64), lambda g: (0, g + first)),
            pl.BlockSpec((length, GROUP * 64), lambda g: (0, g)),
        ],
        out_specs=pl.BlockSpec((GROUP // 2, state_size + EXTRA, 128), lambda g: (g, 0, 0)),
        out_shape=jax.ShapeDtypeStruct((width // 128, state_size + EXTRA, 128), jnp.bfloat16),
        compiler_params=arbitrary(),
    )(bt, fac_grouped, decay_lanes, tokens)


def local_call(scores, cum_grouped, cum_t, step_t, tokens, skip_lanes, first):
    length, width = tokens.shape
    groups = width // (GROUP * 64)
    return pl.pallas_call(
        local_kernel,
        grid=(groups,),
        in_specs=[
            pl.BlockSpec((length, length), lambda g: (0, 0)),
            pl.BlockSpec((1, length, GROUP), lambda g: (g + first, 0, 0)),
            pl.BlockSpec((GROUP, length), lambda g: (g + first, 0)),
            pl.BlockSpec((GROUP, length), lambda g: (g + first, 0)),
            pl.BlockSpec((length, GROUP * 64), lambda g: (0, g)),
            pl.BlockSpec((1, GROUP * 64), lambda g: (0, g + first)),
        ],
        out_specs=pl.BlockSpec((length, GROUP * 64), lambda g: (0, g)),
        out_shape=jax.ShapeDtypeStruct((length, width), jnp.float32),
        compiler_params=arbitrary(),
    )(scores, cum_grouped, cum_t, step_t, tokens, skip_lanes)


def combine_call(buffer, place, partial, gathered, cum_grouped, readout, first, total_width):
    length, width = partial.shape
    groups = width // (GROUP * 64)
    state_rows = gathered.shape[2]
    in_specs = [
        pl.BlockSpec((length, GROUP * 64), lambda g: (0, g)),
        pl.BlockSpec((gathered.shape[0], GROUP // 2, state_rows, 128), lambda g: (0, g, 0, 0)),
        pl.BlockSpec((1, length, GROUP), lambda g: (g + first, 0, 0)),
        pl.BlockSpec(readout.shape, lambda g: (0, 0)),
    ]
    operands = [partial, gathered, cum_grouped, readout]
    aliases = {}
    if buffer is not None:
        in_specs = [pl.BlockSpec(memory_space=pl.ANY)] + in_specs
        operands = [buffer] + operands
        aliases = {1: 0}
    return pl.pallas_call(
        combine_kernel,
        grid=(groups,),
        in_specs=[pl.BlockSpec(memory_space=pltpu.SMEM)] + in_specs,
        out_specs=pl.BlockSpec((length, GROUP * 64), lambda g: (0, g + first)),
        out_shape=jax.ShapeDtypeStruct((length, total_width), jnp.bfloat16),
        input_output_aliases=aliases,
        compiler_params=arbitrary(),
    )(place, *operands)


def send_rows(rows, pick_rows, stream_count, capacity):
    width = rows.shape[1]
    return jnp.take(rows, pick_rows, axis=0, mode="clip").reshape(stream_count, capacity, width)


def receive_rows(arrived, flat_rows):
    width = arrived.shape[2]
    return jnp.take(arrived.reshape(-1, width), flat_rows, axis=0, mode="clip")


def deliver(rows, pick_rows, flat_rows, stream_count, capacity):
    send = send_rows(rows, pick_rows, stream_count, capacity)
    arrived = lax.all_to_all(send, "stream", split_axis=0, concat_axis=0, tiled=True)
    return receive_rows(arrived, flat_rows)


def earlier_blocks(carried):
    peers = lax.axis_size("pos")
    moved = [
        lax.ppermute(carried, "pos", [(i, i + shift) for i in range(peers - shift)])
        for shift in range(1, peers)
    ]
    return jnp.stack(moved)


def on_device(tokens_in, proj_in, step_raw, decay_log, head_skip_weight, row_counts):
    stream_count = lax.axis_size("stream")
    stream_index = lax.axis_index("stream")
    place_index = lax.axis_index("pos")
    tokens = tokens_in[0]
    local_rows, inner = tokens.shape
    head_count = step_raw.shape[2]
    head_size = inner // head_count
    state_size = proj_in.shape[2] // 2
    capacity = 3 * local_rows // (2 * stream_count)

    place_counts = lax.dynamic_index_in_dim(row_counts, place_index, 0, keepdims=False)
    send_counts = lax.dynamic_index_in_dim(place_counts, stream_index, 0, keepdims=False)
    recv_counts = lax.dynamic_index_in_dim(place_counts, stream_index, 1, keepdims=False)
    send_start = jnp.cumsum(send_counts) - send_counts
    slot_range = jnp.arange(capacity, dtype=jnp.int32)
    pick_rows = jnp.clip(send_start[:, None] + slot_range[None, :], 0, local_rows - 1).reshape(-1)
    recv_end = jnp.cumsum(recv_counts)
    recv_start = recv_end - recv_counts
    positions = jnp.arange(local_rows, dtype=jnp.int32)
    source = jnp.sum((recv_end[:, None] <= positions[None, :]).astype(jnp.int32), axis=0)
    source = jnp.clip(source, 0, stream_count - 1)
    source_start = jnp.take(recv_start, source)
    flat_rows = source * capacity + positions - source_start

    small = jnp.concatenate([proj_in[0], step_raw[0]], axis=1)
    ordered_small = deliver(small, pick_rows, flat_rows, stream_count, capacity)
    ordered_proj = ordered_small[:, : 2 * state_size]
    ordered_steps = ordered_small[:, 2 * state_size :]

    inputs = ordered_proj[:, :state_size]
    readout = ordered_proj[:, state_size:]
    decay_rates = -jnp.exp(decay_log)
    steps = jax.nn.softplus(ordered_steps.astype(jnp.float32))
    cum = jnp.cumsum(steps * decay_rates[None, :], axis=0)
    ending = cum[-1]
    factor = jnp.exp(ending[None, :] - cum) * steps
    groups = head_count // GROUP

    def grouped(a):
        return a.reshape(local_rows, groups, GROUP).transpose(1, 0, 2)

    cum_grouped = grouped(cum)
    fac_grouped = grouped(factor)
    cum_t = cum.T
    step_t = steps.T
    decay_lanes = jnp.repeat(jnp.exp(ending), head_size).reshape(1, -1)
    skip_lanes = jnp.repeat(head_skip_weight, head_size).reshape(1, -1)
    scores = jnp.dot(readout, inputs.T, preferred_element_type=jnp.float32)
    bt = inputs.T
    place = place_index.astype(jnp.int32).reshape(1)

    sizes = CHUNK_GROUPS
    firsts = [sum(sizes[:c]) for c in range(len(sizes))]
    group_width = GROUP * head_size
    sends = [
        send_rows(tokens[:, f * group_width : (f + n) * group_width], pick_rows, stream_count, capacity)
        for f, n in zip(firsts, sizes)
    ]
    partials = []
    gathers = []
    result = None
    done = 0
    for c in range(len(sizes)):
        arrived = lax.all_to_all(sends[c], "stream", split_axis=0, concat_axis=0, tiled=True)
        tied = {"arrived": arrived}
        if c + 1 < len(sizes):
            tied["send"] = sends[c + 1]
        if c >= 1:
            tied["partial"] = partials[c - 1]
        if c >= 2:
            result = combine_call(
                result, place, partials[done], gathers[done], cum_grouped, readout,
                firsts[done], inner,
            )
            done += 1
            tied["result"] = result
        tied = lax.optimization_barrier(tied)
        arrived = tied["arrived"]
        if c + 1 < len(sizes):
            sends[c + 1] = tied["send"]
        if c >= 2:
            result = tied["result"]
        chunk_tokens = receive_rows(arrived, flat_rows)
        carried = carried_call(bt, fac_grouped, decay_lanes, chunk_tokens, firsts[c])
        if c + 1 < len(sizes):
            gathers.append(lax.all_gather(carried, "pos"))
        else:
            gathers.append(earlier_blocks(carried))
        partials.append(
            local_call(scores, cum_grouped, cum_t, step_t, chunk_tokens, skip_lanes, firsts[c])
        )
    while done < len(sizes):
        result = combine_call(
            result, place, partials[done], gathers[done], cum_grouped, readout, firsts[done], inner
        )
        done += 1
    return result[None]


def solution(mesh):
    in_specs = (
        P("stream", "pos", None),
        P("stream", "pos", None),
        P("stream", "pos", None),
        P(),
        P(),
        P(),
    )
    out_specs = P("stream", "pos", None)
    return jax.shard_map(
        on_device, mesh=mesh, in_specs=in_specs, out_specs=out_specs, check_vma=False
    )
```

```python
import jax
import jax.numpy as jnp
from jax import lax
from jax.experimental import pallas as pl
from jax.experimental.pallas import tpu as pltpu
from jax.sharding import PartitionSpec as P

GROUP = 8
TILE = 128
CHUNK_GROUPS = (4, 4, 4, 3, 1)
EXTRA = 16


def lane_pick(low, high):
    lane_low = lax.broadcasted_iota(jnp.int32, (1, 128), 1) < 64
    return jnp.where(lane_low, low, high)


def carried_kernel(bt_ref, facg_ref, decay_ref, onehot_ref, arr_ref, out_ref, tok_ref):
    pairs = out_ref.shape[0]
    state_size = bt_ref.shape[0]
    ordered = jnp.dot(onehot_ref[...], arr_ref[...], preferred_element_type=jnp.float32)
    tok_ref[...] = ordered.astype(tok_ref.dtype)
    factors = facg_ref[0]
    heads = factors.shape[1]
    head_row = lax.broadcasted_iota(jnp.int32, (heads, 128), 0)
    lane_high = (lax.broadcasted_iota(jnp.int32, (heads, 128), 1) >= 64).astype(jnp.int32)
    for q in range(pairs):
        x = ordered[:, 128 * q : 128 * (q + 1)]
        spread = (head_row == 2 * q + lane_high).astype(jnp.float32)
        factor = jnp.dot(
            factors, spread, precision=lax.Precision.HIGHEST, preferred_element_type=jnp.float32
        )
        scaled = (factor * x).astype(jnp.bfloat16)
        out_ref[q, 0:state_size, :] = jnp.dot(
            bt_ref[...], scaled, preferred_element_type=jnp.float32
        ).astype(out_ref.dtype)
        rows = lax.broadcasted_iota(jnp.int32, (EXTRA, 128), 0)
        decay = decay_ref[:, 128 * q : 128 * (q + 1)]
        high = decay.astype(out_ref.dtype)
        low = (decay - high.astype(jnp.float32)).astype(out_ref.dtype)
        extra = jnp.where(rows == 0, high, jnp.where(rows == 1, low, jnp.zeros_like(high)))
        out_ref[q, state_size : state_size + EXTRA, :] = extra


def local_kernel(scores_ref, cumg_ref, cumt_ref, stept_ref, tok_ref, skip_ref, out_ref):
    length = scores_ref.shape[0]
    heads = cumt_ref.shape[0]
    for q in range(heads // 2):
        x = tok_ref[:, 128 * q : 128 * (q + 1)]
        skip = skip_ref[:, 128 * q : 128 * (q + 1)]
        for i in range(length // TILE):
            r0 = i * TILE
            width = (i + 1) * TILE
            rows = lax.broadcasted_iota(jnp.int32, (TILE, width), 0) + r0
            cols = lax.broadcasted_iota(jnp.int32, (TILE, width), 1)
            causal = rows >= cols
            sc = scores_ref[r0 : r0 + TILE, 0:width]
            parts = []
            for j in range(2):
                h = 2 * q + j
                ct = cumg_ref[0, r0 : r0 + TILE, h : h + 1]
                cs = cumt_ref[h : h + 1, 0:width]
                st = stept_ref[h : h + 1, 0:width]
                w = jnp.where(causal, jnp.exp(ct - cs), 0.0)
                wb = ((sc * w) * st).astype(jnp.bfloat16)
                parts.append(jnp.dot(wb, x[0:width], preferred_element_type=jnp.float32))
            xt = x[r0 : r0 + TILE].astype(jnp.float32)
            total = lane_pick(parts[0], parts[1]) + skip * xt
            out_ref[r0 : r0 + TILE, 128 * q : 128 * (q + 1)] = total


def combine_kernel(place_ref, *refs):
    if len(refs) == 6:
        refs = refs[1:]
    part_ref, gath_ref, cumg_ref, c_ref, out_ref = refs
    here = place_ref[0]
    peers = gath_ref.shape[0]
    pairs = gath_ref.shape[1]
    state_size = c_ref.shape[1]
    for q in range(pairs):
        run = jnp.ones((1, 128), jnp.float32)
        state = jnp.zeros((state_size, 128), jnp.float32)
        for k in range(peers - 1, -1, -1):
            if k + 1 < peers:
                pair = gath_ref[k + 1, q, state_size : state_size + 2, :].astype(jnp.float32)
                later = pair[0:1] + pair[1:2]
                run = jnp.where(k + 1 < here, run * later, 1.0)
            weight = jnp.where(k < here, run, 0.0)
            state = state + weight * gath_ref[k, q, 0:state_size, :].astype(jnp.float32)
        readable = state.astype(jnp.bfloat16)
        inherited = jnp.dot(c_ref[...], readable, preferred_element_type=jnp.float32)
        decay = lane_pick(
            jnp.exp(cumg_ref[0, :, 2 * q : 2 * q + 1]), jnp.exp(cumg_ref[0, :, 2 * q + 1 : 2 * q + 2])
        )
        total = part_ref[:, 128 * q : 128 * (q + 1)] + decay * inherited
        out_ref[:, 128 * q : 128 * (q + 1)] = total.astype(out_ref.dtype)


def arbitrary():
    return pltpu.CompilerParams(dimension_semantics=("arbitrary",))


def carried_call(bt, fac_grouped, decay_lanes, onehot, arrived, first):
    rows, width = arrived.shape
    length = onehot.shape[0]
    groups = width // (GROUP * 64)
    state_size = bt.shape[0]
    return pl.pallas_call(
        carried_kernel,
        grid=(groups,),
        in_specs=[
            pl.BlockSpec(bt.shape, lambda g: (0, 0)),
            pl.BlockSpec((1, length, GROUP), lambda g: (g + first, 0, 0)),
            pl.BlockSpec((1, GROUP * 64), lambda g: (0, g + first)),
            pl.BlockSpec(onehot.shape, lambda g: (0, 0)),
            pl.BlockSpec((rows, GROUP * 64), lambda g: (0, g)),
        ],
        out_specs=[
            pl.BlockSpec((GROUP // 2, state_size + EXTRA, 128), lambda g: (g, 0, 0)),
            pl.BlockSpec((length, GROUP * 64), lambda g: (0, g)),
        ],
        out_shape=[
            jax.ShapeDtypeStruct((width // 128, state_size + EXTRA, 128), jnp.bfloat16),
            jax.ShapeDtypeStruct((length, width), jnp.bfloat16),
        ],
        compiler_params=arbitrary(),
    )(bt, fac_grouped, decay_lanes, onehot, arrived)


def local_call(scores, cum_grouped, cum_t, step_t, tokens, skip_lanes, first):
    length, width = tokens.shape
    groups = width // (GROUP * 64)
    return pl.pallas_call(
        local_kernel,
        grid=(groups,),
        in_specs=[
            pl.BlockSpec((length, length), lambda g: (0, 0)),
            pl.BlockSpec((1, length, GROUP), lambda g: (g + first, 0, 0)),
            pl.BlockSpec((GROUP, length), lambda g: (g + first, 0)),
            pl.BlockSpec((GROUP, length), lambda g: (g + first, 0)),
            pl.BlockSpec((length, GROUP * 64), lambda g: (0, g)),
            pl.BlockSpec((1, GROUP * 64), lambda g: (0, g + first)),
        ],
        out_specs=pl.BlockSpec((length, GROUP * 64), lambda g: (0, g)),
        out_shape=jax.ShapeDtypeStruct((length, width), jnp.float32),
        compiler_params=arbitrary(),
    )(scores, cum_grouped, cum_t, step_t, tokens, skip_lanes)


def combine_call(buffer, place, partial, gathered, cum_grouped, readout, first, total_width):
    length, width = partial.shape
    groups = width // (GROUP * 64)
    state_rows = gathered.shape[2]
    in_specs = [
        pl.BlockSpec((length, GROUP * 64), lambda g: (0, g)),
        pl.BlockSpec((gathered.shape[0], GROUP // 2, state_rows, 128), lambda g: (0, g, 0, 0)),
        pl.BlockSpec((1, length, GROUP), lambda g: (g + first, 0, 0)),
        pl.BlockSpec(readout.shape, lambda g: (0, 0)),
    ]
    operands = [partial, gathered, cum_grouped, readout]
    aliases = {}
    if buffer is not None:
        in_specs = [pl.BlockSpec(memory_space=pl.ANY)] + in_specs
        operands = [buffer] + operands
        aliases = {1: 0}
    return pl.pallas_call(
        combine_kernel,
        grid=(groups,),
        in_specs=[pl.BlockSpec(memory_space=pltpu.SMEM)] + in_specs,
        out_specs=pl.BlockSpec((length, GROUP * 64), lambda g: (0, g + first)),
        out_shape=jax.ShapeDtypeStruct((length, total_width), jnp.bfloat16),
        input_output_aliases=aliases,
        compiler_params=arbitrary(),
    )(place, *operands)


def send_rows(rows, pick_rows, stream_count, capacity):
    width = rows.shape[1]
    return jnp.take(rows, pick_rows, axis=0, mode="clip").reshape(stream_count, capacity, width)


def receive_rows(arrived, flat_rows):
    width = arrived.shape[2]
    return jnp.take(arrived.reshape(-1, width), flat_rows, axis=0, mode="clip")


def deliver(rows, pick_rows, flat_rows, stream_count, capacity):
    send = send_rows(rows, pick_rows, stream_count, capacity)
    arrived = lax.all_to_all(send, "stream", split_axis=0, concat_axis=0, tiled=True)
    return receive_rows(arrived, flat_rows)


def on_device(tokens_in, proj_in, step_raw, decay_log, head_skip_weight, row_counts):
    stream_count = lax.axis_size("stream")
    stream_index = lax.axis_index("stream")
    place_index = lax.axis_index("pos")
    tokens = tokens_in[0]
    local_rows, inner = tokens.shape
    head_count = step_raw.shape[2]
    head_size = inner // head_count
    state_size = proj_in.shape[2] // 2
    capacity = 3 * local_rows // (2 * stream_count)

    place_counts = lax.dynamic_index_in_dim(row_counts, place_index, 0, keepdims=False)
    send_counts = lax.dynamic_index_in_dim(place_counts, stream_index, 0, keepdims=False)
    recv_counts = lax.dynamic_index_in_dim(place_counts, stream_index, 1, keepdims=False)
    send_start = jnp.cumsum(send_counts) - send_counts
    slot_range = jnp.arange(capacity, dtype=jnp.int32)
    pick_rows = jnp.clip(send_start[:, None] + slot_range[None, :], 0, local_rows - 1).reshape(-1)
    recv_end = jnp.cumsum(recv_counts)
    recv_start = recv_end - recv_counts
    positions = jnp.arange(local_rows, dtype=jnp.int32)
    source = jnp.sum((recv_end[:, None] <= positions[None, :]).astype(jnp.int32), axis=0)
    source = jnp.clip(source, 0, stream_count - 1)
    source_start = jnp.take(recv_start, source)
    flat_rows = source * capacity + positions - source_start

    small = jnp.concatenate([proj_in[0], step_raw[0]], axis=1)
    ordered_small = deliver(small, pick_rows, flat_rows, stream_count, capacity)
    ordered_proj = ordered_small[:, : 2 * state_size]
    ordered_steps = ordered_small[:, 2 * state_size :]

    inputs = ordered_proj[:, :state_size]
    readout = ordered_proj[:, state_size:]
    decay_rates = -jnp.exp(decay_log)
    steps = jax.nn.softplus(ordered_steps.astype(jnp.float32))
    cum = jnp.cumsum(steps * decay_rates[None, :], axis=0)
    ending = cum[-1]
    factor = jnp.exp(ending[None, :] - cum) * steps
    groups = head_count // GROUP

    def grouped(a):
        return a.reshape(local_rows, groups, GROUP).transpose(1, 0, 2)

    cum_grouped = grouped(cum)
    fac_grouped = grouped(factor)
    cum_t = cum.T
    step_t = steps.T
    decay_lanes = jnp.repeat(jnp.exp(ending), head_size).reshape(1, -1)
    skip_lanes = jnp.repeat(head_skip_weight, head_size).reshape(1, -1)
    scores = jnp.dot(readout, inputs.T, preferred_element_type=jnp.float32)
    bt = inputs.T
    place = place_index.astype(jnp.int32).reshape(1)
    slots = jnp.arange(stream_count * capacity, dtype=jnp.int32)
    onehot = (flat_rows[:, None] == slots[None, :]).astype(jnp.bfloat16)

    sizes = CHUNK_GROUPS
    firsts = [sum(sizes[:c]) for c in range(len(sizes))]
    group_width = GROUP * head_size
    sends = [
        send_rows(tokens[:, f * group_width : (f + n) * group_width], pick_rows, stream_count, capacity)
        for f, n in zip(firsts, sizes)
    ]
    partials = []
    gathers = []
    result = None
    done = 0
    for c in range(len(sizes)):
        arrived = lax.all_to_all(sends[c], "stream", split_axis=0, concat_axis=0, tiled=True)
        tied = {"arrived": arrived}
        if c + 1 < len(sizes):
            tied["send"] = sends[c + 1]
        if c >= 1:
            tied["partial"] = partials[c - 1]
        if c >= 2:
            result = combine_call(
                result, place, partials[done], gathers[done], cum_grouped, readout,
                firsts[done], inner,
            )
            done += 1
            tied["result"] = result
        tied = lax.optimization_barrier(tied)
        arrived = tied["arrived"]
        if c + 1 < len(sizes):
            sends[c + 1] = tied["send"]
        if c >= 2:
            result = tied["result"]
        carried, chunk_tokens = carried_call(
            bt, fac_grouped, decay_lanes, onehot, arrived.reshape(-1, arrived.shape[2]), firsts[c]
        )
        gathers.append(lax.all_gather(carried, "pos"))
        partials.append(
            local_call(scores, cum_grouped, cum_t, step_t, chunk_tokens, skip_lanes, firsts[c])
        )
    while done < len(sizes):
        result = combine_call(
            result, place, partials[done], gathers[done], cum_grouped, readout, firsts[done], inner
        )
        done += 1
    return result[None]


def solution(mesh):
    in_specs = (
        P("stream", "pos", None),
        P("stream", "pos", None),
        P("stream", "pos", None),
        P(),
        P(),
        P(),
    )
    out_specs = P("stream", "pos", None)
    return jax.shard_map(
        on_device, mesh=mesh, in_specs=in_specs, out_specs=out_specs, check_vma=False
    )
```

```python
import jax
import jax.numpy as jnp
from jax import lax
from jax.experimental import pallas as pl
from jax.experimental.pallas import tpu as pltpu
from jax.sharding import PartitionSpec as P

GROUP = 8
TILE = 128
CHUNK_GROUPS = (4, 4, 4, 3, 1)
EXTRA = 16


def lane_pick(low, high):
    lane_low = lax.broadcasted_iota(jnp.int32, (1, 128), 1) < 64
    return jnp.where(lane_low, low, high)


def carried_kernel(bt_ref, facg_ref, decay_ref, onehot_ref, arr_ref, out_ref, tok_ref):
    pairs = out_ref.shape[0]
    state_size = bt_ref.shape[0]
    ordered = jnp.dot(onehot_ref[...], arr_ref[...], preferred_element_type=jnp.float32)
    tok_ref[...] = ordered.astype(tok_ref.dtype)
    for q in range(pairs):
        x = ordered[:, 128 * q : 128 * (q + 1)]
        factor = lane_pick(facg_ref[0, :, 2 * q : 2 * q + 1], facg_ref[0, :, 2 * q + 1 : 2 * q + 2])
        scaled = (factor * x).astype(jnp.bfloat16)
        out_ref[q, 0:state_size, :] = jnp.dot(
            bt_ref[...], scaled, preferred_element_type=jnp.float32
        ).astype(out_ref.dtype)
        rows = lax.broadcasted_iota(jnp.int32, (EXTRA, 128), 0)
        decay = decay_ref[:, 128 * q : 128 * (q + 1)]
        high = decay.astype(out_ref.dtype)
        low = (decay - high.astype(jnp.float32)).astype(out_ref.dtype)
        extra = jnp.where(rows == 0, high, jnp.where(rows == 1, low, jnp.zeros_like(high)))
        out_ref[q, state_size : state_size + EXTRA, :] = extra


def local_kernel(scores_ref, cumg_ref, cumt_ref, stept_ref, tok_ref, skip_ref, out_ref):
    length = scores_ref.shape[0]
    heads = cumt_ref.shape[0]
    for q in range(heads // 2):
        x = tok_ref[:, 128 * q : 128 * (q + 1)]
        skip = skip_ref[:, 128 * q : 128 * (q + 1)]
        for i in range(length // TILE):
            r0 = i * TILE
            width = (i + 1) * TILE
            rows = lax.broadcasted_iota(jnp.int32, (TILE, width), 0) + r0
            cols = lax.broadcasted_iota(jnp.int32, (TILE, width), 1)
            causal = rows >= cols
            sc = scores_ref[r0 : r0 + TILE, 0:width]
            parts = []
            for j in range(2):
                h = 2 * q + j
                ct = cumg_ref[0, r0 : r0 + TILE, h : h + 1]
                cs = cumt_ref[h : h + 1, 0:width]
                st = stept_ref[h : h + 1, 0:width]
                w = jnp.where(causal, jnp.exp(ct - cs), 0.0)
                wb = ((sc * w) * st).astype(jnp.bfloat16)
                parts.append(jnp.dot(wb, x[0:width], preferred_element_type=jnp.float32))
            xt = x[r0 : r0 + TILE].astype(jnp.float32)
            total = lane_pick(parts[0], parts[1]) + skip * xt
            out_ref[r0 : r0 + TILE, 128 * q : 128 * (q + 1)] = total


def combine_kernel(place_ref, *refs):
    if len(refs) == 6:
        refs = refs[1:]
    part_ref, gath_ref, cumg_ref, c_ref, out_ref = refs
    here = place_ref[0]
    peers = gath_ref.shape[0]
    pairs = gath_ref.shape[1]
    state_size = c_ref.shape[1]
    for q in range(pairs):
        run = jnp.ones((1, 128), jnp.float32)
        state = jnp.zeros((state_size, 128), jnp.float32)
        for k in range(peers - 1, -1, -1):
            if k + 1 < peers:
                pair = gath_ref[k + 1, q, state_size : state_size + 2, :].astype(jnp.float32)
                later = pair[0:1] + pair[1:2]
                run = jnp.where(k + 1 < here, run * later, 1.0)
            weight = jnp.where(k < here, run, 0.0)
            state = state + weight * gath_ref[k, q, 0:state_size, :].astype(jnp.float32)
        readable = state.astype(jnp.bfloat16)
        inherited = jnp.dot(c_ref[...], readable, preferred_element_type=jnp.float32)
        decay = lane_pick(
            jnp.exp(cumg_ref[0, :, 2 * q : 2 * q + 1]), jnp.exp(cumg_ref[0, :, 2 * q + 1 : 2 * q + 2])
        )
        total = part_ref[:, 128 * q : 128 * (q + 1)] + decay * inherited
        out_ref[:, 128 * q : 128 * (q + 1)] = total.astype(out_ref.dtype)


def arbitrary():
    return pltpu.CompilerParams(dimension_semantics=("arbitrary",))


def carried_call(bt, fac_grouped, decay_lanes, onehot, arrived, first):
    rows, width = arrived.shape
    length = onehot.shape[0]
    groups = width // (GROUP * 64)
    state_size = bt.shape[0]
    return pl.pallas_call(
        carried_kernel,
        grid=(groups,),
        in_specs=[
            pl.BlockSpec(bt.shape, lambda g: (0, 0)),
            pl.BlockSpec((1, length, GROUP), lambda g: (g + first, 0, 0)),
            pl.BlockSpec((1, GROUP * 64), lambda g: (0, g + first)),
            pl.BlockSpec(onehot.shape, lambda g: (0, 0)),
            pl.BlockSpec((rows, GROUP * 64), lambda g: (0, g)),
        ],
        out_specs=[
            pl.BlockSpec((GROUP // 2, state_size + EXTRA, 128), lambda g: (g, 0, 0)),
            pl.BlockSpec((length, GROUP * 64), lambda g: (0, g)),
        ],
        out_shape=[
            jax.ShapeDtypeStruct((width // 128, state_size + EXTRA, 128), jnp.bfloat16),
            jax.ShapeDtypeStruct((length, width), jnp.bfloat16),
        ],
        compiler_params=arbitrary(),
    )(bt, fac_grouped, decay_lanes, onehot, arrived)


def local_call(scores, cum_grouped, cum_t, step_t, tokens, skip_lanes, first):
    length, width = tokens.shape
    groups = width // (GROUP * 64)
    return pl.pallas_call(
        local_kernel,
        grid=(groups,),
        in_specs=[
            pl.BlockSpec((length, length), lambda g: (0, 0)),
            pl.BlockSpec((1, length, GROUP), lambda g: (g + first, 0, 0)),
            pl.BlockSpec((GROUP, length), lambda g: (g + first, 0)),
            pl.BlockSpec((GROUP, length), lambda g: (g + first, 0)),
            pl.BlockSpec((length, GROUP * 64), lambda g: (0, g)),
            pl.BlockSpec((1, GROUP * 64), lambda g: (0, g + first)),
        ],
        out_specs=pl.BlockSpec((length, GROUP * 64), lambda g: (0, g)),
        out_shape=jax.ShapeDtypeStruct((length, width), jnp.float32),
        compiler_params=arbitrary(),
    )(scores, cum_grouped, cum_t, step_t, tokens, skip_lanes)


def combine_call(buffer, place, partial, gathered, cum_grouped, readout, first, total_width):
    length, width = partial.shape
    groups = width // (GROUP * 64)
    state_rows = gathered.shape[2]
    in_specs = [
        pl.BlockSpec((length, GROUP * 64), lambda g: (0, g)),
        pl.BlockSpec((gathered.shape[0], GROUP // 2, state_rows, 128), lambda g: (0, g, 0, 0)),
        pl.BlockSpec((1, length, GROUP), lambda g: (g + first, 0, 0)),
        pl.BlockSpec(readout.shape, lambda g: (0, 0)),
    ]
    operands = [partial, gathered, cum_grouped, readout]
    aliases = {}
    if buffer is not None:
        in_specs = [pl.BlockSpec(memory_space=pl.ANY)] + in_specs
        operands = [buffer] + operands
        aliases = {1: 0}
    return pl.pallas_call(
        combine_kernel,
        grid=(groups,),
        in_specs=[pl.BlockSpec(memory_space=pltpu.SMEM)] + in_specs,
        out_specs=pl.BlockSpec((length, GROUP * 64), lambda g: (0, g + first)),
        out_shape=jax.ShapeDtypeStruct((length, total_width), jnp.bfloat16),
        input_output_aliases=aliases,
        compiler_params=arbitrary(),
    )(place, *operands)


def send_rows(rows, pick_rows, stream_count, capacity):
    width = rows.shape[1]
    return jnp.take(rows, pick_rows, axis=0, mode="clip").reshape(stream_count, capacity, width)


def receive_rows(arrived, flat_rows):
    width = arrived.shape[2]
    return jnp.take(arrived.reshape(-1, width), flat_rows, axis=0, mode="clip")


def deliver(rows, pick_rows, flat_rows, stream_count, capacity):
    send = send_rows(rows, pick_rows, stream_count, capacity)
    arrived = lax.all_to_all(send, "stream", split_axis=0, concat_axis=0, tiled=True)
    return receive_rows(arrived, flat_rows)


def on_device(tokens_in, proj_in, step_raw, decay_log, head_skip_weight, row_counts):
    stream_count = lax.axis_size("stream")
    stream_index = lax.axis_index("stream")
    place_index = lax.axis_index("pos")
    tokens = tokens_in[0]
    local_rows, inner = tokens.shape
    head_count = step_raw.shape[2]
    head_size = inner // head_count
    state_size = proj_in.shape[2] // 2
    capacity = 3 * local_rows // (2 * stream_count)

    place_counts = lax.dynamic_index_in_dim(row_counts, place_index, 0, keepdims=False)
    send_counts = lax.dynamic_index_in_dim(place_counts, stream_index, 0, keepdims=False)
    recv_counts = lax.dynamic_index_in_dim(place_counts, stream_index, 1, keepdims=False)
    send_start = jnp.cumsum(send_counts) - send_counts
    slot_range = jnp.arange(capacity, dtype=jnp.int32)
    pick_rows = jnp.clip(send_start[:, None] + slot_range[None, :], 0, local_rows - 1).reshape(-1)
    recv_end = jnp.cumsum(recv_counts)
    recv_start = recv_end - recv_counts
    positions = jnp.arange(local_rows, dtype=jnp.int32)
    source = jnp.sum((recv_end[:, None] <= positions[None, :]).astype(jnp.int32), axis=0)
    source = jnp.clip(source, 0, stream_count - 1)
    source_start = jnp.take(recv_start, source)
    flat_rows = source * capacity + positions - source_start

    small = jnp.concatenate([proj_in[0], step_raw[0]], axis=1)
    ordered_small = deliver(small, pick_rows, flat_rows, stream_count, capacity)
    ordered_proj = ordered_small[:, : 2 * state_size]
    ordered_steps = ordered_small[:, 2 * state_size :]

    inputs = ordered_proj[:, :state_size]
    readout = ordered_proj[:, state_size:]
    decay_rates = -jnp.exp(decay_log)
    steps = jax.nn.softplus(ordered_steps.astype(jnp.float32))
    cum = jnp.cumsum(steps * decay_rates[None, :], axis=0)
    ending = cum[-1]
    factor = jnp.exp(ending[None, :] - cum) * steps
    groups = head_count // GROUP

    def grouped(a):
        return a.reshape(local_rows, groups, GROUP).transpose(1, 0, 2)

    cum_grouped = grouped(cum)
    fac_grouped = grouped(factor)
    cum_t = cum.T
    step_t = steps.T
    decay_lanes = jnp.repeat(jnp.exp(ending), head_size).reshape(1, -1)
    skip_lanes = jnp.repeat(head_skip_weight, head_size).reshape(1, -1)
    scores = jnp.dot(readout, inputs.T, preferred_element_type=jnp.float32)
    bt = inputs.T
    place = place_index.astype(jnp.int32).reshape(1)
    slots = jnp.arange(stream_count * capacity, dtype=jnp.int32)
    onehot = (flat_rows[:, None] == slots[None, :]).astype(jnp.bfloat16)

    sizes = CHUNK_GROUPS
    firsts = [sum(sizes[:c]) for c in range(len(sizes))]
    group_width = GROUP * head_size
    sends = [
        send_rows(tokens[:, f * group_width : (f + n) * group_width], pick_rows, stream_count, capacity)
        for f, n in zip(firsts, sizes)
    ]
    partials = []
    gathers = []
    result = None
    done = 0
    for c in range(len(sizes)):
        arrived = lax.all_to_all(sends[c], "stream", split_axis=0, concat_axis=0, tiled=True)
        tied = {"arrived": arrived}
        if c + 1 < len(sizes):
            tied["send"] = sends[c + 1]
        if c >= 1:
            tied["partial"] = partials[c - 1]
        if c >= 2:
            result = combine_call(
                result, place, partials[done], gathers[done], cum_grouped, readout,
                firsts[done], inner,
            )
            done += 1
            tied["result"] = result
        tied = lax.optimization_barrier(tied)
        arrived = tied["arrived"]
        if c + 1 < len(sizes):
            sends[c + 1] = tied["send"]
        if c >= 2:
            result = tied["result"]
        carried, chunk_tokens = carried_call(
            bt, fac_grouped, decay_lanes, onehot, arrived.reshape(-1, arrived.shape[2]), firsts[c]
        )
        gathers.append(lax.all_gather(carried, "pos"))
        partials.append(
            local_call(scores, cum_grouped, cum_t, step_t, chunk_tokens, skip_lanes, firsts[c])
        )
    while done < len(sizes):
        result = combine_call(
            result, place, partials[done], gathers[done], cum_grouped, readout, firsts[done], inner
        )
        done += 1
    return result[None]


def solution(mesh):
    in_specs = (
        P("stream", "pos", None),
        P("stream", "pos", None),
        P("stream", "pos", None),
        P(),
        P(),
        P(),
    )
    out_specs = P("stream", "pos", None)
    return jax.shard_map(
        on_device, mesh=mesh, in_specs=in_specs, out_specs=out_specs, check_vma=False
    )
```

```python
import jax
import jax.numpy as jnp
from jax import lax
from jax.experimental import pallas as pl
from jax.experimental.pallas import tpu as pltpu
from jax.sharding import PartitionSpec as P

GROUP = 8
TILE = 128
CHUNK_GROUPS = (4, 4, 4, 3, 1)
EXTRA = 16


def lane_pick(low, high):
    lane_low = lax.broadcasted_iota(jnp.int32, (1, 128), 1) < 64
    return jnp.where(lane_low, low, high)


def carried_kernel(bt_ref, facg_ref, decay_ref, onehot_ref, arr_ref, out_ref, tok_ref):
    pairs = out_ref.shape[0]
    state_size = bt_ref.shape[0]
    ordered = jnp.dot(onehot_ref[...], arr_ref[...], preferred_element_type=jnp.float32)
    tok_ref[...] = ordered.astype(tok_ref.dtype)
    for q in range(pairs):
        x = ordered[:, 128 * q : 128 * (q + 1)]
        factor = lane_pick(facg_ref[0, :, 2 * q : 2 * q + 1], facg_ref[0, :, 2 * q + 1 : 2 * q + 2])
        scaled = (factor * x).astype(jnp.bfloat16)
        out_ref[q, 0:state_size, :] = jnp.dot(
            bt_ref[...], scaled, preferred_element_type=jnp.float32
        ).astype(out_ref.dtype)
        rows = lax.broadcasted_iota(jnp.int32, (EXTRA, 128), 0)
        decay = decay_ref[:, 128 * q : 128 * (q + 1)]
        high = decay.astype(out_ref.dtype)
        low = (decay - high.astype(jnp.float32)).astype(out_ref.dtype)
        extra = jnp.where(rows == 0, high, jnp.where(rows == 1, low, jnp.zeros_like(high)))
        out_ref[q, state_size : state_size + EXTRA, :] = extra


def send_kernel(onehot_ref, tok_ref, out_ref):
    out_ref[...] = jnp.dot(
        onehot_ref[...], tok_ref[...], preferred_element_type=jnp.float32
    ).astype(out_ref.dtype)


def send_call(onehot, tokens, first, groups, stream_count):
    rows, length = onehot.shape
    width = GROUP * 64
    picked = pl.pallas_call(
        send_kernel,
        grid=(groups,),
        in_specs=[
            pl.BlockSpec(onehot.shape, lambda g: (0, 0)),
            pl.BlockSpec((length, width), lambda g: (0, g + first)),
        ],
        out_specs=pl.BlockSpec((rows, width), lambda g: (0, g)),
        out_shape=jax.ShapeDtypeStruct((rows, groups * width), tokens.dtype),
        compiler_params=arbitrary(),
    )(onehot, tokens)
    return picked.reshape(stream_count, rows // stream_count, groups * width)


def local_kernel(scores_ref, cumg_ref, cumt_ref, stept_ref, tok_ref, skip_ref, out_ref):
    length = scores_ref.shape[0]
    heads = cumt_ref.shape[0]
    for q in range(heads // 2):
        x = tok_ref[:, 128 * q : 128 * (q + 1)]
        skip = skip_ref[:, 128 * q : 128 * (q + 1)]
        for i in range(length // TILE):
            r0 = i * TILE
            width = (i + 1) * TILE
            rows = lax.broadcasted_iota(jnp.int32, (TILE, width), 0) + r0
            cols = lax.broadcasted_iota(jnp.int32, (TILE, width), 1)
            causal = rows >= cols
            sc = scores_ref[r0 : r0 + TILE, 0:width]
            parts = []
            for j in range(2):
                h = 2 * q + j
                ct = cumg_ref[0, r0 : r0 + TILE, h : h + 1]
                cs = cumt_ref[h : h + 1, 0:width]
                st = stept_ref[h : h + 1, 0:width]
                w = jnp.where(causal, jnp.exp(ct - cs), 0.0)
                wb = ((sc * w) * st).astype(jnp.bfloat16)
                parts.append(jnp.dot(wb, x[0:width], preferred_element_type=jnp.float32))
            xt = x[r0 : r0 + TILE].astype(jnp.float32)
            total = lane_pick(parts[0], parts[1]) + skip * xt
            out_ref[r0 : r0 + TILE, 128 * q : 128 * (q + 1)] = total


def combine_kernel(place_ref, *refs):
    if len(refs) == 6:
        refs = refs[1:]
    part_ref, gath_ref, cumg_ref, c_ref, out_ref = refs
    here = place_ref[0]
    peers = gath_ref.shape[0]
    pairs = gath_ref.shape[1]
    state_size = c_ref.shape[1]
    for q in range(pairs):
        run = jnp.ones((1, 128), jnp.float32)
        state = jnp.zeros((state_size, 128), jnp.float32)
        for k in range(peers - 1, -1, -1):
            if k + 1 < peers:
                pair = gath_ref[k + 1, q, state_size : state_size + 2, :].astype(jnp.float32)
                later = pair[0:1] + pair[1:2]
                run = jnp.where(k + 1 < here, run * later, 1.0)
            weight = jnp.where(k < here, run, 0.0)
            state = state + weight * gath_ref[k, q, 0:state_size, :].astype(jnp.float32)
        readable = state.astype(jnp.bfloat16)
        inherited = jnp.dot(c_ref[...], readable, preferred_element_type=jnp.float32)
        decay = lane_pick(
            jnp.exp(cumg_ref[0, :, 2 * q : 2 * q + 1]), jnp.exp(cumg_ref[0, :, 2 * q + 1 : 2 * q + 2])
        )
        total = part_ref[:, 128 * q : 128 * (q + 1)] + decay * inherited
        out_ref[:, 128 * q : 128 * (q + 1)] = total.astype(out_ref.dtype)


def arbitrary():
    return pltpu.CompilerParams(dimension_semantics=("arbitrary",))


def carried_call(bt, fac_grouped, decay_lanes, onehot, arrived, first):
    rows, width = arrived.shape
    length = onehot.shape[0]
    groups = width // (GROUP * 64)
    state_size = bt.shape[0]
    return pl.pallas_call(
        carried_kernel,
        grid=(groups,),
        in_specs=[
            pl.BlockSpec(bt.shape, lambda g: (0, 0)),
            pl.BlockSpec((1, length, GROUP), lambda g: (g + first, 0, 0)),
            pl.BlockSpec((1, GROUP * 64), lambda g: (0, g + first)),
            pl.BlockSpec(onehot.shape, lambda g: (0, 0)),
            pl.BlockSpec((rows, GROUP * 64), lambda g: (0, g)),
        ],
        out_specs=[
            pl.BlockSpec((GROUP // 2, state_size + EXTRA, 128), lambda g: (g, 0, 0)),
            pl.BlockSpec((length, GROUP * 64), lambda g: (0, g)),
        ],
        out_shape=[
            jax.ShapeDtypeStruct((width // 128, state_size + EXTRA, 128), jnp.bfloat16),
            jax.ShapeDtypeStruct((length, width), jnp.bfloat16),
        ],
        compiler_params=arbitrary(),
    )(bt, fac_grouped, decay_lanes, onehot, arrived)


def local_call(scores, cum_grouped, cum_t, step_t, tokens, skip_lanes, first):
    length, width = tokens.shape
    groups = width // (GROUP * 64)
    return pl.pallas_call(
        local_kernel,
        grid=(groups,),
        in_specs=[
            pl.BlockSpec((length, length), lambda g: (0, 0)),
            pl.BlockSpec((1, length, GROUP), lambda g: (g + first, 0, 0)),
            pl.BlockSpec((GROUP, length), lambda g: (g + first, 0)),
            pl.BlockSpec((GROUP, length), lambda g: (g + first, 0)),
            pl.BlockSpec((length, GROUP * 64), lambda g: (0, g)),
            pl.BlockSpec((1, GROUP * 64), lambda g: (0, g + first)),
        ],
        out_specs=pl.BlockSpec((length, GROUP * 64), lambda g: (0, g)),
        out_shape=jax.ShapeDtypeStruct((length, width), jnp.float32),
        compiler_params=arbitrary(),
    )(scores, cum_grouped, cum_t, step_t, tokens, skip_lanes)


def combine_call(buffer, place, partial, gathered, cum_grouped, readout, first, total_width):
    length, width = partial.shape
    groups = width // (GROUP * 64)
    state_rows = gathered.shape[2]
    in_specs = [
        pl.BlockSpec((length, GROUP * 64), lambda g: (0, g)),
        pl.BlockSpec((gathered.shape[0], GROUP // 2, state_rows, 128), lambda g: (0, g, 0, 0)),
        pl.BlockSpec((1, length, GROUP), lambda g: (g + first, 0, 0)),
        pl.BlockSpec(readout.shape, lambda g: (0, 0)),
    ]
    operands = [partial, gathered, cum_grouped, readout]
    aliases = {}
    if buffer is not None:
        in_specs = [pl.BlockSpec(memory_space=pl.ANY)] + in_specs
        operands = [buffer] + operands
        aliases = {1: 0}
    return pl.pallas_call(
        combine_kernel,
        grid=(groups,),
        in_specs=[pl.BlockSpec(memory_space=pltpu.SMEM)] + in_specs,
        out_specs=pl.BlockSpec((length, GROUP * 64), lambda g: (0, g + first)),
        out_shape=jax.ShapeDtypeStruct((length, total_width), jnp.bfloat16),
        input_output_aliases=aliases,
        compiler_params=arbitrary(),
    )(place, *operands)


def send_rows(rows, pick_rows, stream_count, capacity):
    width = rows.shape[1]
    return jnp.take(rows, pick_rows, axis=0, mode="clip").reshape(stream_count, capacity, width)


def receive_rows(arrived, flat_rows):
    width = arrived.shape[2]
    return jnp.take(arrived.reshape(-1, width), flat_rows, axis=0, mode="clip")


def deliver(rows, pick_rows, flat_rows, stream_count, capacity):
    send = send_rows(rows, pick_rows, stream_count, capacity)
    arrived = lax.all_to_all(send, "stream", split_axis=0, concat_axis=0, tiled=True)
    return receive_rows(arrived, flat_rows)


def on_device(tokens_in, proj_in, step_raw, decay_log, head_skip_weight, row_counts):
    stream_count = lax.axis_size("stream")
    stream_index = lax.axis_index("stream")
    place_index = lax.axis_index("pos")
    tokens = tokens_in[0]
    local_rows, inner = tokens.shape
    head_count = step_raw.shape[2]
    head_size = inner // head_count
    state_size = proj_in.shape[2] // 2
    capacity = 3 * local_rows // (2 * stream_count)

    place_counts = lax.dynamic_index_in_dim(row_counts, place_index, 0, keepdims=False)
    send_counts = lax.dynamic_index_in_dim(place_counts, stream_index, 0, keepdims=False)
    recv_counts = lax.dynamic_index_in_dim(place_counts, stream_index, 1, keepdims=False)
    send_start = jnp.cumsum(send_counts) - send_counts
    slot_range = jnp.arange(capacity, dtype=jnp.int32)
    pick_rows = jnp.clip(send_start[:, None] + slot_range[None, :], 0, local_rows - 1).reshape(-1)
    recv_end = jnp.cumsum(recv_counts)
    recv_start = recv_end - recv_counts
    positions = jnp.arange(local_rows, dtype=jnp.int32)
    source = jnp.sum((recv_end[:, None] <= positions[None, :]).astype(jnp.int32), axis=0)
    source = jnp.clip(source, 0, stream_count - 1)
    source_start = jnp.take(recv_start, source)
    flat_rows = source * capacity + positions - source_start

    small = jnp.concatenate([proj_in[0], step_raw[0]], axis=1)
    ordered_small = deliver(small, pick_rows, flat_rows, stream_count, capacity)
    ordered_proj = ordered_small[:, : 2 * state_size]
    ordered_steps = ordered_small[:, 2 * state_size :]

    inputs = ordered_proj[:, :state_size]
    readout = ordered_proj[:, state_size:]
    decay_rates = -jnp.exp(decay_log)
    steps = jax.nn.softplus(ordered_steps.astype(jnp.float32))
    cum = jnp.cumsum(steps * decay_rates[None, :], axis=0)
    ending = cum[-1]
    factor = jnp.exp(ending[None, :] - cum) * steps
    groups = head_count // GROUP

    def grouped(a):
        return a.reshape(local_rows, groups, GROUP).transpose(1, 0, 2)

    cum_grouped = grouped(cum)
    fac_grouped = grouped(factor)
    cum_t = cum.T
    step_t = steps.T
    decay_lanes = jnp.repeat(jnp.exp(ending), head_size).reshape(1, -1)
    skip_lanes = jnp.repeat(head_skip_weight, head_size).reshape(1, -1)
    scores = jnp.dot(readout, inputs.T, preferred_element_type=jnp.float32)
    bt = inputs.T
    place = place_index.astype(jnp.int32).reshape(1)
    slots = jnp.arange(stream_count * capacity, dtype=jnp.int32)
    onehot = (flat_rows[:, None] == slots[None, :]).astype(jnp.bfloat16)

    sizes = CHUNK_GROUPS
    firsts = [sum(sizes[:c]) for c in range(len(sizes))]
    group_width = GROUP * head_size
    send_onehot = (pick_rows[:, None] == positions[None, :]).astype(jnp.bfloat16)
    sends = [send_call(send_onehot, tokens, f, n, stream_count) for f, n in zip(firsts, sizes)]
    partials = []
    gathers = []
    result = None
    done = 0
    for c in range(len(sizes)):
        arrived = lax.all_to_all(sends[c], "stream", split_axis=0, concat_axis=0, tiled=True)
        tied = {"arrived": arrived}
        if c + 1 < len(sizes):
            tied["send"] = sends[c + 1]
        if c >= 1:
            tied["partial"] = partials[c - 1]
        if c >= 2:
            result = combine_call(
                result, place, partials[done], gathers[done], cum_grouped, readout,
                firsts[done], inner,
            )
            done += 1
            tied["result"] = result
        tied = lax.optimization_barrier(tied)
        arrived = tied["arrived"]
        if c + 1 < len(sizes):
            sends[c + 1] = tied["send"]
        if c >= 2:
            result = tied["result"]
        carried, chunk_tokens = carried_call(
            bt, fac_grouped, decay_lanes, onehot, arrived.reshape(-1, arrived.shape[2]), firsts[c]
        )
        gathers.append(lax.all_gather(carried, "pos"))
        partials.append(
            local_call(scores, cum_grouped, cum_t, step_t, chunk_tokens, skip_lanes, firsts[c])
        )
    while done < len(sizes):
        result = combine_call(
            result, place, partials[done], gathers[done], cum_grouped, readout, firsts[done], inner
        )
        done += 1
    return result[None]


def solution(mesh):
    in_specs = (
        P("stream", "pos", None),
        P("stream", "pos", None),
        P("stream", "pos", None),
        P(),
        P(),
        P(),
    )
    out_specs = P("stream", "pos", None)
    return jax.shard_map(
        on_device, mesh=mesh, in_specs=in_specs, out_specs=out_specs, check_vma=False
    )
```

```python
import jax
import jax.numpy as jnp
from jax import lax
from jax.experimental import pallas as pl
from jax.experimental.pallas import tpu as pltpu
from jax.sharding import PartitionSpec as P

GROUP = 8
TILE = 128
CHUNK_GROUPS = (4, 4, 4, 3, 1)
EXTRA = 16


def lane_pick(low, high):
    lane_low = lax.broadcasted_iota(jnp.int32, (1, 128), 1) < 64
    return jnp.where(lane_low, low, high)


def carried_kernel(bt_ref, facg_ref, decay_ref, onehot_ref, arr_ref, out_ref, tok_ref):
    pairs = out_ref.shape[0]
    state_size = bt_ref.shape[0]
    ordered = jnp.dot(onehot_ref[...], arr_ref[...], preferred_element_type=jnp.float32)
    tok_ref[...] = ordered.astype(tok_ref.dtype)
    for q in range(pairs):
        x = ordered[:, 128 * q : 128 * (q + 1)]
        factor = lane_pick(facg_ref[0, :, 2 * q : 2 * q + 1], facg_ref[0, :, 2 * q + 1 : 2 * q + 2])
        scaled = (factor * x).astype(jnp.bfloat16)
        out_ref[q, 0:state_size, :] = jnp.dot(
            bt_ref[...], scaled, preferred_element_type=jnp.float32
        ).astype(out_ref.dtype)
        rows = lax.broadcasted_iota(jnp.int32, (EXTRA, 128), 0)
        decay = decay_ref[:, 128 * q : 128 * (q + 1)]
        high = decay.astype(out_ref.dtype)
        low = (decay - high.astype(jnp.float32)).astype(out_ref.dtype)
        extra = jnp.where(rows == 0, high, jnp.where(rows == 1, low, jnp.zeros_like(high)))
        out_ref[q, state_size : state_size + EXTRA, :] = extra


def send_kernel(onehot_ref, tok_ref, out_ref):
    out_ref[...] = jnp.dot(
        onehot_ref[...], tok_ref[...], preferred_element_type=jnp.float32
    ).astype(out_ref.dtype)


def send_call(onehot, tokens, first, groups, stream_count):
    rows, length = onehot.shape
    width = GROUP * 64
    picked = pl.pallas_call(
        send_kernel,
        grid=(groups,),
        in_specs=[
            pl.BlockSpec(onehot.shape, lambda g: (0, 0)),
            pl.BlockSpec((length, width), lambda g: (0, g + first)),
        ],
        out_specs=pl.BlockSpec((rows, width), lambda g: (0, g)),
        out_shape=jax.ShapeDtypeStruct((rows, groups * width), tokens.dtype),
        compiler_params=arbitrary(),
    )(onehot, tokens)
    return picked.reshape(stream_count, rows // stream_count, groups * width)


def local_kernel(scores_ref, cumg_ref, cumt_ref, stept_ref, tok_ref, skip_ref, out_ref):
    length = scores_ref.shape[0]
    heads = cumt_ref.shape[0]
    for q in range(heads // 2):
        x = tok_ref[:, 128 * q : 128 * (q + 1)]
        skip = skip_ref[:, 128 * q : 128 * (q + 1)]
        for i in range(length // TILE):
            r0 = i * TILE
            width = (i + 1) * TILE
            rows = lax.broadcasted_iota(jnp.int32, (TILE, width), 0) + r0
            cols = lax.broadcasted_iota(jnp.int32, (TILE, width), 1)
            causal = rows >= cols
            sc = scores_ref[r0 : r0 + TILE, 0:width]
            parts = []
            for j in range(2):
                h = 2 * q + j
                ct = cumg_ref[0, r0 : r0 + TILE, h : h + 1]
                cs = cumt_ref[h : h + 1, 0:width]
                st = stept_ref[h : h + 1, 0:width]
                w = jnp.where(causal, jnp.exp(ct - cs), 0.0)
                wb = ((sc * w) * st).astype(jnp.bfloat16)
                parts.append(jnp.dot(wb, x[0:width], preferred_element_type=jnp.float32))
            xt = x[r0 : r0 + TILE].astype(jnp.float32)
            total = lane_pick(parts[0], parts[1]) + skip * xt
            out_ref[r0 : r0 + TILE, 128 * q : 128 * (q + 1)] = total


def combine_kernel(place_ref, *refs):
    if len(refs) == 6:
        refs = refs[1:]
    part_ref, gath_ref, cumg_ref, c_ref, out_ref = refs
    here = place_ref[0]
    peers = gath_ref.shape[0]
    pairs = gath_ref.shape[1]
    state_size = c_ref.shape[1]
    for q in range(pairs):
        run = jnp.ones((1, 128), jnp.float32)
        state = jnp.zeros((state_size, 128), jnp.float32)
        for k in range(peers - 1, -1, -1):
            if k + 1 < peers:
                pair = gath_ref[k + 1, q, state_size : state_size + 2, :].astype(jnp.float32)
                later = pair[0:1] + pair[1:2]
                run = jnp.where(k + 1 < here, run * later, 1.0)
            weight = jnp.where(k < here, run, 0.0)
            state = state + weight * gath_ref[k, q, 0:state_size, :].astype(jnp.float32)
        readable = state.astype(jnp.bfloat16)
        inherited = jnp.dot(c_ref[...], readable, preferred_element_type=jnp.float32)
        decay = lane_pick(
            jnp.exp(cumg_ref[0, :, 2 * q : 2 * q + 1]), jnp.exp(cumg_ref[0, :, 2 * q + 1 : 2 * q + 2])
        )
        total = part_ref[:, 128 * q : 128 * (q + 1)] + decay * inherited
        out_ref[:, 128 * q : 128 * (q + 1)] = total.astype(out_ref.dtype)


def arbitrary():
    return pltpu.CompilerParams(dimension_semantics=("arbitrary",))


def carried_call(bt, fac_grouped, decay_lanes, onehot, arrived, first):
    rows, width = arrived.shape
    length = onehot.shape[0]
    groups = width // (GROUP * 64)
    state_size = bt.shape[0]
    return pl.pallas_call(
        carried_kernel,
        grid=(groups,),
        in_specs=[
            pl.BlockSpec(bt.shape, lambda g: (0, 0)),
            pl.BlockSpec((1, length, GROUP), lambda g: (g + first, 0, 0)),
            pl.BlockSpec((1, GROUP * 64), lambda g: (0, g + first)),
            pl.BlockSpec(onehot.shape, lambda g: (0, 0)),
            pl.BlockSpec((rows, GROUP * 64), lambda g: (0, g)),
        ],
        out_specs=[
            pl.BlockSpec((GROUP // 2, state_size + EXTRA, 128), lambda g: (g, 0, 0)),
            pl.BlockSpec((length, GROUP * 64), lambda g: (0, g)),
        ],
        out_shape=[
            jax.ShapeDtypeStruct((width // 128, state_size + EXTRA, 128), jnp.bfloat16),
            jax.ShapeDtypeStruct((length, width), jnp.bfloat16),
        ],
        compiler_params=arbitrary(),
    )(bt, fac_grouped, decay_lanes, onehot, arrived)


def local_call(scores, cum_grouped, cum_t, step_t, tokens, skip_lanes, first):
    length, width = tokens.shape
    groups = width // (GROUP * 64)
    return pl.pallas_call(
        local_kernel,
        grid=(groups,),
        in_specs=[
            pl.BlockSpec((length, length), lambda g: (0, 0)),
            pl.BlockSpec((1, length, GROUP), lambda g: (g + first, 0, 0)),
            pl.BlockSpec((GROUP, length), lambda g: (g + first, 0)),
            pl.BlockSpec((GROUP, length), lambda g: (g + first, 0)),
            pl.BlockSpec((length, GROUP * 64), lambda g: (0, g)),
            pl.BlockSpec((1, GROUP * 64), lambda g: (0, g + first)),
        ],
        out_specs=pl.BlockSpec((length, GROUP * 64), lambda g: (0, g)),
        out_shape=jax.ShapeDtypeStruct((length, width), jnp.float32),
        compiler_params=arbitrary(),
    )(scores, cum_grouped, cum_t, step_t, tokens, skip_lanes)


def combine_call(buffer, place, partial, gathered, cum_grouped, readout, first, total_width):
    length, width = partial.shape
    groups = width // (GROUP * 64)
    state_rows = gathered.shape[2]
    in_specs = [
        pl.BlockSpec((length, GROUP * 64), lambda g: (0, g)),
        pl.BlockSpec((gathered.shape[0], GROUP // 2, state_rows, 128), lambda g: (0, g, 0, 0)),
        pl.BlockSpec((1, length, GROUP), lambda g: (g + first, 0, 0)),
        pl.BlockSpec(readout.shape, lambda g: (0, 0)),
    ]
    operands = [partial, gathered, cum_grouped, readout]
    aliases = {}
    if buffer is not None:
        in_specs = [pl.BlockSpec(memory_space=pl.ANY)] + in_specs
        operands = [buffer] + operands
        aliases = {1: 0}
    return pl.pallas_call(
        combine_kernel,
        grid=(groups,),
        in_specs=[pl.BlockSpec(memory_space=pltpu.SMEM)] + in_specs,
        out_specs=pl.BlockSpec((length, GROUP * 64), lambda g: (0, g + first)),
        out_shape=jax.ShapeDtypeStruct((length, total_width), jnp.bfloat16),
        input_output_aliases=aliases,
        compiler_params=arbitrary(),
    )(place, *operands)


def send_rows(rows, pick_rows, stream_count, capacity):
    width = rows.shape[1]
    return jnp.take(rows, pick_rows, axis=0, mode="clip").reshape(stream_count, capacity, width)


def receive_rows(arrived, flat_rows):
    width = arrived.shape[2]
    return jnp.take(arrived.reshape(-1, width), flat_rows, axis=0, mode="clip")


def deliver(rows, pick_rows, flat_rows, stream_count, capacity):
    send = send_rows(rows, pick_rows, stream_count, capacity)
    arrived = lax.all_to_all(send, "stream", split_axis=0, concat_axis=0, tiled=True)
    return receive_rows(arrived, flat_rows)


def on_device(tokens_in, proj_in, step_raw, decay_log, head_skip_weight, row_counts):
    stream_count = lax.axis_size("stream")
    stream_index = lax.axis_index("stream")
    place_index = lax.axis_index("pos")
    tokens = tokens_in[0]
    local_rows, inner = tokens.shape
    head_count = step_raw.shape[2]
    head_size = inner // head_count
    state_size = proj_in.shape[2] // 2
    capacity = 3 * local_rows // (2 * stream_count)

    place_counts = lax.dynamic_index_in_dim(row_counts, place_index, 0, keepdims=False)
    send_counts = lax.dynamic_index_in_dim(place_counts, stream_index, 0, keepdims=False)
    recv_counts = lax.dynamic_index_in_dim(place_counts, stream_index, 1, keepdims=False)
    send_start = jnp.cumsum(send_counts) - send_counts
    slot_range = jnp.arange(capacity, dtype=jnp.int32)
    pick_rows = jnp.clip(send_start[:, None] + slot_range[None, :], 0, local_rows - 1).reshape(-1)
    recv_end = jnp.cumsum(recv_counts)
    recv_start = recv_end - recv_counts
    positions = jnp.arange(local_rows, dtype=jnp.int32)
    source = jnp.sum((recv_end[:, None] <= positions[None, :]).astype(jnp.int32), axis=0)
    source = jnp.clip(source, 0, stream_count - 1)
    source_start = jnp.take(recv_start, source)
    flat_rows = source * capacity + positions - source_start

    small = jnp.concatenate([proj_in[0], step_raw[0]], axis=1)
    small_send = send_rows(small, pick_rows, stream_count, capacity)
    sizes = CHUNK_GROUPS
    firsts = [sum(sizes[:c]) for c in range(len(sizes))]
    positions = jnp.arange(local_rows, dtype=jnp.int32)
    send_onehot = (pick_rows[:, None] == positions[None, :]).astype(jnp.bfloat16)
    first_send = send_call(send_onehot, tokens, firsts[0], sizes[0], stream_count)
    first_width = first_send.shape[2]
    first_arrived = lax.all_to_all(
        jnp.concatenate([first_send, small_send], axis=2), "stream", 0, 0, tiled=True
    )
    ordered_small = receive_rows(first_arrived[:, :, first_width:], flat_rows)
    ordered_proj = ordered_small[:, : 2 * state_size]
    ordered_steps = ordered_small[:, 2 * state_size :]

    inputs = ordered_proj[:, :state_size]
    readout = ordered_proj[:, state_size:]
    decay_rates = -jnp.exp(decay_log)
    steps = jax.nn.softplus(ordered_steps.astype(jnp.float32))
    cum = jnp.cumsum(steps * decay_rates[None, :], axis=0)
    ending = cum[-1]
    factor = jnp.exp(ending[None, :] - cum) * steps
    groups = head_count // GROUP

    def grouped(a):
        return a.reshape(local_rows, groups, GROUP).transpose(1, 0, 2)

    cum_grouped = grouped(cum)
    fac_grouped = grouped(factor)
    cum_t = cum.T
    step_t = steps.T
    decay_lanes = jnp.repeat(jnp.exp(ending), head_size).reshape(1, -1)
    skip_lanes = jnp.repeat(head_skip_weight, head_size).reshape(1, -1)
    scores = jnp.dot(readout, inputs.T, preferred_element_type=jnp.float32)
    bt = inputs.T
    place = place_index.astype(jnp.int32).reshape(1)
    slots = jnp.arange(stream_count * capacity, dtype=jnp.int32)
    onehot = (flat_rows[:, None] == slots[None, :]).astype(jnp.bfloat16)

    sends = [None] + [
        send_call(send_onehot, tokens, f, n, stream_count) for f, n in zip(firsts[1:], sizes[1:])
    ]
    partials = []
    gathers = []
    result = None
    done = 0
    for c in range(len(sizes)):
        if c == 0:
            arrived = first_arrived
        else:
            arrived = lax.all_to_all(sends[c], "stream", split_axis=0, concat_axis=0, tiled=True)
        tied = {"arrived": arrived}
        if c + 1 < len(sizes):
            tied["send"] = sends[c + 1]
        if c >= 1:
            tied["partial"] = partials[c - 1]
        if c >= 2:
            result = combine_call(
                result, place, partials[done], gathers[done], cum_grouped, readout,
                firsts[done], inner,
            )
            done += 1
            tied["result"] = result
        tied = lax.optimization_barrier(tied)
        arrived = tied["arrived"]
        if c + 1 < len(sizes):
            sends[c + 1] = tied["send"]
        if c >= 2:
            result = tied["result"]
        carried, chunk_tokens = carried_call(
            bt, fac_grouped, decay_lanes, onehot, arrived.reshape(-1, arrived.shape[2]), firsts[c]
        )
        gathers.append(lax.all_gather(carried, "pos"))
        partials.append(
            local_call(scores, cum_grouped, cum_t, step_t, chunk_tokens, skip_lanes, firsts[c])
        )
    while done < len(sizes):
        result = combine_call(
            result, place, partials[done], gathers[done], cum_grouped, readout, firsts[done], inner
        )
        done += 1
    return result[None]


def solution(mesh):
    in_specs = (
        P("stream", "pos", None),
        P("stream", "pos", None),
        P("stream", "pos", None),
        P(),
        P(),
        P(),
    )
    out_specs = P("stream", "pos", None)
    return jax.shard_map(
        on_device, mesh=mesh, in_specs=in_specs, out_specs=out_specs, check_vma=False
    )
```

```python
import jax
import jax.numpy as jnp
from jax import lax
from jax.experimental import pallas as pl
from jax.experimental.pallas import tpu as pltpu
from jax.sharding import PartitionSpec as P

GROUP = 8
TILE = 128
CHUNK_GROUPS = (4, 4, 4, 3, 1)
EXTRA = 16


def lane_pick(low, high):
    lane_low = lax.broadcasted_iota(jnp.int32, (1, 128), 1) < 64
    return jnp.where(lane_low, low, high)


def carried_kernel(bt_ref, facg_ref, decay_ref, onehot_ref, arr_ref, out_ref, tok_ref):
    pairs = out_ref.shape[0]
    state_size = bt_ref.shape[0]
    ordered = jnp.dot(onehot_ref[...], arr_ref[...], preferred_element_type=jnp.float32)
    tok_ref[...] = ordered.astype(tok_ref.dtype)
    for q in range(pairs):
        x = ordered[:, 128 * q : 128 * (q + 1)]
        factor = facg_ref[:, 128 * q : 128 * (q + 1)]
        scaled = (factor * x).astype(jnp.bfloat16)
        out_ref[q, 0:state_size, :] = jnp.dot(
            bt_ref[...], scaled, preferred_element_type=jnp.float32
        ).astype(out_ref.dtype)
        rows = lax.broadcasted_iota(jnp.int32, (EXTRA, 128), 0)
        decay = decay_ref[:, 128 * q : 128 * (q + 1)]
        high = decay.astype(out_ref.dtype)
        low = (decay - high.astype(jnp.float32)).astype(out_ref.dtype)
        extra = jnp.where(rows == 0, high, jnp.where(rows == 1, low, jnp.zeros_like(high)))
        out_ref[q, state_size : state_size + EXTRA, :] = extra


def send_kernel(onehot_ref, tok_ref, out_ref):
    out_ref[...] = jnp.dot(
        onehot_ref[...], tok_ref[...], preferred_element_type=jnp.float32
    ).astype(out_ref.dtype)


def send_call(onehot, tokens, first, groups, stream_count):
    rows, length = onehot.shape
    width = GROUP * 64
    picked = pl.pallas_call(
        send_kernel,
        grid=(groups,),
        in_specs=[
            pl.BlockSpec(onehot.shape, lambda g: (0, 0)),
            pl.BlockSpec((length, width), lambda g: (0, g + first)),
        ],
        out_specs=pl.BlockSpec((rows, width), lambda g: (0, g)),
        out_shape=jax.ShapeDtypeStruct((rows, groups * width), tokens.dtype),
        compiler_params=arbitrary(),
    )(onehot, tokens)
    return picked.reshape(stream_count, rows // stream_count, groups * width)


def local_kernel(scores_ref, cumg_ref, cumt_ref, stept_ref, tok_ref, skip_ref, out_ref):
    length = scores_ref.shape[0]
    heads = cumt_ref.shape[0]
    for q in range(heads // 2):
        x = tok_ref[:, 128 * q : 128 * (q + 1)]
        skip = skip_ref[:, 128 * q : 128 * (q + 1)]
        for i in range(length // TILE):
            r0 = i * TILE
            width = (i + 1) * TILE
            rows = lax.broadcasted_iota(jnp.int32, (TILE, width), 0) + r0
            cols = lax.broadcasted_iota(jnp.int32, (TILE, width), 1)
            causal = rows >= cols
            sc = scores_ref[r0 : r0 + TILE, 0:width]
            parts = []
            for j in range(2):
                h = 2 * q + j
                ct = cumg_ref[0, r0 : r0 + TILE, h : h + 1]
                cs = cumt_ref[h : h + 1, 0:width]
                st = stept_ref[h : h + 1, 0:width]
                w = jnp.where(causal, jnp.exp(ct - cs), 0.0)
                wb = ((sc * w) * st).astype(jnp.bfloat16)
                parts.append(jnp.dot(wb, x[0:width], preferred_element_type=jnp.float32))
            xt = x[r0 : r0 + TILE].astype(jnp.float32)
            total = lane_pick(parts[0], parts[1]) + skip * xt
            out_ref[r0 : r0 + TILE, 128 * q : 128 * (q + 1)] = total


def combine_kernel(place_ref, *refs):
    if len(refs) == 6:
        refs = refs[1:]
    part_ref, gath_ref, cumg_ref, c_ref, out_ref = refs
    here = place_ref[0]
    peers = gath_ref.shape[0]
    pairs = gath_ref.shape[1]
    state_size = c_ref.shape[1]
    for q in range(pairs):
        run = jnp.ones((1, 128), jnp.float32)
        state = jnp.zeros((state_size, 128), jnp.float32)
        for k in range(peers - 1, -1, -1):
            if k + 1 < peers:
                pair = gath_ref[k + 1, q, state_size : state_size + 2, :].astype(jnp.float32)
                later = pair[0:1] + pair[1:2]
                run = jnp.where(k + 1 < here, run * later, 1.0)
            weight = jnp.where(k < here, run, 0.0)
            state = state + weight * gath_ref[k, q, 0:state_size, :].astype(jnp.float32)
        readable = state.astype(jnp.bfloat16)
        inherited = jnp.dot(c_ref[...], readable, preferred_element_type=jnp.float32)
        decay = lane_pick(
            jnp.exp(cumg_ref[0, :, 2 * q : 2 * q + 1]), jnp.exp(cumg_ref[0, :, 2 * q + 1 : 2 * q + 2])
        )
        total = part_ref[:, 128 * q : 128 * (q + 1)] + decay * inherited
        out_ref[:, 128 * q : 128 * (q + 1)] = total.astype(out_ref.dtype)


def arbitrary():
    return pltpu.CompilerParams(dimension_semantics=("arbitrary",))


def carried_call(bt, fac_grouped, decay_lanes, onehot, arrived, first):
    rows, width = arrived.shape
    length = onehot.shape[0]
    groups = width // (GROUP * 64)
    state_size = bt.shape[0]
    return pl.pallas_call(
        carried_kernel,
        grid=(groups,),
        in_specs=[
            pl.BlockSpec(bt.shape, lambda g: (0, 0)),
            pl.BlockSpec((length, GROUP * 64), lambda g: (0, g + first)),
            pl.BlockSpec((1, GROUP * 64), lambda g: (0, g + first)),
            pl.BlockSpec(onehot.shape, lambda g: (0, 0)),
            pl.BlockSpec((rows, GROUP * 64), lambda g: (0, g)),
        ],
        out_specs=[
            pl.BlockSpec((GROUP // 2, state_size + EXTRA, 128), lambda g: (g, 0, 0)),
            pl.BlockSpec((length, GROUP * 64), lambda g: (0, g)),
        ],
        out_shape=[
            jax.ShapeDtypeStruct((width // 128, state_size + EXTRA, 128), jnp.bfloat16),
            jax.ShapeDtypeStruct((length, width), jnp.bfloat16),
        ],
        compiler_params=arbitrary(),
    )(bt, fac_grouped, decay_lanes, onehot, arrived)


def local_call(scores, cum_grouped, cum_t, step_t, tokens, skip_lanes, first):
    length, width = tokens.shape
    groups = width // (GROUP * 64)
    return pl.pallas_call(
        local_kernel,
        grid=(groups,),
        in_specs=[
            pl.BlockSpec((length, length), lambda g: (0, 0)),
            pl.BlockSpec((1, length, GROUP), lambda g: (g + first, 0, 0)),
            pl.BlockSpec((GROUP, length), lambda g: (g + first, 0)),
            pl.BlockSpec((GROUP, length), lambda g: (g + first, 0)),
            pl.BlockSpec((length, GROUP * 64), lambda g: (0, g)),
            pl.BlockSpec((1, GROUP * 64), lambda g: (0, g + first)),
        ],
        out_specs=pl.BlockSpec((length, GROUP * 64), lambda g: (0, g)),
        out_shape=jax.ShapeDtypeStruct((length, width), jnp.float32),
        compiler_params=arbitrary(),
    )(scores, cum_grouped, cum_t, step_t, tokens, skip_lanes)


def combine_call(buffer, place, partial, gathered, cum_grouped, readout, first, total_width):
    length, width = partial.shape
    groups = width // (GROUP * 64)
    state_rows = gathered.shape[2]
    in_specs = [
        pl.BlockSpec((length, GROUP * 64), lambda g: (0, g)),
        pl.BlockSpec((gathered.shape[0], GROUP // 2, state_rows, 128), lambda g: (0, g, 0, 0)),
        pl.BlockSpec((1, length, GROUP), lambda g: (g + first, 0, 0)),
        pl.BlockSpec(readout.shape, lambda g: (0, 0)),
    ]
    operands = [partial, gathered, cum_grouped, readout]
    aliases = {}
    if buffer is not None:
        in_specs = [pl.BlockSpec(memory_space=pl.ANY)] + in_specs
        operands = [buffer] + operands
        aliases = {1: 0}
    return pl.pallas_call(
        combine_kernel,
        grid=(groups,),
        in_specs=[pl.BlockSpec(memory_space=pltpu.SMEM)] + in_specs,
        out_specs=pl.BlockSpec((length, GROUP * 64), lambda g: (0, g + first)),
        out_shape=jax.ShapeDtypeStruct((length, total_width), jnp.bfloat16),
        input_output_aliases=aliases,
        compiler_params=arbitrary(),
    )(place, *operands)


def send_rows(rows, pick_rows, stream_count, capacity):
    width = rows.shape[1]
    return jnp.take(rows, pick_rows, axis=0, mode="clip").reshape(stream_count, capacity, width)


def receive_rows(arrived, flat_rows):
    width = arrived.shape[2]
    return jnp.take(arrived.reshape(-1, width), flat_rows, axis=0, mode="clip")


def deliver(rows, pick_rows, flat_rows, stream_count, capacity):
    send = send_rows(rows, pick_rows, stream_count, capacity)
    arrived = lax.all_to_all(send, "stream", split_axis=0, concat_axis=0, tiled=True)
    return receive_rows(arrived, flat_rows)


def on_device(tokens_in, proj_in, step_raw, decay_log, head_skip_weight, row_counts):
    stream_count = lax.axis_size("stream")
    stream_index = lax.axis_index("stream")
    place_index = lax.axis_index("pos")
    tokens = tokens_in[0]
    local_rows, inner = tokens.shape
    head_count = step_raw.shape[2]
    head_size = inner // head_count
    state_size = proj_in.shape[2] // 2
    capacity = 3 * local_rows // (2 * stream_count)

    place_counts = lax.dynamic_index_in_dim(row_counts, place_index, 0, keepdims=False)
    send_counts = lax.dynamic_index_in_dim(place_counts, stream_index, 0, keepdims=False)
    recv_counts = lax.dynamic_index_in_dim(place_counts, stream_index, 1, keepdims=False)
    send_start = jnp.cumsum(send_counts) - send_counts
    slot_range = jnp.arange(capacity, dtype=jnp.int32)
    pick_rows = jnp.clip(send_start[:, None] + slot_range[None, :], 0, local_rows - 1).reshape(-1)
    recv_end = jnp.cumsum(recv_counts)
    recv_start = recv_end - recv_counts
    positions = jnp.arange(local_rows, dtype=jnp.int32)
    source = jnp.sum((recv_end[:, None] <= positions[None, :]).astype(jnp.int32), axis=0)
    source = jnp.clip(source, 0, stream_count - 1)
    source_start = jnp.take(recv_start, source)
    flat_rows = source * capacity + positions - source_start

    small = jnp.concatenate([proj_in[0], step_raw[0]], axis=1)
    ordered_small = deliver(small, pick_rows, flat_rows, stream_count, capacity)
    ordered_proj = ordered_small[:, : 2 * state_size]
    ordered_steps = ordered_small[:, 2 * state_size :]

    inputs = ordered_proj[:, :state_size]
    readout = ordered_proj[:, state_size:]
    decay_rates = -jnp.exp(decay_log)
    steps = jax.nn.softplus(ordered_steps.astype(jnp.float32))
    cum = jnp.cumsum(steps * decay_rates[None, :], axis=0)
    ending = cum[-1]
    factor = jnp.exp(ending[None, :] - cum) * steps
    groups = head_count // GROUP

    def grouped(a):
        return a.reshape(local_rows, groups, GROUP).transpose(1, 0, 2)

    cum_grouped = grouped(cum)
    fac_grouped = jnp.repeat(factor, head_size, axis=1)
    cum_t = cum.T
    step_t = steps.T
    decay_lanes = jnp.repeat(jnp.exp(ending), head_size).reshape(1, -1)
    skip_lanes = jnp.repeat(head_skip_weight, head_size).reshape(1, -1)
    scores = jnp.dot(readout, inputs.T, preferred_element_type=jnp.float32)
    bt = inputs.T
    place = place_index.astype(jnp.int32).reshape(1)
    slots = jnp.arange(stream_count * capacity, dtype=jnp.int32)
    onehot = (flat_rows[:, None] == slots[None, :]).astype(jnp.bfloat16)

    sizes = CHUNK_GROUPS
    firsts = [sum(sizes[:c]) for c in range(len(sizes))]
    group_width = GROUP * head_size
    send_onehot = (pick_rows[:, None] == positions[None, :]).astype(jnp.bfloat16)
    sends = [send_call(send_onehot, tokens, f, n, stream_count) for f, n in zip(firsts, sizes)]
    partials = []
    gathers = []
    result = None
    done = 0
    for c in range(len(sizes)):
        arrived = lax.all_to_all(sends[c], "stream", split_axis=0, concat_axis=0, tiled=True)
        tied = {"arrived": arrived}
        if c + 1 < len(sizes):
            tied["send"] = sends[c + 1]
        if c >= 1:
            tied["partial"] = partials[c - 1]
        if c >= 2:
            result = combine_call(
                result, place, partials[done], gathers[done], cum_grouped, readout,
                firsts[done], inner,
            )
            done += 1
            tied["result"] = result
        tied = lax.optimization_barrier(tied)
        arrived = tied["arrived"]
        if c + 1 < len(sizes):
            sends[c + 1] = tied["send"]
        if c >= 2:
            result = tied["result"]
        carried, chunk_tokens = carried_call(
            bt, fac_grouped, decay_lanes, onehot, arrived.reshape(-1, arrived.shape[2]), firsts[c]
        )
        gathers.append(lax.all_gather(carried, "pos"))
        partials.append(
            local_call(scores, cum_grouped, cum_t, step_t, chunk_tokens, skip_lanes, firsts[c])
        )
    while done < len(sizes):
        result = combine_call(
            result, place, partials[done], gathers[done], cum_grouped, readout, firsts[done], inner
        )
        done += 1
    return result[None]


def solution(mesh):
    in_specs = (
        P("stream", "pos", None),
        P("stream", "pos", None),
        P("stream", "pos", None),
        P(),
        P(),
        P(),
    )
    out_specs = P("stream", "pos", None)
    return jax.shard_map(
        on_device, mesh=mesh, in_specs=in_specs, out_specs=out_specs, check_vma=False
    )
```

```python
import jax
import jax.numpy as jnp
from jax import lax
from jax.experimental import pallas as pl
from jax.experimental.pallas import tpu as pltpu
from jax.sharding import PartitionSpec as P

GROUP = 8
TILE = 128
CHUNK_GROUPS = (4, 4, 4, 3, 1)
EXTRA = 16


def lane_pick(low, high):
    lane_low = lax.broadcasted_iota(jnp.int32, (1, 128), 1) < 64
    return jnp.where(lane_low, low, high)


def carried_kernel(bt_ref, facg_ref, decay_ref, onehot_ref, arr_ref, out_ref, tok_ref):
    pairs = out_ref.shape[0]
    state_size = bt_ref.shape[0]
    ordered = jnp.dot(onehot_ref[...], arr_ref[...], preferred_element_type=jnp.float32)
    tok_ref[...] = ordered.astype(tok_ref.dtype)
    for q in range(pairs):
        x = ordered[:, 128 * q : 128 * (q + 1)]
        factor = lane_pick(facg_ref[0, :, 2 * q : 2 * q + 1], facg_ref[0, :, 2 * q + 1 : 2 * q + 2])
        scaled = (factor * x).astype(jnp.bfloat16)
        out_ref[q, 0:state_size, :] = jnp.dot(
            bt_ref[...], scaled, preferred_element_type=jnp.float32
        ).astype(out_ref.dtype)
        rows = lax.broadcasted_iota(jnp.int32, (EXTRA, 128), 0)
        decay = decay_ref[:, 128 * q : 128 * (q + 1)]
        high = decay.astype(out_ref.dtype)
        low = (decay - high.astype(jnp.float32)).astype(out_ref.dtype)
        extra = jnp.where(rows == 0, high, jnp.where(rows == 1, low, jnp.zeros_like(high)))
        out_ref[q, state_size : state_size + EXTRA, :] = extra


def send_kernel(onehot_ref, tok_ref, out_ref):
    out_ref[...] = jnp.dot(
        onehot_ref[...], tok_ref[...], preferred_element_type=jnp.float32
    ).astype(out_ref.dtype)


def send_call(onehot, tokens, first, groups, stream_count):
    rows, length = onehot.shape
    width = GROUP * 64
    picked = pl.pallas_call(
        send_kernel,
        grid=(groups,),
        in_specs=[
            pl.BlockSpec(onehot.shape, lambda g: (0, 0)),
            pl.BlockSpec((length, width), lambda g: (0, g + first)),
        ],
        out_specs=pl.BlockSpec((rows, width), lambda g: (0, g)),
        out_shape=jax.ShapeDtypeStruct((rows, groups * width), tokens.dtype),
        compiler_params=arbitrary(),
    )(onehot, tokens)
    return picked.reshape(stream_count, rows // stream_count, groups * width)


def local_kernel(scores_ref, cumg_ref, cumt_ref, stept_ref, tok_ref, skip_ref, out_ref):
    length = scores_ref.shape[0]
    heads = cumt_ref.shape[0]
    for q in range(heads // 2):
        x = tok_ref[:, 128 * q : 128 * (q + 1)]
        skip = skip_ref[:, 128 * q : 128 * (q + 1)]
        for i in range(length // TILE):
            r0 = i * TILE
            width = (i + 1) * TILE
            rows = lax.broadcasted_iota(jnp.int32, (TILE, width), 0) + r0
            cols = lax.broadcasted_iota(jnp.int32, (TILE, width), 1)
            causal = rows >= cols
            sc = scores_ref[r0 : r0 + TILE, 0:width]
            parts = []
            for j in range(2):
                h = 2 * q + j
                ct = cumg_ref[0, r0 : r0 + TILE, h : h + 1]
                cs = cumt_ref[h : h + 1, 0:width]
                st = stept_ref[h : h + 1, 0:width]
                w = jnp.where(causal, jnp.exp(ct - cs), 0.0)
                wb = ((sc * w) * st).astype(jnp.bfloat16)
                parts.append(jnp.dot(wb, x[0:width], preferred_element_type=jnp.float32))
            xt = x[r0 : r0 + TILE].astype(jnp.float32)
            total = lane_pick(parts[0], parts[1]) + skip * xt
            out_ref[r0 : r0 + TILE, 128 * q : 128 * (q + 1)] = total


def combine_kernel(place_ref, *refs):
    if len(refs) == 6:
        refs = refs[1:]
    part_ref, gath_ref, cumg_ref, c_ref, out_ref = refs
    here = place_ref[0]
    peers = gath_ref.shape[0]
    pairs = gath_ref.shape[1]
    state_size = c_ref.shape[1]
    for q in range(pairs):
        run = jnp.ones((1, 128), jnp.float32)
        state = jnp.zeros((state_size, 128), jnp.float32)
        for k in range(peers - 1, -1, -1):
            if k + 1 < peers:
                pair = gath_ref[k + 1, q, state_size : state_size + 2, :].astype(jnp.float32)
                later = pair[0:1] + pair[1:2]
                run = jnp.where(k + 1 < here, run * later, 1.0)
            weight = jnp.where(k < here, run, 0.0)
            state = state + weight * gath_ref[k, q, 0:state_size, :].astype(jnp.float32)
        readable = state.astype(jnp.bfloat16)
        inherited = jnp.dot(c_ref[...], readable, preferred_element_type=jnp.float32)
        decay = lane_pick(
            jnp.exp(cumg_ref[0, :, 2 * q : 2 * q + 1]), jnp.exp(cumg_ref[0, :, 2 * q + 1 : 2 * q + 2])
        )
        total = part_ref[:, 128 * q : 128 * (q + 1)] + decay * inherited
        out_ref[:, 128 * q : 128 * (q + 1)] = total.astype(out_ref.dtype)


def arbitrary():
    return pltpu.CompilerParams(dimension_semantics=("arbitrary",))


def carried_call(bt, fac_grouped, decay_lanes, onehot, arrived, first):
    rows, width = arrived.shape
    length = onehot.shape[0]
    groups = width // (GROUP * 64)
    state_size = bt.shape[0]
    return pl.pallas_call(
        carried_kernel,
        grid=(groups,),
        in_specs=[
            pl.BlockSpec(bt.shape, lambda g: (0, 0)),
            pl.BlockSpec((1, length, GROUP), lambda g: (g + first, 0, 0)),
            pl.BlockSpec((1, GROUP * 64), lambda g: (0, g + first)),
            pl.BlockSpec(onehot.shape, lambda g: (0, 0)),
            pl.BlockSpec((rows, GROUP * 64), lambda g: (0, g)),
        ],
        out_specs=[
            pl.BlockSpec((GROUP // 2, state_size + EXTRA, 128), lambda g: (g, 0, 0)),
            pl.BlockSpec((length, GROUP * 64), lambda g: (0, g)),
        ],
        out_shape=[
            jax.ShapeDtypeStruct((width // 128, state_size + EXTRA, 128), jnp.bfloat16),
            jax.ShapeDtypeStruct((length, width), jnp.bfloat16),
        ],
        compiler_params=arbitrary(),
    )(bt, fac_grouped, decay_lanes, onehot, arrived)


def local_call(scores, cum_grouped, cum_t, step_t, tokens, skip_lanes, first):
    length, width = tokens.shape
    groups = width // (GROUP * 64)
    return pl.pallas_call(
        local_kernel,
        grid=(groups,),
        in_specs=[
            pl.BlockSpec((length, length), lambda g: (0, 0)),
            pl.BlockSpec((1, length, GROUP), lambda g: (g + first, 0, 0)),
            pl.BlockSpec((GROUP, length), lambda g: (g + first, 0)),
            pl.BlockSpec((GROUP, length), lambda g: (g + first, 0)),
            pl.BlockSpec((length, GROUP * 64), lambda g: (0, g)),
            pl.BlockSpec((1, GROUP * 64), lambda g: (0, g + first)),
        ],
        out_specs=pl.BlockSpec((length, GROUP * 64), lambda g: (0, g)),
        out_shape=jax.ShapeDtypeStruct((length, width), jnp.float32),
        compiler_params=arbitrary(),
    )(scores, cum_grouped, cum_t, step_t, tokens, skip_lanes)


def combine_call(buffer, place, partial, gathered, cum_grouped, readout, first, total_width):
    length, width = partial.shape
    groups = width // (GROUP * 64)
    state_rows = gathered.shape[2]
    in_specs = [
        pl.BlockSpec((length, GROUP * 64), lambda g: (0, g)),
        pl.BlockSpec((gathered.shape[0], GROUP // 2, state_rows, 128), lambda g: (0, g, 0, 0)),
        pl.BlockSpec((1, length, GROUP), lambda g: (g + first, 0, 0)),
        pl.BlockSpec(readout.shape, lambda g: (0, 0)),
    ]
    operands = [partial, gathered, cum_grouped, readout]
    aliases = {}
    if buffer is not None:
        in_specs = [pl.BlockSpec(memory_space=pl.ANY)] + in_specs
        operands = [buffer] + operands
        aliases = {1: 0}
    return pl.pallas_call(
        combine_kernel,
        grid=(groups,),
        in_specs=[pl.BlockSpec(memory_space=pltpu.SMEM)] + in_specs,
        out_specs=pl.BlockSpec((length, GROUP * 64), lambda g: (0, g + first)),
        out_shape=jax.ShapeDtypeStruct((length, total_width), jnp.bfloat16),
        input_output_aliases=aliases,
        compiler_params=arbitrary(),
    )(place, *operands)


def send_rows(rows, pick_rows, stream_count, capacity):
    width = rows.shape[1]
    return jnp.take(rows, pick_rows, axis=0, mode="clip").reshape(stream_count, capacity, width)


def receive_rows(arrived, flat_rows):
    width = arrived.shape[2]
    return jnp.take(arrived.reshape(-1, width), flat_rows, axis=0, mode="clip")


def deliver(rows, pick_rows, flat_rows, stream_count, capacity):
    send = send_rows(rows, pick_rows, stream_count, capacity)
    arrived = lax.all_to_all(send, "stream", split_axis=0, concat_axis=0, tiled=True)
    return receive_rows(arrived, flat_rows)


def on_device(tokens_in, proj_in, step_raw, decay_log, head_skip_weight, row_counts):
    stream_count = lax.axis_size("stream")
    stream_index = lax.axis_index("stream")
    place_index = lax.axis_index("pos")
    tokens = tokens_in[0]
    local_rows, inner = tokens.shape
    head_count = step_raw.shape[2]
    head_size = inner // head_count
    state_size = proj_in.shape[2] // 2
    capacity = 3 * local_rows // (2 * stream_count)

    place_counts = lax.dynamic_index_in_dim(row_counts, place_index, 0, keepdims=False)
    send_counts = lax.dynamic_index_in_dim(place_counts, stream_index, 0, keepdims=False)
    recv_counts = lax.dynamic_index_in_dim(place_counts, stream_index, 1, keepdims=False)
    send_start = jnp.cumsum(send_counts) - send_counts
    slot_range = jnp.arange(capacity, dtype=jnp.int32)
    pick_rows = jnp.clip(send_start[:, None] + slot_range[None, :], 0, local_rows - 1).reshape(-1)
    recv_end = jnp.cumsum(recv_counts)
    recv_start = recv_end - recv_counts
    positions = jnp.arange(local_rows, dtype=jnp.int32)
    source = jnp.sum((recv_end[:, None] <= positions[None, :]).astype(jnp.int32), axis=0)
    source = jnp.clip(source, 0, stream_count - 1)
    source_start = jnp.take(recv_start, source)
    flat_rows = source * capacity + positions - source_start

    small = jnp.concatenate([proj_in[0], step_raw[0]], axis=1)
    ordered_small = deliver(small, pick_rows, flat_rows, stream_count, capacity)
    ordered_proj = ordered_small[:, : 2 * state_size]
    ordered_steps = ordered_small[:, 2 * state_size :]

    inputs = ordered_proj[:, :state_size]
    readout = ordered_proj[:, state_size:]
    decay_rates = -jnp.exp(decay_log)
    steps = jax.nn.softplus(ordered_steps.astype(jnp.float32))
    cum = jnp.cumsum(steps * decay_rates[None, :], axis=0)
    ending = cum[-1]
    factor = jnp.exp(ending[None, :] - cum) * steps
    groups = head_count // GROUP

    def grouped(a):
        return a.reshape(local_rows, groups, GROUP).transpose(1, 0, 2)

    cum_grouped = grouped(cum)
    fac_grouped = grouped(factor)
    cum_t = cum.T
    step_t = steps.T
    decay_lanes = jnp.repeat(jnp.exp(ending), head_size).reshape(1, -1)
    skip_lanes = jnp.repeat(head_skip_weight, head_size).reshape(1, -1)
    scores = jnp.dot(readout, inputs.T, preferred_element_type=jnp.float32)
    bt = inputs.T
    place = place_index.astype(jnp.int32).reshape(1)
    slots = jnp.arange(stream_count * capacity, dtype=jnp.int32)
    onehot = (flat_rows[:, None] == slots[None, :]).astype(jnp.bfloat16)

    sizes = CHUNK_GROUPS
    firsts = [sum(sizes[:c]) for c in range(len(sizes))]
    group_width = GROUP * head_size
    send_onehot = (pick_rows[:, None] == positions[None, :]).astype(jnp.bfloat16)
    sends = [send_call(send_onehot, tokens, f, n, stream_count) for f, n in zip(firsts, sizes)]
    partials = []
    gathers = []
    result = None
    done = 0
    for c in range(len(sizes)):
        arrived = lax.all_to_all(sends[c], "stream", split_axis=0, concat_axis=0, tiled=True)
        tied = {"arrived": arrived}
        if c + 1 < len(sizes):
            tied["send"] = sends[c + 1]
        if c >= 1:
            tied["partial"] = partials[c - 1]
        if c >= 2:
            result = combine_call(
                result, place, partials[done], gathers[done], cum_grouped, readout,
                firsts[done], inner,
            )
            done += 1
            tied["result"] = result
        tied = lax.optimization_barrier(tied)
        arrived = tied["arrived"]
        if c + 1 < len(sizes):
            sends[c + 1] = tied["send"]
        if c >= 2:
            result = tied["result"]
        carried, chunk_tokens = carried_call(
            bt, fac_grouped, decay_lanes, onehot, arrived.reshape(-1, arrived.shape[2]), firsts[c]
        )
        if c + 1 < len(sizes):
            gathers.append(lax.all_gather(carried, "pos"))
        else:
            half = carried.shape[0] // 2
            gathers.append(
                jnp.concatenate(
                    [lax.all_gather(carried[:half], "pos"), lax.all_gather(carried[half:], "pos")],
                    axis=1,
                )
            )
        partials.append(
            local_call(scores, cum_grouped, cum_t, step_t, chunk_tokens, skip_lanes, firsts[c])
        )
    while done < len(sizes):
        result = combine_call(
            result, place, partials[done], gathers[done], cum_grouped, readout, firsts[done], inner
        )
        done += 1
    return result[None]


def solution(mesh):
    in_specs = (
        P("stream", "pos", None),
        P("stream", "pos", None),
        P("stream", "pos", None),
        P(),
        P(),
        P(),
    )
    out_specs = P("stream", "pos", None)
    return jax.shard_map(
        on_device, mesh=mesh, in_specs=in_specs, out_specs=out_specs, check_vma=False
    )
```

```python
import jax
import jax.numpy as jnp
from jax import lax
from jax.experimental import pallas as pl
from jax.experimental.pallas import tpu as pltpu
from jax.sharding import PartitionSpec as P

GROUP = 8
TILE = 128
CHUNK_GROUPS = (4, 4, 4, 4)
EXTRA = 16


def lane_pick(low, high):
    lane_low = lax.broadcasted_iota(jnp.int32, (1, 128), 1) < 64
    return jnp.where(lane_low, low, high)


def carried_kernel(bt_ref, facg_ref, decay_ref, onehot_ref, arr_ref, out_ref, tok_ref):
    pairs = out_ref.shape[0]
    state_size = bt_ref.shape[0]
    ordered = jnp.dot(onehot_ref[...], arr_ref[...], preferred_element_type=jnp.float32)
    tok_ref[...] = ordered.astype(tok_ref.dtype)
    for q in range(pairs):
        x = ordered[:, 128 * q : 128 * (q + 1)]
        factor = lane_pick(facg_ref[0, :, 2 * q : 2 * q + 1], facg_ref[0, :, 2 * q + 1 : 2 * q + 2])
        scaled = (factor * x).astype(jnp.bfloat16)
        out_ref[q, 0:state_size, :] = jnp.dot(
            bt_ref[...], scaled, preferred_element_type=jnp.float32
        ).astype(out_ref.dtype)
        rows = lax.broadcasted_iota(jnp.int32, (EXTRA, 128), 0)
        decay = decay_ref[:, 128 * q : 128 * (q + 1)]
        high = decay.astype(out_ref.dtype)
        low = (decay - high.astype(jnp.float32)).astype(out_ref.dtype)
        extra = jnp.where(rows == 0, high, jnp.where(rows == 1, low, jnp.zeros_like(high)))
        out_ref[q, state_size : state_size + EXTRA, :] = extra


def send_kernel(onehot_ref, tok_ref, out_ref):
    out_ref[...] = jnp.dot(
        onehot_ref[...], tok_ref[...], preferred_element_type=jnp.float32
    ).astype(out_ref.dtype)


def send_call(onehot, tokens, first, groups, stream_count):
    rows, length = onehot.shape
    width = GROUP * 64
    picked = pl.pallas_call(
        send_kernel,
        grid=(groups,),
        in_specs=[
            pl.BlockSpec(onehot.shape, lambda g: (0, 0)),
            pl.BlockSpec((length, width), lambda g: (0, g + first)),
        ],
        out_specs=pl.BlockSpec((rows, width), lambda g: (0, g)),
        out_shape=jax.ShapeDtypeStruct((rows, groups * width), tokens.dtype),
        compiler_params=arbitrary(),
    )(onehot, tokens)
    return picked.reshape(stream_count, rows // stream_count, groups * width)


def local_kernel(scores_ref, cumg_ref, cumt_ref, stept_ref, tok_ref, skip_ref, out_ref):
    length = scores_ref.shape[0]
    heads = cumt_ref.shape[0]
    for q in range(heads // 2):
        x = tok_ref[:, 128 * q : 128 * (q + 1)]
        skip = skip_ref[:, 128 * q : 128 * (q + 1)]
        for i in range(length // TILE):
            r0 = i * TILE
            width = (i + 1) * TILE
            rows = lax.broadcasted_iota(jnp.int32, (TILE, width), 0) + r0
            cols = lax.broadcasted_iota(jnp.int32, (TILE, width), 1)
            causal = rows >= cols
            sc = scores_ref[r0 : r0 + TILE, 0:width]
            parts = []
            for j in range(2):
                h = 2 * q + j
                ct = cumg_ref[0, r0 : r0 + TILE, h : h + 1]
                cs = cumt_ref[h : h + 1, 0:width]
                st = stept_ref[h : h + 1, 0:width]
                w = jnp.where(causal, jnp.exp(ct - cs), 0.0)
                wb = ((sc * w) * st).astype(jnp.bfloat16)
                parts.append(jnp.dot(wb, x[0:width], preferred_element_type=jnp.float32))
            xt = x[r0 : r0 + TILE].astype(jnp.float32)
            total = lane_pick(parts[0], parts[1]) + skip * xt
            out_ref[r0 : r0 + TILE, 128 * q : 128 * (q + 1)] = total


def combine_kernel(place_ref, *refs):
    if len(refs) == 6:
        refs = refs[1:]
    part_ref, gath_ref, cumg_ref, c_ref, out_ref = refs
    here = place_ref[0]
    peers = gath_ref.shape[0]
    pairs = gath_ref.shape[1]
    state_size = c_ref.shape[1]
    for q in range(pairs):
        run = jnp.ones((1, 128), jnp.float32)
        state = jnp.zeros((state_size, 128), jnp.float32)
        for k in range(peers - 1, -1, -1):
            if k + 1 < peers:
                pair = gath_ref[k + 1, q, state_size : state_size + 2, :].astype(jnp.float32)
                later = pair[0:1] + pair[1:2]
                run = jnp.where(k + 1 < here, run * later, 1.0)
            weight = jnp.where(k < here, run, 0.0)
            state = state + weight * gath_ref[k, q, 0:state_size, :].astype(jnp.float32)
        readable = state.astype(jnp.bfloat16)
        inherited = jnp.dot(c_ref[...], readable, preferred_element_type=jnp.float32)
        decay = lane_pick(
            jnp.exp(cumg_ref[0, :, 2 * q : 2 * q + 1]), jnp.exp(cumg_ref[0, :, 2 * q + 1 : 2 * q + 2])
        )
        total = part_ref[:, 128 * q : 128 * (q + 1)] + decay * inherited
        out_ref[:, 128 * q : 128 * (q + 1)] = total.astype(out_ref.dtype)


def arbitrary():
    return pltpu.CompilerParams(dimension_semantics=("arbitrary",))


def carried_call(bt, fac_grouped, decay_lanes, onehot, arrived, first):
    rows, width = arrived.shape
    length = onehot.shape[0]
    groups = width // (GROUP * 64)
    state_size = bt.shape[0]
    return pl.pallas_call(
        carried_kernel,
        grid=(groups,),
        in_specs=[
            pl.BlockSpec(bt.shape, lambda g: (0, 0)),
            pl.BlockSpec((1, length, GROUP), lambda g: (g + first, 0, 0)),
            pl.BlockSpec((1, GROUP * 64), lambda g: (0, g + first)),
            pl.BlockSpec(onehot.shape, lambda g: (0, 0)),
            pl.BlockSpec((rows, GROUP * 64), lambda g: (0, g)),
        ],
        out_specs=[
            pl.BlockSpec((GROUP // 2, state_size + EXTRA, 128), lambda g: (g, 0, 0)),
            pl.BlockSpec((length, GROUP * 64), lambda g: (0, g)),
        ],
        out_shape=[
            jax.ShapeDtypeStruct((width // 128, state_size + EXTRA, 128), jnp.bfloat16),
            jax.ShapeDtypeStruct((length, width), jnp.bfloat16),
        ],
        compiler_params=arbitrary(),
    )(bt, fac_grouped, decay_lanes, onehot, arrived)


def local_call(scores, cum_grouped, cum_t, step_t, tokens, skip_lanes, first):
    length, width = tokens.shape
    groups = width // (GROUP * 64)
    return pl.pallas_call(
        local_kernel,
        grid=(groups,),
        in_specs=[
            pl.BlockSpec((length, length), lambda g: (0, 0)),
            pl.BlockSpec((1, length, GROUP), lambda g: (g + first, 0, 0)),
            pl.BlockSpec((GROUP, length), lambda g: (g + first, 0)),
            pl.BlockSpec((GROUP, length), lambda g: (g + first, 0)),
            pl.BlockSpec((length, GROUP * 64), lambda g: (0, g)),
            pl.BlockSpec((1, GROUP * 64), lambda g: (0, g + first)),
        ],
        out_specs=pl.BlockSpec((length, GROUP * 64), lambda g: (0, g)),
        out_shape=jax.ShapeDtypeStruct((length, width), jnp.float32),
        compiler_params=arbitrary(),
    )(scores, cum_grouped, cum_t, step_t, tokens, skip_lanes)


def combine_call(buffer, place, partial, gathered, cum_grouped, readout, first, total_width):
    length, width = partial.shape
    groups = width // (GROUP * 64)
    state_rows = gathered.shape[2]
    in_specs = [
        pl.BlockSpec((length, GROUP * 64), lambda g: (0, g)),
        pl.BlockSpec((gathered.shape[0], GROUP // 2, state_rows, 128), lambda g: (0, g, 0, 0)),
        pl.BlockSpec((1, length, GROUP), lambda g: (g + first, 0, 0)),
        pl.BlockSpec(readout.shape, lambda g: (0, 0)),
    ]
    operands = [partial, gathered, cum_grouped, readout]
    aliases = {}
    if buffer is not None:
        in_specs = [pl.BlockSpec(memory_space=pl.ANY)] + in_specs
        operands = [buffer] + operands
        aliases = {1: 0}
    return pl.pallas_call(
        combine_kernel,
        grid=(groups,),
        in_specs=[pl.BlockSpec(memory_space=pltpu.SMEM)] + in_specs,
        out_specs=pl.BlockSpec((length, GROUP * 64), lambda g: (0, g + first)),
        out_shape=jax.ShapeDtypeStruct((length, total_width), jnp.bfloat16),
        input_output_aliases=aliases,
        compiler_params=arbitrary(),
    )(place, *operands)


def send_rows(rows, pick_rows, stream_count, capacity):
    width = rows.shape[1]
    return jnp.take(rows, pick_rows, axis=0, mode="clip").reshape(stream_count, capacity, width)


def receive_rows(arrived, flat_rows):
    width = arrived.shape[2]
    return jnp.take(arrived.reshape(-1, width), flat_rows, axis=0, mode="clip")


def deliver(rows, pick_rows, flat_rows, stream_count, capacity):
    send = send_rows(rows, pick_rows, stream_count, capacity)
    arrived = lax.all_to_all(send, "stream", split_axis=0, concat_axis=0, tiled=True)
    return receive_rows(arrived, flat_rows)


def on_device(tokens_in, proj_in, step_raw, decay_log, head_skip_weight, row_counts):
    stream_count = lax.axis_size("stream")
    stream_index = lax.axis_index("stream")
    place_index = lax.axis_index("pos")
    tokens = tokens_in[0]
    local_rows, inner = tokens.shape
    head_count = step_raw.shape[2]
    head_size = inner // head_count
    state_size = proj_in.shape[2] // 2
    capacity = 3 * local_rows // (2 * stream_count)

    place_counts = lax.dynamic_index_in_dim(row_counts, place_index, 0, keepdims=False)
    send_counts = lax.dynamic_index_in_dim(place_counts, stream_index, 0, keepdims=False)
    recv_counts = lax.dynamic_index_in_dim(place_counts, stream_index, 1, keepdims=False)
    send_start = jnp.cumsum(send_counts) - send_counts
    slot_range = jnp.arange(capacity, dtype=jnp.int32)
    pick_rows = jnp.clip(send_start[:, None] + slot_range[None, :], 0, local_rows - 1).reshape(-1)
    recv_end = jnp.cumsum(recv_counts)
    recv_start = recv_end - recv_counts
    positions = jnp.arange(local_rows, dtype=jnp.int32)
    source = jnp.sum((recv_end[:, None] <= positions[None, :]).astype(jnp.int32), axis=0)
    source = jnp.clip(source, 0, stream_count - 1)
    source_start = jnp.take(recv_start, source)
    flat_rows = source * capacity + positions - source_start

    small = jnp.concatenate([proj_in[0], step_raw[0]], axis=1)
    ordered_small = deliver(small, pick_rows, flat_rows, stream_count, capacity)
    ordered_proj = ordered_small[:, : 2 * state_size]
    ordered_steps = ordered_small[:, 2 * state_size :]

    inputs = ordered_proj[:, :state_size]
    readout = ordered_proj[:, state_size:]
    decay_rates = -jnp.exp(decay_log)
    steps = jax.nn.softplus(ordered_steps.astype(jnp.float32))
    cum = jnp.cumsum(steps * decay_rates[None, :], axis=0)
    ending = cum[-1]
    factor = jnp.exp(ending[None, :] - cum) * steps
    groups = head_count // GROUP

    def grouped(a):
        return a.reshape(local_rows, groups, GROUP).transpose(1, 0, 2)

    cum_grouped = grouped(cum)
    fac_grouped = grouped(factor)
    cum_t = cum.T
    step_t = steps.T
    decay_lanes = jnp.repeat(jnp.exp(ending), head_size).reshape(1, -1)
    skip_lanes = jnp.repeat(head_skip_weight, head_size).reshape(1, -1)
    scores = jnp.dot(readout, inputs.T, preferred_element_type=jnp.float32)
    bt = inputs.T
    place = place_index.astype(jnp.int32).reshape(1)
    slots = jnp.arange(stream_count * capacity, dtype=jnp.int32)
    onehot = (flat_rows[:, None] == slots[None, :]).astype(jnp.bfloat16)

    sizes = CHUNK_GROUPS
    firsts = [sum(sizes[:c]) for c in range(len(sizes))]
    group_width = GROUP * head_size
    send_onehot = (pick_rows[:, None] == positions[None, :]).astype(jnp.bfloat16)
    sends = [send_call(send_onehot, tokens, f, n, stream_count) for f, n in zip(firsts, sizes)]
    partials = []
    gathers = []
    result = None
    done = 0
    for c in range(len(sizes)):
        arrived = lax.all_to_all(sends[c], "stream", split_axis=0, concat_axis=0, tiled=True)
        tied = {"arrived": arrived}
        if c + 1 < len(sizes):
            tied["send"] = sends[c + 1]
        if c >= 1:
            tied["partial"] = partials[c - 1]
        if c >= 2:
            result = combine_call(
                result, place, partials[done], gathers[done], cum_grouped, readout,
                firsts[done], inner,
            )
            done += 1
            tied["result"] = result
        tied = lax.optimization_barrier(tied)
        arrived = tied["arrived"]
        if c + 1 < len(sizes):
            sends[c + 1] = tied["send"]
        if c >= 2:
            result = tied["result"]
        carried, chunk_tokens = carried_call(
            bt, fac_grouped, decay_lanes, onehot, arrived.reshape(-1, arrived.shape[2]), firsts[c]
        )
        gathers.append(lax.all_gather(carried, "pos"))
        partials.append(
            local_call(scores, cum_grouped, cum_t, step_t, chunk_tokens, skip_lanes, firsts[c])
        )
    while done < len(sizes):
        result = combine_call(
            result, place, partials[done], gathers[done], cum_grouped, readout, firsts[done], inner
        )
        done += 1
    return result[None]


def solution(mesh):
    in_specs = (
        P("stream", "pos", None),
        P("stream", "pos", None),
        P("stream", "pos", None),
        P(),
        P(),
        P(),
    )
    out_specs = P("stream", "pos", None)
    return jax.shard_map(
        on_device, mesh=mesh, in_specs=in_specs, out_specs=out_specs, check_vma=False
    )
```

```python
import jax
import jax.numpy as jnp
from jax import lax
from jax.experimental import pallas as pl
from jax.experimental.pallas import tpu as pltpu
from jax.sharding import PartitionSpec as P

GROUP = 8
TILE = 128
CHUNK_GROUPS = (2, 4, 4, 4, 2)
EXTRA = 16


def lane_pick(low, high):
    lane_low = lax.broadcasted_iota(jnp.int32, (1, 128), 1) < 64
    return jnp.where(lane_low, low, high)


def carried_kernel(bt_ref, facg_ref, decay_ref, onehot_ref, arr_ref, out_ref, tok_ref):
    pairs = out_ref.shape[0]
    state_size = bt_ref.shape[0]
    ordered = jnp.dot(onehot_ref[...], arr_ref[...], preferred_element_type=jnp.float32)
    tok_ref[...] = ordered.astype(tok_ref.dtype)
    for q in range(pairs):
        x = ordered[:, 128 * q : 128 * (q + 1)]
        factor = lane_pick(facg_ref[0, :, 2 * q : 2 * q + 1], facg_ref[0, :, 2 * q + 1 : 2 * q + 2])
        scaled = (factor * x).astype(jnp.bfloat16)
        out_ref[q, 0:state_size, :] = jnp.dot(
            bt_ref[...], scaled, preferred_element_type=jnp.float32
        ).astype(out_ref.dtype)
        rows = lax.broadcasted_iota(jnp.int32, (EXTRA, 128), 0)
        decay = decay_ref[:, 128 * q : 128 * (q + 1)]
        high = decay.astype(out_ref.dtype)
        low = (decay - high.astype(jnp.float32)).astype(out_ref.dtype)
        extra = jnp.where(rows == 0, high, jnp.where(rows == 1, low, jnp.zeros_like(high)))
        out_ref[q, state_size : state_size + EXTRA, :] = extra


def send_kernel(onehot_ref, tok_ref, out_ref):
    out_ref[...] = jnp.dot(
        onehot_ref[...], tok_ref[...], preferred_element_type=jnp.float32
    ).astype(out_ref.dtype)


def send_call(onehot, tokens, first, groups, stream_count):
    rows, length = onehot.shape
    width = GROUP * 64
    picked = pl.pallas_call(
        send_kernel,
        grid=(groups,),
        in_specs=[
            pl.BlockSpec(onehot.shape, lambda g: (0, 0)),
            pl.BlockSpec((length, width), lambda g: (0, g + first)),
        ],
        out_specs=pl.BlockSpec((rows, width), lambda g: (0, g)),
        out_shape=jax.ShapeDtypeStruct((rows, groups * width), tokens.dtype),
        compiler_params=arbitrary(),
    )(onehot, tokens)
    return picked.reshape(stream_count, rows // stream_count, groups * width)


def local_kernel(scores_ref, cumg_ref, cumt_ref, stept_ref, tok_ref, skip_ref, out_ref):
    length = scores_ref.shape[0]
    heads = cumt_ref.shape[0]
    for q in range(heads // 2):
        x = tok_ref[:, 128 * q : 128 * (q + 1)]
        skip = skip_ref[:, 128 * q : 128 * (q + 1)]
        for i in range(length // TILE):
            r0 = i * TILE
            width = (i + 1) * TILE
            rows = lax.broadcasted_iota(jnp.int32, (TILE, width), 0) + r0
            cols = lax.broadcasted_iota(jnp.int32, (TILE, width), 1)
            causal = rows >= cols
            sc = scores_ref[r0 : r0 + TILE, 0:width]
            parts = []
            for j in range(2):
                h = 2 * q + j
                ct = cumg_ref[0, r0 : r0 + TILE, h : h + 1]
                cs = cumt_ref[h : h + 1, 0:width]
                st = stept_ref[h : h + 1, 0:width]
                w = jnp.where(causal, jnp.exp(ct - cs), 0.0)
                wb = ((sc * w) * st).astype(jnp.bfloat16)
                parts.append(jnp.dot(wb, x[0:width], preferred_element_type=jnp.float32))
            xt = x[r0 : r0 + TILE].astype(jnp.float32)
            total = lane_pick(parts[0], parts[1]) + skip * xt
            out_ref[r0 : r0 + TILE, 128 * q : 128 * (q + 1)] = total


def combine_kernel(place_ref, *refs):
    if len(refs) == 6:
        refs = refs[1:]
    part_ref, gath_ref, cumg_ref, c_ref, out_ref = refs
    here = place_ref[0]
    peers = gath_ref.shape[0]
    pairs = gath_ref.shape[1]
    state_size = c_ref.shape[1]
    for q in range(pairs):
        run = jnp.ones((1, 128), jnp.float32)
        state = jnp.zeros((state_size, 128), jnp.float32)
        for k in range(peers - 1, -1, -1):
            if k + 1 < peers:
                pair = gath_ref[k + 1, q, state_size : state_size + 2, :].astype(jnp.float32)
                later = pair[0:1] + pair[1:2]
                run = jnp.where(k + 1 < here, run * later, 1.0)
            weight = jnp.where(k < here, run, 0.0)
            state = state + weight * gath_ref[k, q, 0:state_size, :].astype(jnp.float32)
        readable = state.astype(jnp.bfloat16)
        inherited = jnp.dot(c_ref[...], readable, preferred_element_type=jnp.float32)
        decay = lane_pick(
            jnp.exp(cumg_ref[0, :, 2 * q : 2 * q + 1]), jnp.exp(cumg_ref[0, :, 2 * q + 1 : 2 * q + 2])
        )
        total = part_ref[:, 128 * q : 128 * (q + 1)] + decay * inherited
        out_ref[:, 128 * q : 128 * (q + 1)] = total.astype(out_ref.dtype)


def arbitrary():
    return pltpu.CompilerParams(dimension_semantics=("arbitrary",))


def carried_call(bt, fac_grouped, decay_lanes, onehot, arrived, first):
    rows, width = arrived.shape
    length = onehot.shape[0]
    groups = width // (GROUP * 64)
    state_size = bt.shape[0]
    return pl.pallas_call(
        carried_kernel,
        grid=(groups,),
        in_specs=[
            pl.BlockSpec(bt.shape, lambda g: (0, 0)),
            pl.BlockSpec((1, length, GROUP), lambda g: (g + first, 0, 0)),
            pl.BlockSpec((1, GROUP * 64), lambda g: (0, g + first)),
            pl.BlockSpec(onehot.shape, lambda g: (0, 0)),
            pl.BlockSpec((rows, GROUP * 64), lambda g: (0, g)),
        ],
        out_specs=[
            pl.BlockSpec((GROUP // 2, state_size + EXTRA, 128), lambda g: (g, 0, 0)),
            pl.BlockSpec((length, GROUP * 64), lambda g: (0, g)),
        ],
        out_shape=[
            jax.ShapeDtypeStruct((width // 128, state_size + EXTRA, 128), jnp.bfloat16),
            jax.ShapeDtypeStruct((length, width), jnp.bfloat16),
        ],
        compiler_params=arbitrary(),
    )(bt, fac_grouped, decay_lanes, onehot, arrived)


def local_call(scores, cum_grouped, cum_t, step_t, tokens, skip_lanes, first):
    length, width = tokens.shape
    groups = width // (GROUP * 64)
    return pl.pallas_call(
        local_kernel,
        grid=(groups,),
        in_specs=[
            pl.BlockSpec((length, length), lambda g: (0, 0)),
            pl.BlockSpec((1, length, GROUP), lambda g: (g + first, 0, 0)),
            pl.BlockSpec((GROUP, length), lambda g: (g + first, 0)),
            pl.BlockSpec((GROUP, length), lambda g: (g + first, 0)),
            pl.BlockSpec((length, GROUP * 64), lambda g: (0, g)),
            pl.BlockSpec((1, GROUP * 64), lambda g: (0, g + first)),
        ],
        out_specs=pl.BlockSpec((length, GROUP * 64), lambda g: (0, g)),
        out_shape=jax.ShapeDtypeStruct((length, width), jnp.float32),
        compiler_params=arbitrary(),
    )(scores, cum_grouped, cum_t, step_t, tokens, skip_lanes)


def combine_call(buffer, place, partial, gathered, cum_grouped, readout, first, total_width):
    length, width = partial.shape
    groups = width // (GROUP * 64)
    state_rows = gathered.shape[2]
    in_specs = [
        pl.BlockSpec((length, GROUP * 64), lambda g: (0, g)),
        pl.BlockSpec((gathered.shape[0], GROUP // 2, state_rows, 128), lambda g: (0, g, 0, 0)),
        pl.BlockSpec((1, length, GROUP), lambda g: (g + first, 0, 0)),
        pl.BlockSpec(readout.shape, lambda g: (0, 0)),
    ]
    operands = [partial, gathered, cum_grouped, readout]
    aliases = {}
    if buffer is not None:
        in_specs = [pl.BlockSpec(memory_space=pl.ANY)] + in_specs
        operands = [buffer] + operands
        aliases = {1: 0}
    return pl.pallas_call(
        combine_kernel,
        grid=(groups,),
        in_specs=[pl.BlockSpec(memory_space=pltpu.SMEM)] + in_specs,
        out_specs=pl.BlockSpec((length, GROUP * 64), lambda g: (0, g + first)),
        out_shape=jax.ShapeDtypeStruct((length, total_width), jnp.bfloat16),
        input_output_aliases=aliases,
        compiler_params=arbitrary(),
    )(place, *operands)


def send_rows(rows, pick_rows, stream_count, capacity):
    width = rows.shape[1]
    return jnp.take(rows, pick_rows, axis=0, mode="clip").reshape(stream_count, capacity, width)


def receive_rows(arrived, flat_rows):
    width = arrived.shape[2]
    return jnp.take(arrived.reshape(-1, width), flat_rows, axis=0, mode="clip")


def deliver(rows, pick_rows, flat_rows, stream_count, capacity):
    send = send_rows(rows, pick_rows, stream_count, capacity)
    arrived = lax.all_to_all(send, "stream", split_axis=0, concat_axis=0, tiled=True)
    return receive_rows(arrived, flat_rows)


def on_device(tokens_in, proj_in, step_raw, decay_log, head_skip_weight, row_counts):
    stream_count = lax.axis_size("stream")
    stream_index = lax.axis_index("stream")
    place_index = lax.axis_index("pos")
    tokens = tokens_in[0]
    local_rows, inner = tokens.shape
    head_count = step_raw.shape[2]
    head_size = inner // head_count
    state_size = proj_in.shape[2] // 2
    capacity = 3 * local_rows // (2 * stream_count)

    place_counts = lax.dynamic_index_in_dim(row_counts, place_index, 0, keepdims=False)
    send_counts = lax.dynamic_index_in_dim(place_counts, stream_index, 0, keepdims=False)
    recv_counts = lax.dynamic_index_in_dim(place_counts, stream_index, 1, keepdims=False)
    send_start = jnp.cumsum(send_counts) - send_counts
    slot_range = jnp.arange(capacity, dtype=jnp.int32)
    pick_rows = jnp.clip(send_start[:, None] + slot_range[None, :], 0, local_rows - 1).reshape(-1)
    recv_end = jnp.cumsum(recv_counts)
    recv_start = recv_end - recv_counts
    positions = jnp.arange(local_rows, dtype=jnp.int32)
    source = jnp.sum((recv_end[:, None] <= positions[None, :]).astype(jnp.int32), axis=0)
    source = jnp.clip(source, 0, stream_count - 1)
    source_start = jnp.take(recv_start, source)
    flat_rows = source * capacity + positions - source_start

    small = jnp.concatenate([proj_in[0], step_raw[0]], axis=1)
    ordered_small = deliver(small, pick_rows, flat_rows, stream_count, capacity)
    ordered_proj = ordered_small[:, : 2 * state_size]
    ordered_steps = ordered_small[:, 2 * state_size :]

    inputs = ordered_proj[:, :state_size]
    readout = ordered_proj[:, state_size:]
    decay_rates = -jnp.exp(decay_log)
    steps = jax.nn.softplus(ordered_steps.astype(jnp.float32))
    cum = jnp.cumsum(steps * decay_rates[None, :], axis=0)
    ending = cum[-1]
    factor = jnp.exp(ending[None, :] - cum) * steps
    groups = head_count // GROUP

    def grouped(a):
        return a.reshape(local_rows, groups, GROUP).transpose(1, 0, 2)

    cum_grouped = grouped(cum)
    fac_grouped = grouped(factor)
    cum_t = cum.T
    step_t = steps.T
    decay_lanes = jnp.repeat(jnp.exp(ending), head_size).reshape(1, -1)
    skip_lanes = jnp.repeat(head_skip_weight, head_size).reshape(1, -1)
    scores = jnp.dot(readout, inputs.T, preferred_element_type=jnp.float32)
    bt = inputs.T
    place = place_index.astype(jnp.int32).reshape(1)
    slots = jnp.arange(stream_count * capacity, dtype=jnp.int32)
    onehot = (flat_rows[:, None] == slots[None, :]).astype(jnp.bfloat16)

    sizes = CHUNK_GROUPS
    firsts = [sum(sizes[:c]) for c in range(len(sizes))]
    group_width = GROUP * head_size
    send_onehot = (pick_rows[:, None] == positions[None, :]).astype(jnp.bfloat16)
    sends = [send_call(send_onehot, tokens, f, n, stream_count) for f, n in zip(firsts, sizes)]
    partials = []
    gathers = []
    result = None
    done = 0
    for c in range(len(sizes)):
        arrived = lax.all_to_all(sends[c], "stream", split_axis=0, concat_axis=0, tiled=True)
        tied = {"arrived": arrived}
        if c + 1 < len(sizes):
            tied["send"] = sends[c + 1]
        if c >= 1:
            tied["partial"] = partials[c - 1]
        if c >= 2:
            result = combine_call(
                result, place, partials[done], gathers[done], cum_grouped, readout,
                firsts[done], inner,
            )
            done += 1
            tied["result"] = result
        tied = lax.optimization_barrier(tied)
        arrived = tied["arrived"]
        if c + 1 < len(sizes):
            sends[c + 1] = tied["send"]
        if c >= 2:
            result = tied["result"]
        carried, chunk_tokens = carried_call(
            bt, fac_grouped, decay_lanes, onehot, arrived.reshape(-1, arrived.shape[2]), firsts[c]
        )
        gathers.append(lax.all_gather(carried, "pos"))
        partials.append(
            local_call(scores, cum_grouped, cum_t, step_t, chunk_tokens, skip_lanes, firsts[c])
        )
    while done < len(sizes):
        result = combine_call(
            result, place, partials[done], gathers[done], cum_grouped, readout, firsts[done], inner
        )
        done += 1
    return result[None]


def solution(mesh):
    in_specs = (
        P("stream", "pos", None),
        P("stream", "pos", None),
        P("stream", "pos", None),
        P(),
        P(),
        P(),
    )
    out_specs = P("stream", "pos", None)
    return jax.shard_map(
        on_device, mesh=mesh, in_specs=in_specs, out_specs=out_specs, check_vma=False
    )
```

```python
import jax
import jax.numpy as jnp
from jax import lax
from jax.experimental import pallas as pl
from jax.experimental.pallas import tpu as pltpu
from jax.sharding import PartitionSpec as P

GROUP = 8
TILE = 128
CHUNK_GROUPS = (4, 4, 4, 4)
EXTRA = 8


def lane_pick(low, high):
    lane_low = lax.broadcasted_iota(jnp.int32, (1, 128), 1) < 64
    return jnp.where(lane_low, low, high)


def carried_kernel(bt_ref, facg_ref, decay_ref, onehot_ref, arr_ref, out_ref, tok_ref):
    pairs = out_ref.shape[0]
    state_size = bt_ref.shape[0]
    ordered = jnp.dot(onehot_ref[...], arr_ref[...], preferred_element_type=jnp.float32)
    tok_ref[...] = ordered.astype(tok_ref.dtype)
    for q in range(pairs):
        x = ordered[:, 128 * q : 128 * (q + 1)]
        factor = lane_pick(facg_ref[0, :, 2 * q : 2 * q + 1], facg_ref[0, :, 2 * q + 1 : 2 * q + 2])
        scaled = (factor * x).astype(jnp.bfloat16)
        out_ref[q, 0:state_size, :] = jnp.dot(
            bt_ref[...], scaled, preferred_element_type=jnp.float32
        ).astype(out_ref.dtype)
        rows = lax.broadcasted_iota(jnp.int32, (EXTRA, 128), 0)
        decay = decay_ref[:, 128 * q : 128 * (q + 1)]
        high = decay.astype(out_ref.dtype)
        low = (decay - high.astype(jnp.float32)).astype(out_ref.dtype)
        extra = jnp.where(rows == 0, high, jnp.where(rows == 1, low, jnp.zeros_like(high)))
        out_ref[q, state_size : state_size + EXTRA, :] = extra


def send_kernel(onehot_ref, tok_ref, out_ref):
    out_ref[...] = jnp.dot(
        onehot_ref[...], tok_ref[...], preferred_element_type=jnp.float32
    ).astype(out_ref.dtype)


def send_call(onehot, tokens, first, groups, stream_count):
    rows, length = onehot.shape
    width = GROUP * 64
    picked = pl.pallas_call(
        send_kernel,
        grid=(groups,),
        in_specs=[
            pl.BlockSpec(onehot.shape, lambda g: (0, 0)),
            pl.BlockSpec((length, width), lambda g: (0, g + first)),
        ],
        out_specs=pl.BlockSpec((rows, width), lambda g: (0, g)),
        out_shape=jax.ShapeDtypeStruct((rows, groups * width), tokens.dtype),
        compiler_params=arbitrary(),
    )(onehot, tokens)
    return picked.reshape(stream_count, rows // stream_count, groups * width)


def local_kernel(scores_ref, cumg_ref, cumt_ref, stept_ref, tok_ref, skip_ref, out_ref):
    length = scores_ref.shape[0]
    heads = cumt_ref.shape[0]
    for q in range(heads // 2):
        x = tok_ref[:, 128 * q : 128 * (q + 1)]
        skip = skip_ref[:, 128 * q : 128 * (q + 1)]
        for i in range(length // TILE):
            r0 = i * TILE
            width = (i + 1) * TILE
            rows = lax.broadcasted_iota(jnp.int32, (TILE, width), 0) + r0
            cols = lax.broadcasted_iota(jnp.int32, (TILE, width), 1)
            causal = rows >= cols
            sc = scores_ref[r0 : r0 + TILE, 0:width]
            parts = []
            for j in range(2):
                h = 2 * q + j
                ct = cumg_ref[0, r0 : r0 + TILE, h : h + 1]
                cs = cumt_ref[h : h + 1, 0:width]
                st = stept_ref[h : h + 1, 0:width]
                w = jnp.where(causal, jnp.exp(ct - cs), 0.0)
                wb = ((sc * w) * st).astype(jnp.bfloat16)
                parts.append(jnp.dot(wb, x[0:width], preferred_element_type=jnp.float32))
            xt = x[r0 : r0 + TILE].astype(jnp.float32)
            total = lane_pick(parts[0], parts[1]) + skip * xt
            out_ref[r0 : r0 + TILE, 128 * q : 128 * (q + 1)] = total


def combine_kernel(place_ref, *refs):
    if len(refs) == 6:
        refs = refs[1:]
    part_ref, gath_ref, cumg_ref, c_ref, out_ref = refs
    here = place_ref[0]
    peers = gath_ref.shape[0]
    pairs = gath_ref.shape[1]
    state_size = c_ref.shape[1]
    for q in range(pairs):
        run = jnp.ones((1, 128), jnp.float32)
        state = jnp.zeros((state_size, 128), jnp.float32)
        for k in range(peers - 1, -1, -1):
            if k + 1 < peers:
                pair = gath_ref[k + 1, q, state_size : state_size + 2, :].astype(jnp.float32)
                later = pair[0:1] + pair[1:2]
                run = jnp.where(k + 1 < here, run * later, 1.0)
            weight = jnp.where(k < here, run, 0.0)
            state = state + weight * gath_ref[k, q, 0:state_size, :].astype(jnp.float32)
        readable = state.astype(jnp.bfloat16)
        inherited = jnp.dot(c_ref[...], readable, preferred_element_type=jnp.float32)
        decay = lane_pick(
            jnp.exp(cumg_ref[0, :, 2 * q : 2 * q + 1]), jnp.exp(cumg_ref[0, :, 2 * q + 1 : 2 * q + 2])
        )
        total = part_ref[:, 128 * q : 128 * (q + 1)] + decay * inherited
        out_ref[:, 128 * q : 128 * (q + 1)] = total.astype(out_ref.dtype)


def arbitrary():
    return pltpu.CompilerParams(dimension_semantics=("arbitrary",))


def carried_call(bt, fac_grouped, decay_lanes, onehot, arrived, first):
    rows, width = arrived.shape
    length = onehot.shape[0]
    groups = width // (GROUP * 64)
    state_size = bt.shape[0]
    return pl.pallas_call(
        carried_kernel,
        grid=(groups,),
        in_specs=[
            pl.BlockSpec(bt.shape, lambda g: (0, 0)),
            pl.BlockSpec((1, length, GROUP), lambda g: (g + first, 0, 0)),
            pl.BlockSpec((1, GROUP * 64), lambda g: (0, g + first)),
            pl.BlockSpec(onehot.shape, lambda g: (0, 0)),
            pl.BlockSpec((rows, GROUP * 64), lambda g: (0, g)),
        ],
        out_specs=[
            pl.BlockSpec((GROUP // 2, state_size + EXTRA, 128), lambda g: (g, 0, 0)),
            pl.BlockSpec((length, GROUP * 64), lambda g: (0, g)),
        ],
        out_shape=[
            jax.ShapeDtypeStruct((width // 128, state_size + EXTRA, 128), jnp.bfloat16),
            jax.ShapeDtypeStruct((length, width), jnp.bfloat16),
        ],
        compiler_params=arbitrary(),
    )(bt, fac_grouped, decay_lanes, onehot, arrived)


def local_call(scores, cum_grouped, cum_t, step_t, tokens, skip_lanes, first):
    length, width = tokens.shape
    groups = width // (GROUP * 64)
    return pl.pallas_call(
        local_kernel,
        grid=(groups,),
        in_specs=[
            pl.BlockSpec((length, length), lambda g: (0, 0)),
            pl.BlockSpec((1, length, GROUP), lambda g: (g + first, 0, 0)),
            pl.BlockSpec((GROUP, length), lambda g: (g + first, 0)),
            pl.BlockSpec((GROUP, length), lambda g: (g + first, 0)),
            pl.BlockSpec((length, GROUP * 64), lambda g: (0, g)),
            pl.BlockSpec((1, GROUP * 64), lambda g: (0, g + first)),
        ],
        out_specs=pl.BlockSpec((length, GROUP * 64), lambda g: (0, g)),
        out_shape=jax.ShapeDtypeStruct((length, width), jnp.float32),
        compiler_params=arbitrary(),
    )(scores, cum_grouped, cum_t, step_t, tokens, skip_lanes)


def combine_call(buffer, place, partial, gathered, cum_grouped, readout, first, total_width):
    length, width = partial.shape
    groups = width // (GROUP * 64)
    state_rows = gathered.shape[2]
    in_specs = [
        pl.BlockSpec((length, GROUP * 64), lambda g: (0, g)),
        pl.BlockSpec((gathered.shape[0], GROUP // 2, state_rows, 128), lambda g: (0, g, 0, 0)),
        pl.BlockSpec((1, length, GROUP), lambda g: (g + first, 0, 0)),
        pl.BlockSpec(readout.shape, lambda g: (0, 0)),
    ]
    operands = [partial, gathered, cum_grouped, readout]
    aliases = {}
    if buffer is not None:
        in_specs = [pl.BlockSpec(memory_space=pl.ANY)] + in_specs
        operands = [buffer] + operands
        aliases = {1: 0}
    return pl.pallas_call(
        combine_kernel,
        grid=(groups,),
        in_specs=[pl.BlockSpec(memory_space=pltpu.SMEM)] + in_specs,
        out_specs=pl.BlockSpec((length, GROUP * 64), lambda g: (0, g + first)),
        out_shape=jax.ShapeDtypeStruct((length, total_width), jnp.bfloat16),
        input_output_aliases=aliases,
        compiler_params=arbitrary(),
    )(place, *operands)


def send_rows(rows, pick_rows, stream_count, capacity):
    width = rows.shape[1]
    return jnp.take(rows, pick_rows, axis=0, mode="clip").reshape(stream_count, capacity, width)


def receive_rows(arrived, flat_rows):
    width = arrived.shape[2]
    return jnp.take(arrived.reshape(-1, width), flat_rows, axis=0, mode="clip")


def deliver(rows, pick_rows, flat_rows, stream_count, capacity):
    send = send_rows(rows, pick_rows, stream_count, capacity)
    arrived = lax.all_to_all(send, "stream", split_axis=0, concat_axis=0, tiled=True)
    return receive_rows(arrived, flat_rows)


def on_device(tokens_in, proj_in, step_raw, decay_log, head_skip_weight, row_counts):
    stream_count = lax.axis_size("stream")
    stream_index = lax.axis_index("stream")
    place_index = lax.axis_index("pos")
    tokens = tokens_in[0]
    local_rows, inner = tokens.shape
    head_count = step_raw.shape[2]
    head_size = inner // head_count
    state_size = proj_in.shape[2] // 2
    capacity = 3 * local_rows // (2 * stream_count)

    place_counts = lax.dynamic_index_in_dim(row_counts, place_index, 0, keepdims=False)
    send_counts = lax.dynamic_index_in_dim(place_counts, stream_index, 0, keepdims=False)
    recv_counts = lax.dynamic_index_in_dim(place_counts, stream_index, 1, keepdims=False)
    send_start = jnp.cumsum(send_counts) - send_counts
    slot_range = jnp.arange(capacity, dtype=jnp.int32)
    pick_rows = jnp.clip(send_start[:, None] + slot_range[None, :], 0, local_rows - 1).reshape(-1)
    recv_end = jnp.cumsum(recv_counts)
    recv_start = recv_end - recv_counts
    positions = jnp.arange(local_rows, dtype=jnp.int32)
    source = jnp.sum((recv_end[:, None] <= positions[None, :]).astype(jnp.int32), axis=0)
    source = jnp.clip(source, 0, stream_count - 1)
    source_start = jnp.take(recv_start, source)
    flat_rows = source * capacity + positions - source_start

    small = jnp.concatenate([proj_in[0], step_raw[0]], axis=1)
    ordered_small = deliver(small, pick_rows, flat_rows, stream_count, capacity)
    ordered_proj = ordered_small[:, : 2 * state_size]
    ordered_steps = ordered_small[:, 2 * state_size :]

    inputs = ordered_proj[:, :state_size]
    readout = ordered_proj[:, state_size:]
    decay_rates = -jnp.exp(decay_log)
    steps = jax.nn.softplus(ordered_steps.astype(jnp.float32))
    cum = jnp.cumsum(steps * decay_rates[None, :], axis=0)
    ending = cum[-1]
    factor = jnp.exp(ending[None, :] - cum) * steps
    groups = head_count // GROUP

    def grouped(a):
        return a.reshape(local_rows, groups, GROUP).transpose(1, 0, 2)

    cum_grouped = grouped(cum)
    fac_grouped = grouped(factor)
    cum_t = cum.T
    step_t = steps.T
    decay_lanes = jnp.repeat(jnp.exp(ending), head_size).reshape(1, -1)
    skip_lanes = jnp.repeat(head_skip_weight, head_size).reshape(1, -1)
    scores = jnp.dot(readout, inputs.T, preferred_element_type=jnp.float32)
    bt = inputs.T
    place = place_index.astype(jnp.int32).reshape(1)
    slots = jnp.arange(stream_count * capacity, dtype=jnp.int32)
    onehot = (flat_rows[:, None] == slots[None, :]).astype(jnp.bfloat16)

    sizes = CHUNK_GROUPS
    firsts = [sum(sizes[:c]) for c in range(len(sizes))]
    group_width = GROUP * head_size
    send_onehot = (pick_rows[:, None] == positions[None, :]).astype(jnp.bfloat16)
    sends = [send_call(send_onehot, tokens, f, n, stream_count) for f, n in zip(firsts, sizes)]
    partials = []
    gathers = []
    result = None
    done = 0
    for c in range(len(sizes)):
        arrived = lax.all_to_all(sends[c], "stream", split_axis=0, concat_axis=0, tiled=True)
        tied = {"arrived": arrived}
        if c + 1 < len(sizes):
            tied["send"] = sends[c + 1]
        if c >= 1:
            tied["partial"] = partials[c - 1]
        if c >= 2:
            result = combine_call(
                result, place, partials[done], gathers[done], cum_grouped, readout,
                firsts[done], inner,
            )
            done += 1
            tied["result"] = result
        tied = lax.optimization_barrier(tied)
        arrived = tied["arrived"]
        if c + 1 < len(sizes):
            sends[c + 1] = tied["send"]
        if c >= 2:
            result = tied["result"]
        carried, chunk_tokens = carried_call(
            bt, fac_grouped, decay_lanes, onehot, arrived.reshape(-1, arrived.shape[2]), firsts[c]
        )
        gathers.append(lax.all_gather(carried, "pos"))
        partials.append(
            local_call(scores, cum_grouped, cum_t, step_t, chunk_tokens, skip_lanes, firsts[c])
        )
    while done < len(sizes):
        result = combine_call(
            result, place, partials[done], gathers[done], cum_grouped, readout, firsts[done], inner
        )
        done += 1
    return result[None]


def solution(mesh):
    in_specs = (
        P("stream", "pos", None),
        P("stream", "pos", None),
        P("stream", "pos", None),
        P(),
        P(),
        P(),
    )
    out_specs = P("stream", "pos", None)
    return jax.shard_map(
        on_device, mesh=mesh, in_specs=in_specs, out_specs=out_specs, check_vma=False
    )
```
